32 devices in a mesh: seq: 8 (over y, x, core), head: 4 (over z).
Axes of the slice: x: 2, y: 2, z: 4, core: 2. Of those that a mesh axis runs over, the one named last changes fastest.
Arguments:
- queries: bfloat16 [4096, 64, 128], P(('seq', 'head')), may hold values from -36 to 36
- keys: bfloat16 [4096, 8, 128], P(('seq', 'head')), may hold values from -6 to 6
- values: bfloat16 [4096, 8, 128], P(('seq', 'head')), may hold values from -6 to 6
- output_gradient: bfloat16 [4096, 64, 128], P(('seq', 'head')), may hold values from -6 to 6
- global_blocks: int32 [2], replicated, may hold values from 0 to 31, as said below
- random_blocks: int32 [32, 3], replicated, may hold values from 0 to 31, as said below
Outputs:
- out: bfloat16 [4096, 64, 128], P(('seq', 'head'))
- grad_queries: bfloat16 [4096, 64, 128], P(('seq', 'head'))
- grad_keys: bfloat16 [4096, 8, 128], P(('seq', 'head'))
- grad_values: bfloat16 [4096, 8, 128], P(('seq', 'head'))
The draws below stay inside these ranges and needn't reach their ends.
Inputs may be any that keep to these rules, and one draw needn't show every extreme that they name: `global_blocks`: the two blocks differ; one of them is the last block, 31. `random_blocks`: call 4 consecutive blocks starting at a multiple of 4 a group. The entries listed by a group's query blocks never lie in that group's own blocks, and at most 2 of them lie in any one other group; in every group some other group is hit exactly 2 times.
All inputs are finite; a program needn't handle non-finite values.
Results may differ from the reference program's by a relative error of at most 0.035.
Values may be sent and summed in bfloat16 or wider, within the bound.
No kernel may reach another device: no remote copies, remote signals or barrier semaphores. Data moves between devices by JAX's collectives and lax.ppermute only.
A program may use at most 128 MiB of HBM per device.

```python
import math
import jax
import jax.numpy as jnp
from jax import lax

QUERY_HEADS = 64
KEY_VALUE_HEADS = 8
HEAD_SIZE = 128
BLOCK_TOKENS = 128
SEQUENCE_TOKENS = 4096
BPS = 4
NB = 32
CAP = 2


def draw_keys(key, part):
    start_offset = jax.random.truncated_normal(jax.random.fold_in(key, 2), -6.0, 6.0, (SEQUENCE_TOKENS, KEY_VALUE_HEADS, HEAD_SIZE), jnp.float32)
    return start_offset.astype(jnp.bfloat16)


def draw_queries(key, part):
    start_offset = jax.random.truncated_normal(jax.random.fold_in(key, 1), -6.0, 6.0, (SEQUENCE_TOKENS, QUERY_HEADS, HEAD_SIZE), jnp.float32) * 2.0
    return start_offset.astype(jnp.bfloat16)


def draw_global_blocks(key, part):
    other_block = jax.random.randint(jax.random.fold_in(key, 7), (), 0, NB - 1).astype(jnp.int32)
    last_block = jnp.array(NB - 1, jnp.int32)
    order_bit = jax.random.randint(jax.random.fold_in(key, 8), (), 0, 2)
    first = jnp.where(order_bit == 0, last_block, other_block)
    second = jnp.where(order_bit == 0, other_block, last_block)
    return jnp.stack([first, second]).astype(jnp.int32)


def draw_random_blocks(key, part):
    group_count = NB // BPS
    entry_count = 3 * BPS
    pool_size = CAP * (group_count - 1)
    owner_weight = jax.random.randint(jax.random.fold_in(key, 31), (group_count,), 1, 5)

    def one_group(group_idx):
        group_key = jax.random.fold_in(jax.random.fold_in(key, 32), group_idx)
        pool_ids = jnp.arange(pool_size, dtype=jnp.int32)
        others = (group_idx + 1 + jnp.arange(group_count - 1, dtype=jnp.int32)) % group_count
        pool_owner = others[pool_ids % (group_count - 1)]
        forced = jax.random.randint(jax.random.fold_in(group_key, 1), (), 0, group_count - 1)
        raw = jax.random.randint(jax.random.fold_in(group_key, 2), (pool_size,), 0, 2 ** 16)
        ranked = raw * owner_weight[pool_owner] + jnp.where(pool_ids % (group_count - 1) == forced, 2 ** 20, 0)
        ranked = ranked * pool_size + pool_ids
        unused_values, chosen = lax.top_k(ranked, entry_count)
        owners = pool_owner[chosen]
        offsets = jax.random.randint(jax.random.fold_in(group_key, 3), (entry_count,), 0, BPS)
        listed = owners * BPS + offsets
        return listed.reshape(3, BPS).T
    return jax.vmap(one_group)(jnp.arange(group_count, dtype=jnp.int32)).reshape(NB, 3).astype(jnp.int32)


def shard_levels(own_key, extent, cuts, least, high):
    def one(axis_at, blocks):
        steps = jax.random.uniform(jax.random.fold_in(jax.random.fold_in(own_key, 6), axis_at), (blocks,), jnp.float32, least / len(cuts), high / len(cuts))
        return jnp.repeat(jnp.exp(steps), extent[axis_at] // blocks).reshape((-1,) + (1,) * (len(extent) - axis_at - 1))

    factor_of = one(*cuts[0])
    for cut in cuts[1:]:
        factor_of = factor_of * one(*cut)
    return factor_of


def normal_values(stream_key, shape, spread, bound, pieces=(), kind=jnp.bfloat16):
    factor_of = shard_levels(stream_key, shape, pieces, -0.22, 0.18) if pieces else 1.0
    values = jax.random.normal(stream_key, shape, jnp.float32) * spread * factor_of
    return jnp.minimum(jnp.maximum(values, -bound), bound).astype(kind)


def setup_inputs(seed: int = 0) -> dict:
    streams_of = jax.random.split(jax.random.key(seed), 7)
    return {
        "queries": draw_queries(jax.random.fold_in(streams_of[6], 71), 0),
        "keys": draw_keys(jax.random.fold_in(streams_of[6], 71), 0),
        "values": normal_values(streams_of[2], (SEQUENCE_TOKENS, KEY_VALUE_HEADS, HEAD_SIZE), 1.0, 6.0, ((0, 32),)),
        "output_gradient": normal_values(streams_of[3], (SEQUENCE_TOKENS, QUERY_HEADS, HEAD_SIZE), 1.0, 6.0, ((0, 32),)),
        "global_blocks": draw_global_blocks(jax.random.fold_in(streams_of[6], 71), 0),
        "random_blocks": draw_random_blocks(jax.random.fold_in(streams_of[6], 71), 0),
    }


def round_low(array):
    return lax.optimization_barrier(array.astype(jnp.bfloat16)).astype(jnp.float32)

def reference(queries, keys, values, output_gradient, global_blocks, random_blocks):
    block_total_count = SEQUENCE_TOKENS // BLOCK_TOKENS
    heads_per_group = QUERY_HEADS // KEY_VALUE_HEADS
    score_scale = 1.0 / math.sqrt(HEAD_SIZE)
    key_block_tiles = keys.reshape(block_total_count, BLOCK_TOKENS, KEY_VALUE_HEADS, HEAD_SIZE)
    value_block_tiles = values.reshape(block_total_count, BLOCK_TOKENS, KEY_VALUE_HEADS, HEAD_SIZE)
    query_block_tiles = queries.reshape(block_total_count, BLOCK_TOKENS, KEY_VALUE_HEADS, heads_per_group, HEAD_SIZE)
    gradient_tile_set = output_gradient.reshape(block_total_count, BLOCK_TOKENS, KEY_VALUE_HEADS, heads_per_group, HEAD_SIZE)
    tile_order = jnp.arange(8, dtype=jnp.int32)
    earlier = tile_order[None, :] < tile_order[:, None]
    remote = (tile_order >= 5)[:, None, None, None]

    def attend(sums, inputs):
        key_gradient_sum, value_gradient_sum = sums
        block_id, query_blk, grad_blk, random_row = inputs
        neighbours = jnp.stack([block_id - 1, block_id, block_id + 1]).astype(jnp.int32)
        listed = jnp.concatenate([neighbours, global_blocks.astype(jnp.int32), random_row.astype(jnp.int32)])
        inside = (listed >= 0) & (listed < block_total_count)
        repeat = jnp.any((listed[:, None] == listed[None, :]) & earlier, axis=1)
        live_row = inside & jnp.logical_not(repeat)
        clamped = jnp.clip(listed, 0, block_total_count - 1).astype(jnp.int32)
        key_t = key_block_tiles[clamped].astype(jnp.float32)
        value_t = value_block_tiles[clamped].astype(jnp.float32)
        query_f = query_blk.astype(jnp.float32)
        grad_f = grad_blk.astype(jnp.float32)
        scores = jnp.einsum('qkgd,tbkd->kgqtb', query_f, key_t) * score_scale
        scores = jnp.where(live_row[None, None, None, :, None], scores, -jnp.inf)
        row_max = lax.optimization_barrier(jnp.max(scores, axis=(3, 4), keepdims=True))
        expo = jnp.exp(scores - row_max)
        attn_prob = expo / lax.optimization_barrier(jnp.sum(expo, axis=(3, 4), keepdims=True))
        prob_low = round_low(attn_prob)
        attended = jnp.einsum('kgqtb,tbkd->qkgd', prob_low, value_t)
        out_low = round_low(attended)
        row_delta = lax.optimization_barrier(jnp.sum(grad_f * out_low, axis=-1))
        grad_prob = jnp.einsum('qkgd,tbkd->kgqtb', grad_f, value_t)
        grad_score = attn_prob * (grad_prob - jnp.transpose(row_delta, (1, 2, 0))[:, :, :, None, None])
        score_low = round_low(grad_score)
        query_grad = jnp.einsum('kgqtb,tbkd->qkgd', score_low, key_t) * score_scale
        key_grad = jnp.einsum('kgqtb,qkgd->tbkd', score_low, query_f) * score_scale
        value_grad = jnp.einsum('kgqtb,qkgd->tbkd', prob_low, grad_f)
        key_grad = jnp.where(remote, round_low(key_grad), key_grad)
        value_grad = jnp.where(remote, round_low(value_grad), value_grad)
        key_gradient_sum = key_gradient_sum.at[clamped].add(key_grad)
        value_gradient_sum = value_gradient_sum.at[clamped].add(value_grad)
        return ((key_gradient_sum, value_gradient_sum), (attended.astype(jnp.bfloat16), query_grad.astype(jnp.bfloat16)))
    zero_filled = jnp.zeros((block_total_count, BLOCK_TOKENS, KEY_VALUE_HEADS, HEAD_SIZE), jnp.float32)
    block_ids = jnp.arange(block_total_count, dtype=jnp.int32)
    (key_gradient_sum, value_gradient_sum), (output_block_rows, query_gradient_rows) = lax.scan(attend, (zero_filled, zero_filled), (block_ids, query_block_tiles, gradient_tile_set, random_blocks))
    return (output_block_rows.reshape(SEQUENCE_TOKENS, QUERY_HEADS, HEAD_SIZE), query_gradient_rows.reshape(SEQUENCE_TOKENS, QUERY_HEADS, HEAD_SIZE), key_gradient_sum.astype(jnp.bfloat16).reshape(SEQUENCE_TOKENS, KEY_VALUE_HEADS, HEAD_SIZE), value_gradient_sum.astype(jnp.bfloat16).reshape(SEQUENCE_TOKENS, KEY_VALUE_HEADS, HEAD_SIZE))
```

```python
import math

import jax
import jax.numpy as jnp
from jax import lax
from jax.sharding import PartitionSpec as P

BLOCK_TOKENS = 128


def padded(shard, sides, width):
    for axis, dim in sides:
        count, length = (lax.axis_size(axis), shard.shape[dim])
        up = [(i, (i + 1) % count) for i in range(count - 1)]
        down = [(j, i) for i, j in up]
        last = lax.slice_in_dim(shard, length - width, length, axis=dim)
        leading = lax.slice_in_dim(shard, 0, width, axis=dim)
        before = lax.ppermute(last, axis, up)
        after = lax.ppermute(leading, axis, down)
        shard = jnp.concatenate([before, shard, after], axis=dim)
    return shard


def from_root(block, axis, owner):
    block = jnp.where(lax.axis_index(axis) == owner, block, jnp.zeros_like(block))
    return lax.psum(block, axis)


def tree_sum(part, axis):
    count = lax.axis_size(axis)
    if count & (count - 1):
        return lax.psum(part.astype(jnp.bfloat16), axis).astype(jnp.float32)
    stride = 1
    while stride < count:
        pairs = [(i, i ^ stride) for i in range(count)]
        other = lax.ppermute(part.astype(jnp.bfloat16), axis, pairs)
        part = part + other.astype(jnp.float32)
        stride *= 2
    return part


def per_device(queries, keys, values, output_gradient, global_blocks, random_blocks):
    query_loc, key_loc, value_loc, grad_loc = (
        lax.all_to_all(queries, "head", split_axis=1, concat_axis=0, tiled=True),
        lax.all_to_all(keys, "head", split_axis=1, concat_axis=0, tiled=True),
        lax.all_to_all(values, "head", split_axis=1, concat_axis=0, tiled=True),
        lax.all_to_all(output_gradient, "head", split_axis=1, concat_axis=0, tiled=True),
    )
    shard_len, heads_q, head_width = query_loc.shape
    heads_kv = key_loc.shape[1]
    heads_per_group = heads_q // heads_kv
    kv_width = heads_kv * head_width
    blocks = shard_len // BLOCK_TOKENS
    seq_count = lax.axis_size("seq")
    own_index = lax.axis_index("seq")
    block_total_count = seq_count * blocks
    capacity = (3 * blocks + seq_count - 2) // (seq_count - 1)
    entry_count = 3 * blocks
    score_scale = 1.0 / math.sqrt(head_width)
    kv_pair = jnp.stack(
        [key_loc.reshape(shard_len, kv_width), value_loc.reshape(shard_len, kv_width)]
    )
    extended = padded(kv_pair, (("seq", 1),), BLOCK_TOKENS)
    kv_tiles = kv_pair.reshape(2, blocks, BLOCK_TOKENS, kv_width).transpose(1, 0, 2, 3)
    global_owner = global_blocks // blocks
    global_offset = global_blocks % blocks
    own_global = (jnp.arange(blocks)[None, :] == global_offset[:, None]) & (
        global_owner == own_index
    )[:, None]
    all_entries = (
        random_blocks.reshape(seq_count, blocks, 3)
        .transpose(0, 2, 1)
        .reshape(seq_count, entry_count)
    )
    all_owner = all_entries // blocks
    entry_ids = jnp.arange(entry_count)
    entry_earlier = entry_ids[None, :] < entry_ids[:, None]
    all_rank = jnp.sum(
        (all_owner[:, :, None] == all_owner[:, None, :]) & entry_earlier[None], axis=2
    )
    my_entries = lax.dynamic_index_in_dim(all_entries, own_index, 0, keepdims=False)
    my_owner = lax.dynamic_index_in_dim(all_owner, own_index, 0, keepdims=False)
    my_rank = lax.dynamic_index_in_dim(all_rank, own_index, 0, keepdims=False)
    my_slot = my_owner * capacity + my_rank
    owned_here = (all_owner == own_index)[:, :, None] & (
        all_rank[:, :, None] == jnp.arange(capacity)[None, None, :]
    )
    offset_match = (all_entries % blocks)[:, :, None] == jnp.arange(blocks)[None, None, :]
    selector = jnp.einsum(
        "tec,teo->tco",
        owned_here.astype(jnp.bfloat16),
        offset_match.astype(jnp.bfloat16),
        preferred_element_type=jnp.float32,
    ).astype(jnp.bfloat16)
    everything = lax.all_gather(kv_pair, "seq", axis=1, tiled=True)
    tiled_all = everything.reshape(2, block_total_count, BLOCK_TOKENS, kv_width)
    random_tiles = jnp.take(tiled_all, my_entries, axis=1).transpose(1, 0, 2, 3)
    global_tiles = jnp.take(tiled_all, global_blocks, axis=1).transpose(1, 0, 2, 3)
    random_by_block = random_tiles.reshape(3, blocks, 2, BLOCK_TOKENS, kv_width).transpose(
        1, 0, 2, 3, 4
    )
    block_ids = own_index * blocks + jnp.arange(blocks)
    listed = jnp.concatenate(
        [
            jnp.stack([block_ids - 1, block_ids, block_ids + 1], axis=1),
            jnp.broadcast_to(global_blocks[None, :], (blocks, 2)),
            my_entries.reshape(3, blocks).T,
        ],
        axis=1,
    )
    inside = (listed >= 0) & (listed < block_total_count)
    tile_ids = jnp.arange(8)
    tile_earlier = tile_ids[None, :] < tile_ids[:, None]
    repeat = jnp.any((listed[:, :, None] == listed[:, None, :]) & tile_earlier[None], axis=2)
    live = inside & jnp.logical_not(repeat)

    def attend(unused_state, inputs):
        query_blk, grad_blk, random_blk, live_row, position = inputs
        near_tiles = lax.dynamic_slice_in_dim(
            extended, position * BLOCK_TOKENS, 3 * BLOCK_TOKENS, 1
        )
        near_tiles = near_tiles.reshape(2, 3, BLOCK_TOKENS, kv_width).transpose(1, 0, 2, 3)
        all_tiles = jnp.concatenate([near_tiles, global_tiles, random_blk], axis=0)
        key_t = all_tiles[:, 0].reshape(8, BLOCK_TOKENS, heads_kv, head_width)
        value_t = all_tiles[:, 1].reshape(8, BLOCK_TOKENS, heads_kv, head_width)
        query_grid = query_blk.reshape(BLOCK_TOKENS, heads_kv, heads_per_group, head_width)
        grad_grid = grad_blk.reshape(BLOCK_TOKENS, heads_kv, heads_per_group, head_width)
        scores = (
            jnp.einsum("qkgd,tbkd->kgqtb", query_grid, key_t, preferred_element_type=jnp.float32)
            * score_scale
        )
        scores = jnp.where(live_row[None, None, None, :, None], scores, -jnp.inf)
        row_max = jnp.max(scores, axis=(3, 4), keepdims=True)
        expo = jnp.exp(scores - row_max)
        attn_prob = expo / jnp.sum(expo, axis=(3, 4), keepdims=True)
        prob_low = attn_prob.astype(jnp.bfloat16)
        attended = jnp.einsum(
            "kgqtb,tbkd->qkgd", prob_low, value_t, preferred_element_type=jnp.float32
        )
        out_low = attended.astype(jnp.bfloat16)
        row_delta = jnp.sum(grad_grid.astype(jnp.float32) * out_low.astype(jnp.float32), axis=-1)
        grad_prob = jnp.einsum(
            "qkgd,tbkd->kgqtb", grad_grid, value_t, preferred_element_type=jnp.float32
        )
        grad_score = attn_prob * (
            grad_prob - jnp.transpose(row_delta, (1, 2, 0))[:, :, :, None, None]
        )
        score_low = grad_score.astype(jnp.bfloat16)
        query_grad = (
            jnp.einsum("kgqtb,tbkd->qkgd", score_low, key_t, preferred_element_type=jnp.float32)
            * score_scale
        )
        key_grad = (
            jnp.einsum(
                "kgqtb,qkgd->tbkd", score_low, query_grid, preferred_element_type=jnp.float32
            )
            * score_scale
        )
        value_grad = jnp.einsum(
            "kgqtb,qkgd->tbkd", prob_low, grad_grid, preferred_element_type=jnp.float32
        )
        tile_terms = jnp.stack(
            [
                key_grad.reshape(8, BLOCK_TOKENS, kv_width),
                value_grad.reshape(8, BLOCK_TOKENS, kv_width),
            ],
            axis=1,
        )
        return (
            unused_state,
            (
                out_low.reshape(BLOCK_TOKENS, heads_q, head_width),
                query_grad.astype(jnp.bfloat16).reshape(BLOCK_TOKENS, heads_q, head_width),
                tile_terms,
            ),
        )

    unused_final, (output_block_rows, query_gradient_rows, tile_grads) = lax.scan(
        attend,
        0,
        (
            query_loc.reshape(blocks, BLOCK_TOKENS, heads_q, head_width),
            grad_loc.reshape(blocks, BLOCK_TOKENS, heads_q, head_width),
            random_by_block,
            live,
            jnp.arange(blocks),
        ),
    )
    pad_spec_low = ((0, 2), (0, 0), (0, 0), (0, 0))
    pad_spec_mid = ((1, 1), (0, 0), (0, 0), (0, 0))
    pad_spec_high = ((2, 0), (0, 0), (0, 0), (0, 0))
    window_sum = (
        jnp.pad(tile_grads[:, 0], pad_spec_low)
        + jnp.pad(tile_grads[:, 1], pad_spec_mid)
        + jnp.pad(tile_grads[:, 2], pad_spec_high)
    )
    rims = jnp.concatenate([window_sum[0], window_sum[blocks + 1]], axis=1)
    returned_rims = padded(rims.astype(jnp.bfloat16), (("seq", 1),), BLOCK_TOKENS).astype(
        rims.dtype
    )
    interior = window_sum[1 : blocks + 1]
    interior = (
        interior.at[0]
        .add(returned_rims[:, :BLOCK_TOKENS])
        .at[blocks - 1]
        .add(returned_rims[:, 3 * BLOCK_TOKENS :])
    )
    global_terms = jnp.sum(tile_grads[:, 3:5], axis=0)
    global_total = tree_sum(global_terms, "seq")
    own_weight = own_global.astype(jnp.float32)[:, :, None, None, None]
    interior = interior + jnp.sum(own_weight * global_total[:, None], axis=0)
    random_terms = (
        tile_grads[:, 5:8]
        .transpose(1, 0, 2, 3, 4)
        .reshape(entry_count, 2, BLOCK_TOKENS, kv_width)
        .astype(jnp.bfloat16)
    )
    slot_onehot = (my_slot[:, None] == jnp.arange(seq_count * capacity)[None, :]).astype(
        jnp.bfloat16
    )
    back_buffer = jnp.einsum(
        "es,exbw->sxbw", slot_onehot, random_terms, preferred_element_type=jnp.float32
    ).astype(jnp.bfloat16)
    returned_terms = lax.all_to_all(back_buffer, "seq", split_axis=0, concat_axis=0, tiled=True)
    interior = interior + jnp.einsum(
        "tco,tcxbw->oxbw",
        selector,
        returned_terms.reshape(seq_count, capacity, 2, BLOCK_TOKENS, kv_width),
        preferred_element_type=jnp.float32,
    )
    kv_grad = interior.transpose(1, 0, 2, 3).reshape(2, shard_len, kv_width).astype(jnp.bfloat16)
    out_all = output_block_rows.reshape(shard_len, heads_q, head_width)
    query_grad_all = query_gradient_rows.reshape(shard_len, heads_q, head_width)
    key_grad_all = kv_grad[0].reshape(shard_len, heads_kv, head_width)
    value_grad_all = kv_grad[1].reshape(shard_len, heads_kv, head_width)
    return (
        lax.all_to_all(out_all, "head", split_axis=0, concat_axis=1, tiled=True),
        lax.all_to_all(query_grad_all, "head", split_axis=0, concat_axis=1, tiled=True),
        lax.all_to_all(key_grad_all, "head", split_axis=0, concat_axis=1, tiled=True),
        lax.all_to_all(value_grad_all, "head", split_axis=0, concat_axis=1, tiled=True),
    )


def solution(mesh):
    placed = (
        P(("seq", "head"), None, None),
        P(("seq", "head"), None, None),
        P(("seq", "head"), None, None),
        P(("seq", "head"), None, None),
        P(),
        P(),
    )
    return jax.shard_map(
        per_device,
        mesh=mesh,
        in_specs=placed,
        out_specs=(
            P(("seq", "head"), None, None),
            P(("seq", "head"), None, None),
            P(("seq", "head"), None, None),
            P(("seq", "head"), None, None),
        ),
        check_vma=False,
    )
```

```python
import math

import jax
import jax.numpy as jnp
from jax import lax
from jax.sharding import PartitionSpec as P

BLOCK_TOKENS = 128


def padded(shard, sides, width):
    for axis, dim in sides:
        count, length = (lax.axis_size(axis), shard.shape[dim])
        up = [(i, (i + 1) % count) for i in range(count - 1)]
        down = [(j, i) for i, j in up]
        last = lax.slice_in_dim(shard, length - width, length, axis=dim)
        leading = lax.slice_in_dim(shard, 0, width, axis=dim)
        before = lax.ppermute(last, axis, up)
        after = lax.ppermute(leading, axis, down)
        shard = jnp.concatenate([before, shard, after], axis=dim)
    return shard


def from_root(block, axis, owner):
    block = jnp.where(lax.axis_index(axis) == owner, block, jnp.zeros_like(block))
    return lax.psum(block, axis)


def tree_sum(part, axis):
    count = lax.axis_size(axis)
    if count & (count - 1):
        return lax.psum(part.astype(jnp.bfloat16), axis).astype(jnp.float32)
    stride = 1
    while stride < count:
        pairs = [(i, i ^ stride) for i in range(count)]
        other = lax.ppermute(part.astype(jnp.bfloat16), axis, pairs)
        part = part + other.astype(jnp.float32)
        stride *= 2
    return part


def head_exchange(array, split_axis, concat_axis):
    count = lax.axis_size("head")
    own = lax.axis_index("head")
    piece = array.shape[split_axis] // count
    received = []
    for shift in range(count):
        target = (own + shift) % count
        part = lax.dynamic_slice_in_dim(array, target * piece, piece, split_axis)
        if shift:
            pairs = [(i, (i + shift) % count) for i in range(count)]
            part = lax.ppermute(part, "head", pairs)
        received.append(part)
    order = (own - jnp.arange(count)) % count
    stacked = jnp.take(jnp.stack(received), order, axis=0)
    stacked = jnp.moveaxis(stacked, 0, concat_axis)
    shape = list(array.shape)
    shape[split_axis] = piece
    shape[concat_axis] *= count
    return stacked.reshape(shape)


def per_chunk(queries, keys, values, output_gradient, global_blocks, random_blocks, gate):
    query_loc, key_loc, value_loc, grad_loc = (
        lax.all_to_all(queries, "head", split_axis=1, concat_axis=0, tiled=True),
        lax.all_to_all(keys, "head", split_axis=1, concat_axis=0, tiled=True),
        lax.all_to_all(values, "head", split_axis=1, concat_axis=0, tiled=True),
        lax.all_to_all(output_gradient, "head", split_axis=1, concat_axis=0, tiled=True),
    )
    if gate is not None:
        (query_loc, grad_loc), gate = lax.optimization_barrier(((query_loc, grad_loc), gate))
    shard_len, heads_q, head_width = query_loc.shape
    heads_kv = key_loc.shape[1]
    heads_per_group = heads_q // heads_kv
    kv_width = heads_kv * head_width
    blocks = shard_len // BLOCK_TOKENS
    seq_count = lax.axis_size("seq")
    own_index = lax.axis_index("seq")
    block_total_count = seq_count * blocks
    capacity = (3 * blocks + seq_count - 2) // (seq_count - 1)
    entry_count = 3 * blocks
    score_scale = 1.0 / math.sqrt(head_width)
    kv_pair = jnp.stack(
        [key_loc.reshape(shard_len, kv_width), value_loc.reshape(shard_len, kv_width)]
    )
    extended = padded(kv_pair, (("seq", 1),), BLOCK_TOKENS)
    kv_tiles = kv_pair.reshape(2, blocks, BLOCK_TOKENS, kv_width).transpose(1, 0, 2, 3)
    global_owner = global_blocks // blocks
    global_offset = global_blocks % blocks
    own_global = (jnp.arange(blocks)[None, :] == global_offset[:, None]) & (
        global_owner == own_index
    )[:, None]
    all_entries = (
        random_blocks.reshape(seq_count, blocks, 3)
        .transpose(0, 2, 1)
        .reshape(seq_count, entry_count)
    )
    all_owner = all_entries // blocks
    entry_ids = jnp.arange(entry_count)
    entry_earlier = entry_ids[None, :] < entry_ids[:, None]
    all_rank = jnp.sum(
        (all_owner[:, :, None] == all_owner[:, None, :]) & entry_earlier[None], axis=2
    )
    my_entries = lax.dynamic_index_in_dim(all_entries, own_index, 0, keepdims=False)
    my_owner = lax.dynamic_index_in_dim(all_owner, own_index, 0, keepdims=False)
    my_rank = lax.dynamic_index_in_dim(all_rank, own_index, 0, keepdims=False)
    my_slot = my_owner * capacity + my_rank
    owned_here = (all_owner == own_index)[:, :, None] & (
        all_rank[:, :, None] == jnp.arange(capacity)[None, None, :]
    )
    offset_match = (all_entries % blocks)[:, :, None] == jnp.arange(blocks)[None, None, :]
    selector = jnp.einsum(
        "tec,teo->tco",
        owned_here.astype(jnp.bfloat16),
        offset_match.astype(jnp.bfloat16),
        preferred_element_type=jnp.float32,
    ).astype(jnp.bfloat16)
    everything = lax.all_gather(kv_pair, "seq", axis=1, tiled=True)
    tiled_all = everything.reshape(2, block_total_count, BLOCK_TOKENS, kv_width)
    random_tiles = jnp.take(tiled_all, my_entries, axis=1).transpose(1, 0, 2, 3)
    global_tiles = jnp.take(tiled_all, global_blocks, axis=1).transpose(1, 0, 2, 3)
    random_by_block = random_tiles.reshape(3, blocks, 2, BLOCK_TOKENS, kv_width).transpose(
        1, 0, 2, 3, 4
    )
    block_ids = own_index * blocks + jnp.arange(blocks)
    listed = jnp.concatenate(
        [
            jnp.stack([block_ids - 1, block_ids, block_ids + 1], axis=1),
            jnp.broadcast_to(global_blocks[None, :], (blocks, 2)),
            my_entries.reshape(3, blocks).T,
        ],
        axis=1,
    )
    inside = (listed >= 0) & (listed < block_total_count)
    tile_ids = jnp.arange(8)
    tile_earlier = tile_ids[None, :] < tile_ids[:, None]
    repeat = jnp.any((listed[:, :, None] == listed[:, None, :]) & tile_earlier[None], axis=2)
    live = inside & jnp.logical_not(repeat)

    def attend(unused_state, inputs):
        query_blk, grad_blk, random_blk, live_row, position = inputs
        near_tiles = lax.dynamic_slice_in_dim(
            extended, position * BLOCK_TOKENS, 3 * BLOCK_TOKENS, 1
        )
        near_tiles = near_tiles.reshape(2, 3, BLOCK_TOKENS, kv_width).transpose(1, 0, 2, 3)
        all_tiles = jnp.concatenate([near_tiles, global_tiles, random_blk], axis=0)
        key_t = all_tiles[:, 0].reshape(8, BLOCK_TOKENS, heads_kv, head_width)
        value_t = all_tiles[:, 1].reshape(8, BLOCK_TOKENS, heads_kv, head_width)
        query_grid = query_blk.reshape(BLOCK_TOKENS, heads_kv, heads_per_group, head_width)
        grad_grid = grad_blk.reshape(BLOCK_TOKENS, heads_kv, heads_per_group, head_width)
        scores = (
            jnp.einsum("qkgd,tbkd->kgqtb", query_grid, key_t, preferred_element_type=jnp.float32)
            * score_scale
        )
        scores = jnp.where(live_row[None, None, None, :, None], scores, -jnp.inf)
        row_max = jnp.max(scores, axis=(3, 4), keepdims=True)
        expo = jnp.exp(scores - row_max)
        attn_prob = expo / jnp.sum(expo, axis=(3, 4), keepdims=True)
        prob_low = attn_prob.astype(jnp.bfloat16)
        attended = jnp.einsum(
            "kgqtb,tbkd->qkgd", prob_low, value_t, preferred_element_type=jnp.float32
        )
        out_low = attended.astype(jnp.bfloat16)
        row_delta = jnp.sum(grad_grid.astype(jnp.float32) * out_low.astype(jnp.float32), axis=-1)
        grad_prob = jnp.einsum(
            "qkgd,tbkd->kgqtb", grad_grid, value_t, preferred_element_type=jnp.float32
        )
        grad_score = attn_prob * (
            grad_prob - jnp.transpose(row_delta, (1, 2, 0))[:, :, :, None, None]
        )
        score_low = grad_score.astype(jnp.bfloat16)
        query_grad = (
            jnp.einsum("kgqtb,tbkd->qkgd", score_low, key_t, preferred_element_type=jnp.float32)
            * score_scale
        )
        key_grad = (
            jnp.einsum(
                "kgqtb,qkgd->tbkd", score_low, query_grid, preferred_element_type=jnp.float32
            )
            * score_scale
        )
        value_grad = jnp.einsum(
            "kgqtb,qkgd->tbkd", prob_low, grad_grid, preferred_element_type=jnp.float32
        )
        tile_terms = jnp.stack(
            [
                key_grad.reshape(8, BLOCK_TOKENS, kv_width),
                value_grad.reshape(8, BLOCK_TOKENS, kv_width),
            ],
            axis=1,
        )
        return (
            unused_state,
            (
                out_low.reshape(BLOCK_TOKENS, heads_q, head_width),
                query_grad.astype(jnp.bfloat16).reshape(BLOCK_TOKENS, heads_q, head_width),
                tile_terms,
            ),
        )

    unused_final, (output_block_rows, query_gradient_rows, tile_grads) = lax.scan(
        attend,
        0,
        (
            query_loc.reshape(blocks, BLOCK_TOKENS, heads_q, head_width),
            grad_loc.reshape(blocks, BLOCK_TOKENS, heads_q, head_width),
            random_by_block,
            live,
            jnp.arange(blocks),
        ),
    )
    pad_spec_low = ((0, 2), (0, 0), (0, 0), (0, 0))
    pad_spec_mid = ((1, 1), (0, 0), (0, 0), (0, 0))
    pad_spec_high = ((2, 0), (0, 0), (0, 0), (0, 0))
    window_sum = (
        jnp.pad(tile_grads[:, 0], pad_spec_low)
        + jnp.pad(tile_grads[:, 1], pad_spec_mid)
        + jnp.pad(tile_grads[:, 2], pad_spec_high)
    )
    rims = jnp.concatenate([window_sum[0], window_sum[blocks + 1]], axis=1)
    returned_rims = padded(rims.astype(jnp.bfloat16), (("seq", 1),), BLOCK_TOKENS).astype(
        rims.dtype
    )
    interior = window_sum[1 : blocks + 1]
    interior = (
        interior.at[0]
        .add(returned_rims[:, :BLOCK_TOKENS])
        .at[blocks - 1]
        .add(returned_rims[:, 3 * BLOCK_TOKENS :])
    )
    global_terms = jnp.sum(tile_grads[:, 3:5], axis=0)
    global_total = tree_sum(global_terms, "seq")
    own_weight = own_global.astype(jnp.float32)[:, :, None, None, None]
    interior = interior + jnp.sum(own_weight * global_total[:, None], axis=0)
    random_terms = (
        tile_grads[:, 5:8]
        .transpose(1, 0, 2, 3, 4)
        .reshape(entry_count, 2, BLOCK_TOKENS, kv_width)
        .astype(jnp.bfloat16)
    )
    slot_onehot = (my_slot[:, None] == jnp.arange(seq_count * capacity)[None, :]).astype(
        jnp.bfloat16
    )
    back_buffer = jnp.einsum(
        "es,exbw->sxbw", slot_onehot, random_terms, preferred_element_type=jnp.float32
    ).astype(jnp.bfloat16)
    returned_terms = lax.all_to_all(back_buffer, "seq", split_axis=0, concat_axis=0, tiled=True)
    interior = interior + jnp.einsum(
        "tco,tcxbw->oxbw",
        selector,
        returned_terms.reshape(seq_count, capacity, 2, BLOCK_TOKENS, kv_width),
        preferred_element_type=jnp.float32,
    )
    kv_grad = interior.transpose(1, 0, 2, 3).reshape(2, shard_len, kv_width).astype(jnp.bfloat16)
    out_all = output_block_rows.reshape(shard_len, heads_q, head_width)
    query_grad_all = query_gradient_rows.reshape(shard_len, heads_q, head_width)
    key_grad_all = kv_grad[0].reshape(shard_len, heads_kv, head_width)
    value_grad_all = kv_grad[1].reshape(shard_len, heads_kv, head_width)
    return (out_all, query_grad_all, key_grad_all, value_grad_all), gate


def head_part(array, chunks, chunk):
    tokens, heads, width = array.shape
    lanes = chunks * lax.axis_size("head")
    grid = array.reshape(tokens, lanes // chunks, chunks, heads // lanes, width)
    return grid[:, :, chunk].reshape(tokens, heads // chunks, width)


def head_join(parts):
    tokens, heads, width = parts[0].shape
    lanes = lax.axis_size("head")
    grid = jnp.stack([p.reshape(tokens, lanes, heads // lanes, width) for p in parts], axis=2)
    return grid.reshape(tokens, heads * len(parts), width)


def per_device(queries, keys, values, output_gradient, global_blocks, random_blocks):
    chunks = max(1, keys.shape[1] // lax.axis_size("head"))
    results = []
    gate = None
    for chunk in range(chunks):
        local, passed = per_chunk(
            head_part(queries, chunks, chunk),
            head_part(keys, chunks, chunk),
            head_part(values, chunks, chunk),
            head_part(output_gradient, chunks, chunk),
            global_blocks,
            random_blocks,
            gate,
        )
        if passed is not None:
            results.append(tuple(head_exchange(x, 0, 1) for x in passed))
        gate = local
    results.append(tuple(head_exchange(x, 0, 1) for x in gate))
    return tuple(head_join([r[i] for r in results]) for i in range(4))


def solution(mesh):
    placed = (
        P(("seq", "head"), None, None),
        P(("seq", "head"), None, None),
        P(("seq", "head"), None, None),
        P(("seq", "head"), None, None),
        P(),
        P(),
    )
    return jax.shard_map(
        per_device,
        mesh=mesh,
        in_specs=placed,
        out_specs=(
            P(("seq", "head"), None, None),
            P(("seq", "head"), None, None),
            P(("seq", "head"), None, None),
            P(("seq", "head"), None, None),
        ),
        check_vma=False,
    )
```

```python
import functools
import math

import jax
import jax.numpy as jnp
from jax import lax
from jax.experimental import pallas as pl
from jax.sharding import PartitionSpec as P

BLOCK_TOKENS = 128


def attention_kernel(q_ref, k_ref, v_ref, do_ref, bias_ref, out_ref, dq_ref, dk_ref, dv_ref, *, scale):
    q = q_ref[...]
    k = k_ref[...]
    v = v_ref[...]
    do = do_ref[...]
    rows_by_cols = (((1,), (1,)), ((), ()))
    over_rows = (((0,), (0,)), ((), ()))
    s = lax.dot_general(q, k, rows_by_cols, preferred_element_type=jnp.float32) * scale
    s = s + bias_ref[...]
    e = jnp.exp(s - jnp.max(s, axis=1, keepdims=True))
    p = e / jnp.sum(e, axis=1, keepdims=True)
    p_low = p.astype(jnp.bfloat16)
    o_low = jnp.dot(p_low, v, preferred_element_type=jnp.float32).astype(jnp.bfloat16)
    out_ref[...] = o_low
    delta = jnp.sum(do.astype(jnp.float32) * o_low.astype(jnp.float32), axis=1, keepdims=True)
    dp = lax.dot_general(do, v, rows_by_cols, preferred_element_type=jnp.float32)
    ds_low = (p * (dp - delta)).astype(jnp.bfloat16)
    dq = jnp.dot(ds_low, k, preferred_element_type=jnp.float32) * scale
    dq_ref[...] = dq.astype(jnp.bfloat16)
    dk_ref[...] = lax.dot_general(ds_low, q, over_rows, preferred_element_type=jnp.float32) * scale
    dv_ref[...] = lax.dot_general(p_low, do, over_rows, preferred_element_type=jnp.float32)


def attention_call(q, k, v, do, bias, scale, interpret=False):
    blocks, heads_kv, rows, width = q.shape
    keys_n = k.shape[2]
    q_spec = pl.BlockSpec((None, None, rows, width), lambda j, h: (j, h, 0, 0))
    k_spec = pl.BlockSpec((None, None, keys_n, width), lambda j, h: (j, h, 0, 0))
    b_spec = pl.BlockSpec((None, 1, keys_n), lambda j, h: (j, 0, 0))
    return pl.pallas_call(
        functools.partial(attention_kernel, scale=scale),
        grid=(blocks, heads_kv),
        in_specs=[q_spec, k_spec, k_spec, q_spec, b_spec],
        out_specs=[q_spec, q_spec, k_spec, k_spec],
        out_shape=[
            jax.ShapeDtypeStruct(q.shape, jnp.bfloat16),
            jax.ShapeDtypeStruct(q.shape, jnp.bfloat16),
            jax.ShapeDtypeStruct(k.shape, jnp.float32),
            jax.ShapeDtypeStruct(k.shape, jnp.float32),
        ],
        interpret=interpret,
    )(q, k, v, do, bias)


def padded(shard, sides, width):
    for axis, dim in sides:
        count, length = (lax.axis_size(axis), shard.shape[dim])
        up = [(i, (i + 1) % count) for i in range(count - 1)]
        down = [(j, i) for i, j in up]
        last = lax.slice_in_dim(shard, length - width, length, axis=dim)
        leading = lax.slice_in_dim(shard, 0, width, axis=dim)
        before = lax.ppermute(last, axis, up)
        after = lax.ppermute(leading, axis, down)
        shard = jnp.concatenate([before, shard, after], axis=dim)
    return shard


def from_root(block, axis, owner):
    block = jnp.where(lax.axis_index(axis) == owner, block, jnp.zeros_like(block))
    return lax.psum(block, axis)


def tree_sum(part, axis):
    count = lax.axis_size(axis)
    if count & (count - 1):
        return lax.psum(part.astype(jnp.bfloat16), axis).astype(jnp.float32)
    stride = 1
    while stride < count:
        pairs = [(i, i ^ stride) for i in range(count)]
        other = lax.ppermute(part.astype(jnp.bfloat16), axis, pairs)
        part = part + other.astype(jnp.float32)
        stride *= 2
    return part


def per_device(queries, keys, values, output_gradient, global_blocks, random_blocks):
    query_loc, key_loc, value_loc, grad_loc = (
        lax.all_to_all(queries, "head", split_axis=1, concat_axis=0, tiled=True),
        lax.all_to_all(keys, "head", split_axis=1, concat_axis=0, tiled=True),
        lax.all_to_all(values, "head", split_axis=1, concat_axis=0, tiled=True),
        lax.all_to_all(output_gradient, "head", split_axis=1, concat_axis=0, tiled=True),
    )
    shard_len, heads_q, head_width = query_loc.shape
    heads_kv = key_loc.shape[1]
    heads_per_group = heads_q // heads_kv
    kv_width = heads_kv * head_width
    blocks = shard_len // BLOCK_TOKENS
    seq_count = lax.axis_size("seq")
    own_index = lax.axis_index("seq")
    block_total_count = seq_count * blocks
    capacity = (3 * blocks + seq_count - 2) // (seq_count - 1)
    entry_count = 3 * blocks
    score_scale = 1.0 / math.sqrt(head_width)
    kv_pair = jnp.stack(
        [key_loc.reshape(shard_len, kv_width), value_loc.reshape(shard_len, kv_width)]
    )
    extended = padded(kv_pair, (("seq", 1),), BLOCK_TOKENS)
    kv_tiles = kv_pair.reshape(2, blocks, BLOCK_TOKENS, kv_width).transpose(1, 0, 2, 3)
    global_owner = global_blocks // blocks
    global_offset = global_blocks % blocks
    own_global = (jnp.arange(blocks)[None, :] == global_offset[:, None]) & (
        global_owner == own_index
    )[:, None]
    all_entries = (
        random_blocks.reshape(seq_count, blocks, 3)
        .transpose(0, 2, 1)
        .reshape(seq_count, entry_count)
    )
    all_owner = all_entries // blocks
    entry_ids = jnp.arange(entry_count)
    entry_earlier = entry_ids[None, :] < entry_ids[:, None]
    all_rank = jnp.sum(
        (all_owner[:, :, None] == all_owner[:, None, :]) & entry_earlier[None], axis=2
    )
    my_entries = lax.dynamic_index_in_dim(all_entries, own_index, 0, keepdims=False)
    my_owner = lax.dynamic_index_in_dim(all_owner, own_index, 0, keepdims=False)
    my_rank = lax.dynamic_index_in_dim(all_rank, own_index, 0, keepdims=False)
    my_slot = my_owner * capacity + my_rank
    owned_here = (all_owner == own_index)[:, :, None] & (
        all_rank[:, :, None] == jnp.arange(capacity)[None, None, :]
    )
    offset_match = (all_entries % blocks)[:, :, None] == jnp.arange(blocks)[None, None, :]
    selector = jnp.einsum(
        "tec,teo->tco",
        owned_here.astype(jnp.bfloat16),
        offset_match.astype(jnp.bfloat16),
        preferred_element_type=jnp.float32,
    ).astype(jnp.bfloat16)
    everything = lax.all_gather(kv_pair, "seq", axis=1, tiled=True)
    tiled_all = everything.reshape(2, block_total_count, BLOCK_TOKENS, kv_width)
    random_tiles = jnp.take(tiled_all, my_entries, axis=1).transpose(1, 0, 2, 3)
    global_tiles = jnp.take(tiled_all, global_blocks, axis=1).transpose(1, 0, 2, 3)
    random_by_block = random_tiles.reshape(3, blocks, 2, BLOCK_TOKENS, kv_width).transpose(
        1, 0, 2, 3, 4
    )
    block_ids = own_index * blocks + jnp.arange(blocks)
    listed = jnp.concatenate(
        [
            jnp.stack([block_ids - 1, block_ids, block_ids + 1], axis=1),
            jnp.broadcast_to(global_blocks[None, :], (blocks, 2)),
            my_entries.reshape(3, blocks).T,
        ],
        axis=1,
    )
    inside = (listed >= 0) & (listed < block_total_count)
    tile_ids = jnp.arange(8)
    tile_earlier = tile_ids[None, :] < tile_ids[:, None]
    repeat = jnp.any((listed[:, :, None] == listed[:, None, :]) & tile_earlier[None], axis=2)
    live = inside & jnp.logical_not(repeat)

    tiles_per_block = []
    for position in range(blocks):
        near_tiles = lax.slice_in_dim(
            extended, position * BLOCK_TOKENS, (position + 3) * BLOCK_TOKENS, axis=1
        )
        near_tiles = near_tiles.reshape(2, 3, BLOCK_TOKENS, kv_width).transpose(1, 0, 2, 3)
        tiles_per_block.append(
            jnp.concatenate([near_tiles, global_tiles, random_by_block[position]], axis=0)
        )
    all_tiles = jnp.stack(tiles_per_block)
    tile_count = all_tiles.shape[1]
    key_rows = tile_count * BLOCK_TOKENS

    def key_major(part):
        grid = part.reshape(blocks, tile_count, BLOCK_TOKENS, heads_kv, head_width)
        return grid.transpose(0, 3, 1, 2, 4).reshape(blocks, heads_kv, key_rows, head_width)

    def query_major(part):
        grid = part.reshape(blocks, BLOCK_TOKENS, heads_kv, heads_per_group, head_width)
        grid = grid.transpose(0, 2, 3, 1, 4)
        return grid.reshape(blocks, heads_kv, heads_per_group * BLOCK_TOKENS, head_width)

    def query_back(part):
        grid = part.reshape(blocks, heads_kv, heads_per_group, BLOCK_TOKENS, head_width)
        return grid.transpose(0, 3, 1, 2, 4).reshape(blocks, BLOCK_TOKENS, heads_q, head_width)

    def key_back(part):
        grid = part.reshape(blocks, heads_kv, tile_count, BLOCK_TOKENS, head_width)
        return grid.transpose(0, 2, 3, 1, 4).reshape(blocks, tile_count, BLOCK_TOKENS, kv_width)

    bias = jnp.where(live, 0.0, -jnp.inf).astype(jnp.float32)
    bias = jnp.repeat(bias, BLOCK_TOKENS, axis=1).reshape(blocks, 1, key_rows)
    out_q, grad_q, grad_k, grad_v = attention_call(
        query_major(query_loc),
        key_major(all_tiles[:, :, 0]),
        key_major(all_tiles[:, :, 1]),
        query_major(grad_loc),
        bias,
        score_scale,
    )
    output_block_rows = query_back(out_q)
    query_gradient_rows = query_back(grad_q)
    tile_grads = jnp.stack([key_back(grad_k), key_back(grad_v)], axis=2)
    pad_spec_low = ((0, 2), (0, 0), (0, 0), (0, 0))
    pad_spec_mid = ((1, 1), (0, 0), (0, 0), (0, 0))
    pad_spec_high = ((2, 0), (0, 0), (0, 0), (0, 0))
    window_sum = (
        jnp.pad(tile_grads[:, 0], pad_spec_low)
        + jnp.pad(tile_grads[:, 1], pad_spec_mid)
        + jnp.pad(tile_grads[:, 2], pad_spec_high)
    )
    rims = jnp.concatenate([window_sum[0], window_sum[blocks + 1]], axis=1)
    returned_rims = padded(rims.astype(jnp.bfloat16), (("seq", 1),), BLOCK_TOKENS).astype(
        rims.dtype
    )
    interior = window_sum[1 : blocks + 1]
    interior = (
        interior.at[0]
        .add(returned_rims[:, :BLOCK_TOKENS])
        .at[blocks - 1]
        .add(returned_rims[:, 3 * BLOCK_TOKENS :])
    )
    global_terms = jnp.sum(tile_grads[:, 3:5], axis=0)
    global_total = tree_sum(global_terms, "seq")
    own_weight = own_global.astype(jnp.float32)[:, :, None, None, None]
    interior = interior + jnp.sum(own_weight * global_total[:, None], axis=0)
    random_terms = (
        tile_grads[:, 5:8]
        .transpose(1, 0, 2, 3, 4)
        .reshape(entry_count, 2, BLOCK_TOKENS, kv_width)
        .astype(jnp.bfloat16)
    )
    slot_onehot = (my_slot[:, None] == jnp.arange(seq_count * capacity)[None, :]).astype(
        jnp.bfloat16
    )
    back_buffer = jnp.einsum(
        "es,exbw->sxbw", slot_onehot, random_terms, preferred_element_type=jnp.float32
    ).astype(jnp.bfloat16)
    returned_terms = lax.all_to_all(back_buffer, "seq", split_axis=0, concat_axis=0, tiled=True)
    interior = interior + jnp.einsum(
        "tco,tcxbw->oxbw",
        selector,
        returned_terms.reshape(seq_count, capacity, 2, BLOCK_TOKENS, kv_width),
        preferred_element_type=jnp.float32,
    )
    kv_grad = interior.transpose(1, 0, 2, 3).reshape(2, shard_len, kv_width).astype(jnp.bfloat16)
    out_all = output_block_rows.reshape(shard_len, heads_q, head_width)
    query_grad_all = query_gradient_rows.reshape(shard_len, heads_q, head_width)
    key_grad_all = kv_grad[0].reshape(shard_len, heads_kv, head_width)
    value_grad_all = kv_grad[1].reshape(shard_len, heads_kv, head_width)
    return (
        lax.all_to_all(out_all, "head", split_axis=0, concat_axis=1, tiled=True),
        lax.all_to_all(query_grad_all, "head", split_axis=0, concat_axis=1, tiled=True),
        lax.all_to_all(key_grad_all, "head", split_axis=0, concat_axis=1, tiled=True),
        lax.all_to_all(value_grad_all, "head", split_axis=0, concat_axis=1, tiled=True),
    )


def solution(mesh):
    placed = (
        P(("seq", "head"), None, None),
        P(("seq", "head"), None, None),
        P(("seq", "head"), None, None),
        P(("seq", "head"), None, None),
        P(),
        P(),
    )
    return jax.shard_map(
        per_device,
        mesh=mesh,
        in_specs=placed,
        out_specs=(
            P(("seq", "head"), None, None),
            P(("seq", "head"), None, None),
            P(("seq", "head"), None, None),
            P(("seq", "head"), None, None),
        ),
        check_vma=False,
    )
```

```python
import functools
import math

import jax
import jax.numpy as jnp
from jax import lax
from jax.experimental import pallas as pl
from jax.sharding import PartitionSpec as P

BLOCK_TOKENS = 128


def attention_kernel(q_ref, k_ref, v_ref, do_ref, bias_ref, out_ref, dq_ref, grad_ref, *, scale):
    group = q_ref.shape[1] // q_ref.shape[0]
    width = k_ref.shape[-1]

    def rows_of(ref):
        return jnp.concatenate([ref[:, g * width:(g + 1) * width] for g in range(group)], axis=0)

    def store_rows(ref, value):
        tokens = ref.shape[0]
        for g in range(group):
            ref[:, g * width:(g + 1) * width] = value[g * tokens:(g + 1) * tokens, :]

    q = rows_of(q_ref)
    do = rows_of(do_ref)
    k = k_ref[...].reshape(-1, width)
    v = v_ref[...].reshape(-1, width)
    rows_by_cols = (((1,), (1,)), ((), ()))
    over_rows = (((0,), (0,)), ((), ()))
    s = lax.dot_general(q, k, rows_by_cols, preferred_element_type=jnp.float32) * scale
    s = s + bias_ref[...]
    e = jnp.exp(s - jnp.max(s, axis=1, keepdims=True))
    p = e / jnp.sum(e, axis=1, keepdims=True)
    p_low = p.astype(jnp.bfloat16)
    o_low = jnp.dot(p_low, v, preferred_element_type=jnp.float32).astype(jnp.bfloat16)
    store_rows(out_ref, o_low)
    delta = jnp.sum(do.astype(jnp.float32) * o_low.astype(jnp.float32), axis=1, keepdims=True)
    dp = lax.dot_general(do, v, rows_by_cols, preferred_element_type=jnp.float32)
    ds_low = (p * (dp - delta)).astype(jnp.bfloat16)
    dq = jnp.dot(ds_low, k, preferred_element_type=jnp.float32) * scale
    store_rows(dq_ref, dq.astype(jnp.bfloat16))
    dk = lax.dot_general(ds_low, q, over_rows, preferred_element_type=jnp.float32) * scale
    dv = lax.dot_general(p_low, do, over_rows, preferred_element_type=jnp.float32)
    grad_ref[:, 0] = dk.reshape(grad_ref.shape[0], -1, width)
    grad_ref[:, 1] = dv.reshape(grad_ref.shape[0], -1, width)


def attention_call(q, tiles, do, bias, heads_kv, scale):
    blocks, tokens, q_width = q.shape
    tile_count, head_width = tiles.shape[1], tiles.shape[-1] // heads_kv
    rows_width = q_width // heads_kv
    q_spec = pl.BlockSpec((None, tokens, rows_width), lambda j, h: (j, 0, h))
    k_spec = pl.BlockSpec((None, tile_count, None, tokens, head_width), lambda j, h: (j, 0, 0, 0, h))
    v_spec = pl.BlockSpec((None, tile_count, None, tokens, head_width), lambda j, h: (j, 0, 1, 0, h))
    b_spec = pl.BlockSpec((None, 1, bias.shape[-1]), lambda j, h: (j, 0, 0))
    g_spec = pl.BlockSpec((None, tile_count, 2, tokens, head_width), lambda j, h: (j, 0, 0, 0, h))
    return pl.pallas_call(
        functools.partial(attention_kernel, scale=scale),
        grid=(blocks, heads_kv),
        in_specs=[q_spec, k_spec, v_spec, q_spec, b_spec],
        out_specs=[q_spec, q_spec, g_spec],
        out_shape=[
            jax.ShapeDtypeStruct(q.shape, jnp.bfloat16),
            jax.ShapeDtypeStruct(q.shape, jnp.bfloat16),
            jax.ShapeDtypeStruct(tiles.shape, jnp.float32),
        ],
    )(q, tiles, tiles, do, bias)


def padded(shard, sides, width):
    for axis, dim in sides:
        count, length = (lax.axis_size(axis), shard.shape[dim])
        up = [(i, (i + 1) % count) for i in range(count - 1)]
        down = [(j, i) for i, j in up]
        last = lax.slice_in_dim(shard, length - width, length, axis=dim)
        leading = lax.slice_in_dim(shard, 0, width, axis=dim)
        before = lax.ppermute(last, axis, up)
        after = lax.ppermute(leading, axis, down)
        shard = jnp.concatenate([before, shard, after], axis=dim)
    return shard


def from_root(block, axis, owner):
    block = jnp.where(lax.axis_index(axis) == owner, block, jnp.zeros_like(block))
    return lax.psum(block, axis)


def tree_sum(part, axis):
    count = lax.axis_size(axis)
    if count & (count - 1):
        return lax.psum(part.astype(jnp.bfloat16), axis).astype(jnp.float32)
    stride = 1
    while stride < count:
        pairs = [(i, i ^ stride) for i in range(count)]
        other = lax.ppermute(part.astype(jnp.bfloat16), axis, pairs)
        part = part + other.astype(jnp.float32)
        stride *= 2
    return part


def per_device(queries, keys, values, output_gradient, global_blocks, random_blocks):
    query_loc, key_loc, value_loc, grad_loc = (
        lax.all_to_all(queries, "head", split_axis=1, concat_axis=0, tiled=True),
        lax.all_to_all(keys, "head", split_axis=1, concat_axis=0, tiled=True),
        lax.all_to_all(values, "head", split_axis=1, concat_axis=0, tiled=True),
        lax.all_to_all(output_gradient, "head", split_axis=1, concat_axis=0, tiled=True),
    )
    shard_len, heads_q, head_width = query_loc.shape
    heads_kv = key_loc.shape[1]
    heads_per_group = heads_q // heads_kv
    kv_width = heads_kv * head_width
    blocks = shard_len // BLOCK_TOKENS
    seq_count = lax.axis_size("seq")
    own_index = lax.axis_index("seq")
    block_total_count = seq_count * blocks
    capacity = (3 * blocks + seq_count - 2) // (seq_count - 1)
    entry_count = 3 * blocks
    score_scale = 1.0 / math.sqrt(head_width)
    kv_pair = jnp.stack(
        [key_loc.reshape(shard_len, kv_width), value_loc.reshape(shard_len, kv_width)]
    )
    extended = padded(kv_pair, (("seq", 1),), BLOCK_TOKENS)
    kv_tiles = kv_pair.reshape(2, blocks, BLOCK_TOKENS, kv_width).transpose(1, 0, 2, 3)
    global_owner = global_blocks // blocks
    global_offset = global_blocks % blocks
    own_global = (jnp.arange(blocks)[None, :] == global_offset[:, None]) & (
        global_owner == own_index
    )[:, None]
    all_entries = (
        random_blocks.reshape(seq_count, blocks, 3)
        .transpose(0, 2, 1)
        .reshape(seq_count, entry_count)
    )
    all_owner = all_entries // blocks
    entry_ids = jnp.arange(entry_count)
    entry_earlier = entry_ids[None, :] < entry_ids[:, None]
    all_rank = jnp.sum(
        (all_owner[:, :, None] == all_owner[:, None, :]) & entry_earlier[None], axis=2
    )
    my_entries = lax.dynamic_index_in_dim(all_entries, own_index, 0, keepdims=False)
    my_owner = lax.dynamic_index_in_dim(all_owner, own_index, 0, keepdims=False)
    my_rank = lax.dynamic_index_in_dim(all_rank, own_index, 0, keepdims=False)
    my_slot = my_owner * capacity + my_rank
    owned_here = (all_owner == own_index)[:, :, None] & (
        all_rank[:, :, None] == jnp.arange(capacity)[None, None, :]
    )
    offset_match = (all_entries % blocks)[:, :, None] == jnp.arange(blocks)[None, None, :]
    selector = jnp.einsum(
        "tec,teo->tco",
        owned_here.astype(jnp.bfloat16),
        offset_match.astype(jnp.bfloat16),
        preferred_element_type=jnp.float32,
    ).astype(jnp.bfloat16)
    everything = lax.all_gather(kv_pair, "seq", axis=1, tiled=True)
    tiled_all = everything.reshape(2, block_total_count, BLOCK_TOKENS, kv_width)
    random_tiles = jnp.take(tiled_all, my_entries, axis=1).transpose(1, 0, 2, 3)
    global_tiles = jnp.take(tiled_all, global_blocks, axis=1).transpose(1, 0, 2, 3)
    random_by_block = random_tiles.reshape(3, blocks, 2, BLOCK_TOKENS, kv_width).transpose(
        1, 0, 2, 3, 4
    )
    block_ids = own_index * blocks + jnp.arange(blocks)
    listed = jnp.concatenate(
        [
            jnp.stack([block_ids - 1, block_ids, block_ids + 1], axis=1),
            jnp.broadcast_to(global_blocks[None, :], (blocks, 2)),
            my_entries.reshape(3, blocks).T,
        ],
        axis=1,
    )
    inside = (listed >= 0) & (listed < block_total_count)
    tile_ids = jnp.arange(8)
    tile_earlier = tile_ids[None, :] < tile_ids[:, None]
    repeat = jnp.any((listed[:, :, None] == listed[:, None, :]) & tile_earlier[None], axis=2)
    live = inside & jnp.logical_not(repeat)

    tiles_per_block = []
    for position in range(blocks):
        near_tiles = lax.slice_in_dim(
            extended, position * BLOCK_TOKENS, (position + 3) * BLOCK_TOKENS, axis=1
        )
        near_tiles = near_tiles.reshape(2, 3, BLOCK_TOKENS, kv_width).transpose(1, 0, 2, 3)
        tiles_per_block.append(
            jnp.concatenate([near_tiles, global_tiles, random_by_block[position]], axis=0)
        )
    all_tiles = jnp.stack(tiles_per_block)
    tile_count = all_tiles.shape[1]
    bias = jnp.where(live, 0.0, -jnp.inf).astype(jnp.float32)
    bias = jnp.repeat(bias, BLOCK_TOKENS, axis=1).reshape(blocks, 1, tile_count * BLOCK_TOKENS)
    out_q, grad_q, tile_grads = attention_call(
        query_loc.reshape(blocks, BLOCK_TOKENS, heads_q * head_width),
        all_tiles,
        grad_loc.reshape(blocks, BLOCK_TOKENS, heads_q * head_width),
        bias,
        heads_kv,
        score_scale,
    )
    output_block_rows = out_q.reshape(blocks, BLOCK_TOKENS, heads_q, head_width)
    query_gradient_rows = grad_q.reshape(blocks, BLOCK_TOKENS, heads_q, head_width)
    pad_spec_low = ((0, 2), (0, 0), (0, 0), (0, 0))
    pad_spec_mid = ((1, 1), (0, 0), (0, 0), (0, 0))
    pad_spec_high = ((2, 0), (0, 0), (0, 0), (0, 0))
    window_sum = (
        jnp.pad(tile_grads[:, 0], pad_spec_low)
        + jnp.pad(tile_grads[:, 1], pad_spec_mid)
        + jnp.pad(tile_grads[:, 2], pad_spec_high)
    )
    rims = jnp.concatenate([window_sum[0], window_sum[blocks + 1]], axis=1)
    returned_rims = padded(rims.astype(jnp.bfloat16), (("seq", 1),), BLOCK_TOKENS).astype(
        rims.dtype
    )
    interior = window_sum[1 : blocks + 1]
    interior = (
        interior.at[0]
        .add(returned_rims[:, :BLOCK_TOKENS])
        .at[blocks - 1]
        .add(returned_rims[:, 3 * BLOCK_TOKENS :])
    )
    global_terms = jnp.sum(tile_grads[:, 3:5], axis=0)
    global_total = tree_sum(global_terms, "seq")
    own_weight = own_global.astype(jnp.float32)[:, :, None, None, None]
    interior = interior + jnp.sum(own_weight * global_total[:, None], axis=0)
    random_terms = (
        tile_grads[:, 5:8]
        .transpose(1, 0, 2, 3, 4)
        .reshape(entry_count, 2, BLOCK_TOKENS, kv_width)
        .astype(jnp.bfloat16)
    )
    slot_onehot = (my_slot[:, None] == jnp.arange(seq_count * capacity)[None, :]).astype(
        jnp.bfloat16
    )
    back_buffer = jnp.einsum(
        "es,exbw->sxbw", slot_onehot, random_terms, preferred_element_type=jnp.float32
    ).astype(jnp.bfloat16)
    returned_terms = lax.all_to_all(back_buffer, "seq", split_axis=0, concat_axis=0, tiled=True)
    interior = interior + jnp.einsum(
        "tco,tcxbw->oxbw",
        selector,
        returned_terms.reshape(seq_count, capacity, 2, BLOCK_TOKENS, kv_width),
        preferred_element_type=jnp.float32,
    )
    kv_grad = interior.transpose(1, 0, 2, 3).reshape(2, shard_len, kv_width).astype(jnp.bfloat16)
    out_all = output_block_rows.reshape(shard_len, heads_q, head_width)
    query_grad_all = query_gradient_rows.reshape(shard_len, heads_q, head_width)
    key_grad_all = kv_grad[0].reshape(shard_len, heads_kv, head_width)
    value_grad_all = kv_grad[1].reshape(shard_len, heads_kv, head_width)
    return (
        lax.all_to_all(out_all, "head", split_axis=0, concat_axis=1, tiled=True),
        lax.all_to_all(query_grad_all, "head", split_axis=0, concat_axis=1, tiled=True),
        lax.all_to_all(key_grad_all, "head", split_axis=0, concat_axis=1, tiled=True),
        lax.all_to_all(value_grad_all, "head", split_axis=0, concat_axis=1, tiled=True),
    )


def solution(mesh):
    placed = (
        P(("seq", "head"), None, None),
        P(("seq", "head"), None, None),
        P(("seq", "head"), None, None),
        P(("seq", "head"), None, None),
        P(),
        P(),
    )
    return jax.shard_map(
        per_device,
        mesh=mesh,
        in_specs=placed,
        out_specs=(
            P(("seq", "head"), None, None),
            P(("seq", "head"), None, None),
            P(("seq", "head"), None, None),
            P(("seq", "head"), None, None),
        ),
        check_vma=False,
    )
```

```python
import functools
import math

import jax
import jax.numpy as jnp
from jax import lax
from jax.experimental import pallas as pl
from jax.sharding import PartitionSpec as P

BLOCK_TOKENS = 128


def attention_kernel(q_ref, k_ref, v_ref, do_ref, bias_ref, out_ref, dq_ref, grad_ref, *, scale):
    group = q_ref.shape[1] // q_ref.shape[0]
    width = k_ref.shape[-1]

    def rows_of(ref):
        return jnp.concatenate([ref[:, g * width:(g + 1) * width] for g in range(group)], axis=0)

    def store_rows(ref, value):
        tokens = ref.shape[0]
        for g in range(group):
            ref[:, g * width:(g + 1) * width] = value[g * tokens:(g + 1) * tokens, :]

    q = rows_of(q_ref)
    do = rows_of(do_ref)
    k = k_ref[...].reshape(-1, width)
    v = v_ref[...].reshape(-1, width)
    rows_by_cols = (((1,), (1,)), ((), ()))
    over_rows = (((0,), (0,)), ((), ()))
    s = lax.dot_general(q, k, rows_by_cols, preferred_element_type=jnp.float32) * scale
    s = s + bias_ref[...]
    e = jnp.exp(s - jnp.max(s, axis=1, keepdims=True))
    p = e / jnp.sum(e, axis=1, keepdims=True)
    p_low = p.astype(jnp.bfloat16)
    o_low = jnp.dot(p_low, v, preferred_element_type=jnp.float32).astype(jnp.bfloat16)
    store_rows(out_ref, o_low)
    delta = jnp.sum(do.astype(jnp.float32) * o_low.astype(jnp.float32), axis=1, keepdims=True)
    dp = lax.dot_general(do, v, rows_by_cols, preferred_element_type=jnp.float32)
    ds_low = (p * (dp - delta)).astype(jnp.bfloat16)
    dq = jnp.dot(ds_low, k, preferred_element_type=jnp.float32) * scale
    store_rows(dq_ref, dq.astype(jnp.bfloat16))
    dk = lax.dot_general(ds_low, q, over_rows, preferred_element_type=jnp.float32) * scale
    dv = lax.dot_general(p_low, do, over_rows, preferred_element_type=jnp.float32)
    grad_ref[:, 0] = dk.reshape(grad_ref.shape[0], -1, width)
    grad_ref[:, 1] = dv.reshape(grad_ref.shape[0], -1, width)


def attention_call(q, tiles, do, bias, heads_kv, scale):
    blocks, tokens, q_width = q.shape
    tile_count, head_width = tiles.shape[1], tiles.shape[-1] // heads_kv
    rows_width = q_width // heads_kv
    q_spec = pl.BlockSpec((None, tokens, rows_width), lambda j, h: (j, 0, h))
    k_spec = pl.BlockSpec((None, tile_count, None, tokens, head_width), lambda j, h: (j, 0, 0, 0, h))
    v_spec = pl.BlockSpec((None, tile_count, None, tokens, head_width), lambda j, h: (j, 0, 1, 0, h))
    b_spec = pl.BlockSpec((None, 1, bias.shape[-1]), lambda j, h: (j, 0, 0))
    g_spec = pl.BlockSpec((None, tile_count, 2, tokens, head_width), lambda j, h: (j, 0, 0, 0, h))
    return pl.pallas_call(
        functools.partial(attention_kernel, scale=scale),
        grid=(blocks, heads_kv),
        in_specs=[q_spec, k_spec, v_spec, q_spec, b_spec],
        out_specs=[q_spec, q_spec, g_spec],
        out_shape=[
            jax.ShapeDtypeStruct(q.shape, jnp.bfloat16),
            jax.ShapeDtypeStruct(q.shape, jnp.bfloat16),
            jax.ShapeDtypeStruct(tiles.shape, jnp.float32),
        ],
    )(q, tiles, tiles, do, bias)


def exchange(array, axis, split_axis, concat_axis):
    count = lax.axis_size(axis)
    own = lax.axis_index(axis)
    piece = array.shape[split_axis] // count
    received = []
    for shift in range(count):
        target = (own + shift) % count
        part = lax.dynamic_slice_in_dim(array, target * piece, piece, split_axis)
        if shift:
            pairs = [(i, (i + shift) % count) for i in range(count)]
            part = lax.ppermute(part, axis, pairs)
        received.append(part)
    order = (own - jnp.arange(count)) % count
    stacked = jnp.take(jnp.stack(received), order, axis=0)
    stacked = jnp.moveaxis(stacked, 0, concat_axis)
    shape = list(array.shape)
    shape[split_axis] = piece
    shape[concat_axis] *= count
    return stacked.reshape(shape)


def padded(shard, sides, width):
    for axis, dim in sides:
        count, length = (lax.axis_size(axis), shard.shape[dim])
        up = [(i, (i + 1) % count) for i in range(count - 1)]
        down = [(j, i) for i, j in up]
        last = lax.slice_in_dim(shard, length - width, length, axis=dim)
        leading = lax.slice_in_dim(shard, 0, width, axis=dim)
        before = lax.ppermute(last, axis, up)
        after = lax.ppermute(leading, axis, down)
        shard = jnp.concatenate([before, shard, after], axis=dim)
    return shard


def from_root(block, axis, owner):
    block = jnp.where(lax.axis_index(axis) == owner, block, jnp.zeros_like(block))
    return lax.psum(block, axis)


def tree_sum(part, axis):
    count = lax.axis_size(axis)
    if count & (count - 1):
        return lax.psum(part.astype(jnp.bfloat16), axis).astype(jnp.float32)
    stride = 1
    while stride < count:
        pairs = [(i, i ^ stride) for i in range(count)]
        other = lax.ppermute(part.astype(jnp.bfloat16), axis, pairs)
        part = part + other.astype(jnp.float32)
        stride *= 2
    return part


def per_device(queries, keys, values, output_gradient, global_blocks, random_blocks):
    query_loc, key_loc, value_loc, grad_loc = (
        lax.all_to_all(queries, "head", split_axis=1, concat_axis=0, tiled=True),
        lax.all_to_all(keys, "head", split_axis=1, concat_axis=0, tiled=True),
        lax.all_to_all(values, "head", split_axis=1, concat_axis=0, tiled=True),
        lax.all_to_all(output_gradient, "head", split_axis=1, concat_axis=0, tiled=True),
    )
    shard_len, heads_q, head_width = query_loc.shape
    heads_kv = key_loc.shape[1]
    heads_per_group = heads_q // heads_kv
    kv_width = heads_kv * head_width
    blocks = shard_len // BLOCK_TOKENS
    seq_count = lax.axis_size("seq")
    own_index = lax.axis_index("seq")
    block_total_count = seq_count * blocks
    capacity = (3 * blocks + seq_count - 2) // (seq_count - 1)
    entry_count = 3 * blocks
    score_scale = 1.0 / math.sqrt(head_width)
    kv_pair = jnp.stack(
        [key_loc.reshape(shard_len, kv_width), value_loc.reshape(shard_len, kv_width)]
    )
    extended = padded(kv_pair, (("seq", 1),), BLOCK_TOKENS)
    kv_tiles = kv_pair.reshape(2, blocks, BLOCK_TOKENS, kv_width).transpose(1, 0, 2, 3)
    global_owner = global_blocks // blocks
    global_offset = global_blocks % blocks
    own_global = (jnp.arange(blocks)[None, :] == global_offset[:, None]) & (
        global_owner == own_index
    )[:, None]
    all_entries = (
        random_blocks.reshape(seq_count, blocks, 3)
        .transpose(0, 2, 1)
        .reshape(seq_count, entry_count)
    )
    all_owner = all_entries // blocks
    entry_ids = jnp.arange(entry_count)
    entry_earlier = entry_ids[None, :] < entry_ids[:, None]
    all_rank = jnp.sum(
        (all_owner[:, :, None] == all_owner[:, None, :]) & entry_earlier[None], axis=2
    )
    my_entries = lax.dynamic_index_in_dim(all_entries, own_index, 0, keepdims=False)
    my_owner = lax.dynamic_index_in_dim(all_owner, own_index, 0, keepdims=False)
    my_rank = lax.dynamic_index_in_dim(all_rank, own_index, 0, keepdims=False)
    my_slot = my_owner * capacity + my_rank
    owned_here = (all_owner == own_index)[:, :, None] & (
        all_rank[:, :, None] == jnp.arange(capacity)[None, None, :]
    )
    offset_match = (all_entries % blocks)[:, :, None] == jnp.arange(blocks)[None, None, :]
    selector = jnp.einsum(
        "tec,teo->tco",
        owned_here.astype(jnp.bfloat16),
        offset_match.astype(jnp.bfloat16),
        preferred_element_type=jnp.float32,
    ).astype(jnp.bfloat16)
    everything = lax.all_gather(kv_pair, "seq", axis=1, tiled=True)
    tiled_all = everything.reshape(2, block_total_count, BLOCK_TOKENS, kv_width)
    random_tiles = jnp.take(tiled_all, my_entries, axis=1).transpose(1, 0, 2, 3)
    global_tiles = jnp.take(tiled_all, global_blocks, axis=1).transpose(1, 0, 2, 3)
    random_by_block = random_tiles.reshape(3, blocks, 2, BLOCK_TOKENS, kv_width).transpose(
        1, 0, 2, 3, 4
    )
    block_ids = own_index * blocks + jnp.arange(blocks)
    listed = jnp.concatenate(
        [
            jnp.stack([block_ids - 1, block_ids, block_ids + 1], axis=1),
            jnp.broadcast_to(global_blocks[None, :], (blocks, 2)),
            my_entries.reshape(3, blocks).T,
        ],
        axis=1,
    )
    inside = (listed >= 0) & (listed < block_total_count)
    tile_ids = jnp.arange(8)
    tile_earlier = tile_ids[None, :] < tile_ids[:, None]
    repeat = jnp.any((listed[:, :, None] == listed[:, None, :]) & tile_earlier[None], axis=2)
    live = inside & jnp.logical_not(repeat)

    tiles_per_block = []
    for position in range(blocks):
        near_tiles = lax.slice_in_dim(
            extended, position * BLOCK_TOKENS, (position + 3) * BLOCK_TOKENS, axis=1
        )
        near_tiles = near_tiles.reshape(2, 3, BLOCK_TOKENS, kv_width).transpose(1, 0, 2, 3)
        tiles_per_block.append(
            jnp.concatenate([near_tiles, global_tiles, random_by_block[position]], axis=0)
        )
    all_tiles = jnp.stack(tiles_per_block)
    tile_count = all_tiles.shape[1]
    bias = jnp.where(live, 0.0, -jnp.inf).astype(jnp.float32)
    bias = jnp.repeat(bias, BLOCK_TOKENS, axis=1).reshape(blocks, 1, tile_count * BLOCK_TOKENS)
    out_q, grad_q, tile_grads = attention_call(
        query_loc.reshape(blocks, BLOCK_TOKENS, heads_q * head_width),
        all_tiles,
        grad_loc.reshape(blocks, BLOCK_TOKENS, heads_q * head_width),
        bias,
        heads_kv,
        score_scale,
    )
    output_block_rows = out_q.reshape(blocks, BLOCK_TOKENS, heads_q, head_width)
    query_gradient_rows = grad_q.reshape(blocks, BLOCK_TOKENS, heads_q, head_width)
    pad_spec_low = ((0, 2), (0, 0), (0, 0), (0, 0))
    pad_spec_mid = ((1, 1), (0, 0), (0, 0), (0, 0))
    pad_spec_high = ((2, 0), (0, 0), (0, 0), (0, 0))
    window_sum = (
        jnp.pad(tile_grads[:, 0], pad_spec_low)
        + jnp.pad(tile_grads[:, 1], pad_spec_mid)
        + jnp.pad(tile_grads[:, 2], pad_spec_high)
    )
    rims = jnp.concatenate([window_sum[0], window_sum[blocks + 1]], axis=1)
    returned_rims = padded(rims.astype(jnp.bfloat16), (("seq", 1),), BLOCK_TOKENS).astype(
        rims.dtype
    )
    interior = window_sum[1 : blocks + 1]
    interior = (
        interior.at[0]
        .add(returned_rims[:, :BLOCK_TOKENS])
        .at[blocks - 1]
        .add(returned_rims[:, 3 * BLOCK_TOKENS :])
    )
    global_terms = jnp.sum(tile_grads[:, 3:5], axis=0)
    global_total = tree_sum(global_terms, "seq")
    own_weight = own_global.astype(jnp.float32)[:, :, None, None, None]
    interior = interior + jnp.sum(own_weight * global_total[:, None], axis=0)
    random_terms = (
        tile_grads[:, 5:8]
        .transpose(1, 0, 2, 3, 4)
        .reshape(entry_count, 2, BLOCK_TOKENS, kv_width)
        .astype(jnp.bfloat16)
    )
    slot_onehot = (my_slot[:, None] == jnp.arange(seq_count * capacity)[None, :]).astype(
        jnp.bfloat16
    )
    back_buffer = jnp.einsum(
        "es,exbw->sxbw", slot_onehot, random_terms, preferred_element_type=jnp.float32
    ).astype(jnp.bfloat16)
    returned_terms = exchange(back_buffer, "seq", 0, 0)
    interior = interior + jnp.einsum(
        "tco,tcxbw->oxbw",
        selector,
        returned_terms.reshape(seq_count, capacity, 2, BLOCK_TOKENS, kv_width),
        preferred_element_type=jnp.float32,
    )
    kv_grad = interior.transpose(1, 0, 2, 3).reshape(2, shard_len, kv_width).astype(jnp.bfloat16)
    out_all = output_block_rows.reshape(shard_len, heads_q, head_width)
    query_grad_all = query_gradient_rows.reshape(shard_len, heads_q, head_width)
    key_grad_all = kv_grad[0].reshape(shard_len, heads_kv, head_width)
    value_grad_all = kv_grad[1].reshape(shard_len, heads_kv, head_width)
    out_back = lax.all_to_all(out_all, "head", split_axis=0, concat_axis=1, tiled=True)
    query_back = lax.all_to_all(query_grad_all, "head", split_axis=0, concat_axis=1, tiled=True)
    (out_back, query_back), kv_grad = lax.optimization_barrier(((out_back, query_back), kv_grad))
    kv_grad = kv_grad.reshape(2, shard_len, heads_kv, head_width)
    kv_back = lax.all_to_all(kv_grad, "head", split_axis=1, concat_axis=2, tiled=True)
    return (out_back, query_back, kv_back[0], kv_back[1])


def solution(mesh):
    placed = (
        P(("seq", "head"), None, None),
        P(("seq", "head"), None, None),
        P(("seq", "head"), None, None),
        P(("seq", "head"), None, None),
        P(),
        P(),
    )
    return jax.shard_map(
        per_device,
        mesh=mesh,
        in_specs=placed,
        out_specs=(
            P(("seq", "head"), None, None),
            P(("seq", "head"), None, None),
            P(("seq", "head"), None, None),
            P(("seq", "head"), None, None),
        ),
        check_vma=False,
    )
```

```python
import functools
import math

import jax
import jax.numpy as jnp
from jax import lax
from jax.experimental import pallas as pl
from jax.sharding import PartitionSpec as P

BLOCK_TOKENS = 128


def rows_of(ref, group, width):
    return jnp.concatenate([ref[:, g * width:(g + 1) * width] for g in range(group)], axis=0)


def store_rows(ref, value, group, width):
    tokens = ref.shape[0]
    for g in range(group):
        ref[:, g * width:(g + 1) * width] = value[g * tokens:(g + 1) * tokens, :]


def softmax_rows(q, k, bias, scale):
    rows_by_cols = (((1,), (1,)), ((), ()))
    s = lax.dot_general(q, k, rows_by_cols, preferred_element_type=jnp.float32) * scale
    s = s + bias
    e = jnp.exp(s - jnp.max(s, axis=1, keepdims=True))
    return e / jnp.sum(e, axis=1, keepdims=True)


def forward_kernel(q_ref, k_ref, v_ref, bias_ref, out_ref, *, scale):
    group = q_ref.shape[1] // q_ref.shape[0]
    width = k_ref.shape[-1]
    q = rows_of(q_ref, group, width)
    k = k_ref[...].reshape(-1, width)
    v = v_ref[...].reshape(-1, width)
    p_low = softmax_rows(q, k, bias_ref[...], scale).astype(jnp.bfloat16)
    o_low = jnp.dot(p_low, v, preferred_element_type=jnp.float32).astype(jnp.bfloat16)
    store_rows(out_ref, o_low, group, width)


def backward_kernel(q_ref, k_ref, v_ref, do_ref, o_ref, bias_ref, dq_ref, grad_ref, *, scale):
    group = q_ref.shape[1] // q_ref.shape[0]
    width = k_ref.shape[-1]
    q = rows_of(q_ref, group, width)
    do = rows_of(do_ref, group, width)
    o_low = rows_of(o_ref, group, width)
    k = k_ref[...].reshape(-1, width)
    v = v_ref[...].reshape(-1, width)
    rows_by_cols = (((1,), (1,)), ((), ()))
    over_rows = (((0,), (0,)), ((), ()))
    p = softmax_rows(q, k, bias_ref[...], scale)
    p_low = p.astype(jnp.bfloat16)
    delta = jnp.sum(do.astype(jnp.float32) * o_low.astype(jnp.float32), axis=1, keepdims=True)
    dp = lax.dot_general(do, v, rows_by_cols, preferred_element_type=jnp.float32)
    ds_low = (p * (dp - delta)).astype(jnp.bfloat16)
    dq = jnp.dot(ds_low, k, preferred_element_type=jnp.float32) * scale
    store_rows(dq_ref, dq.astype(jnp.bfloat16), group, width)
    dk = lax.dot_general(ds_low, q, over_rows, preferred_element_type=jnp.float32) * scale
    dv = lax.dot_general(p_low, do, over_rows, preferred_element_type=jnp.float32)
    grad_ref[:, 0] = dk.reshape(grad_ref.shape[0], -1, width)
    grad_ref[:, 1] = dv.reshape(grad_ref.shape[0], -1, width)


def attention_call(q, tiles, do, bias, heads_kv, scale):
    blocks, tokens, q_width = q.shape
    tile_count, head_width = tiles.shape[1], tiles.shape[-1] // heads_kv
    rows_width = q_width // heads_kv
    q_spec = pl.BlockSpec((None, tokens, rows_width), lambda j, h: (j, 0, h))
    k_spec = pl.BlockSpec((None, tile_count, None, tokens, head_width), lambda j, h: (j, 0, 0, 0, h))
    v_spec = pl.BlockSpec((None, tile_count, None, tokens, head_width), lambda j, h: (j, 0, 1, 0, h))
    b_spec = pl.BlockSpec((None, 1, bias.shape[-1]), lambda j, h: (j, 0, 0))
    g_spec = pl.BlockSpec((None, tile_count, 2, tokens, head_width), lambda j, h: (j, 0, 0, 0, h))
    steps = blocks * heads_kv
    rows = tokens * (rows_width // head_width)
    keys_n = tile_count * tokens
    matmul = 2 * rows * keys_n * head_width * steps
    moved = 2 * (3 * q.size + 2 * tiles.size) + 4 * tiles.size
    out = pl.pallas_call(
        functools.partial(forward_kernel, scale=scale),
        cost_estimate=pl.CostEstimate(
            flops=2 * matmul, transcendentals=rows * keys_n * steps, bytes_accessed=moved
        ),
        grid=(blocks, heads_kv),
        in_specs=[q_spec, k_spec, v_spec, b_spec],
        out_specs=q_spec,
        out_shape=jax.ShapeDtypeStruct(q.shape, jnp.bfloat16),
    )(q, tiles, tiles, bias)
    out, do = lax.optimization_barrier((out, do))
    grad_q, grads = pl.pallas_call(
        functools.partial(backward_kernel, scale=scale),
        cost_estimate=pl.CostEstimate(
            flops=5 * matmul, transcendentals=rows * keys_n * steps, bytes_accessed=moved
        ),
        grid=(blocks, heads_kv),
        in_specs=[q_spec, k_spec, v_spec, q_spec, q_spec, b_spec],
        out_specs=[q_spec, g_spec],
        out_shape=[
            jax.ShapeDtypeStruct(q.shape, jnp.bfloat16),
            jax.ShapeDtypeStruct(tiles.shape, jnp.float32),
        ],
    )(q, tiles, tiles, do, out, bias)
    return out, grad_q, grads


def exchange(array, axis, split_axis, concat_axis):
    count = lax.axis_size(axis)
    own = lax.axis_index(axis)
    piece = array.shape[split_axis] // count
    received = []
    for shift in range(count):
        target = (own + shift) % count
        part = lax.dynamic_slice_in_dim(array, target * piece, piece, split_axis)
        if shift:
            pairs = [(i, (i + shift) % count) for i in range(count)]
            part = lax.ppermute(part, axis, pairs)
        received.append(part)
    order = (own - jnp.arange(count)) % count
    stacked = jnp.take(jnp.stack(received), order, axis=0)
    stacked = jnp.moveaxis(stacked, 0, concat_axis)
    shape = list(array.shape)
    shape[split_axis] = piece
    shape[concat_axis] *= count
    return stacked.reshape(shape)


def padded(shard, sides, width):
    for axis, dim in sides:
        count, length = (lax.axis_size(axis), shard.shape[dim])
        up = [(i, (i + 1) % count) for i in range(count - 1)]
        down = [(j, i) for i, j in up]
        last = lax.slice_in_dim(shard, length - width, length, axis=dim)
        leading = lax.slice_in_dim(shard, 0, width, axis=dim)
        before = lax.ppermute(last, axis, up)
        after = lax.ppermute(leading, axis, down)
        shard = jnp.concatenate([before, shard, after], axis=dim)
    return shard


def from_root(block, axis, owner):
    block = jnp.where(lax.axis_index(axis) == owner, block, jnp.zeros_like(block))
    return lax.psum(block, axis)


def tree_sum(part, axis):
    count = lax.axis_size(axis)
    if count & (count - 1):
        return lax.psum(part.astype(jnp.bfloat16), axis).astype(jnp.float32)
    stride = 1
    while stride < count:
        pairs = [(i, i ^ stride) for i in range(count)]
        other = lax.ppermute(part.astype(jnp.bfloat16), axis, pairs)
        part = part + other.astype(jnp.float32)
        stride *= 2
    return part


def per_device(queries, keys, values, output_gradient, global_blocks, random_blocks):
    query_loc, key_loc, value_loc, grad_loc = (
        lax.all_to_all(queries, "head", split_axis=1, concat_axis=0, tiled=True),
        lax.all_to_all(keys, "head", split_axis=1, concat_axis=0, tiled=True),
        lax.all_to_all(values, "head", split_axis=1, concat_axis=0, tiled=True),
        output_gradient,
    )
    shard_len, heads_q, head_width = query_loc.shape
    heads_kv = key_loc.shape[1]
    heads_per_group = heads_q // heads_kv
    kv_width = heads_kv * head_width
    blocks = shard_len // BLOCK_TOKENS
    seq_count = lax.axis_size("seq")
    own_index = lax.axis_index("seq")
    block_total_count = seq_count * blocks
    capacity = (3 * blocks + seq_count - 2) // (seq_count - 1)
    entry_count = 3 * blocks
    score_scale = 1.0 / math.sqrt(head_width)
    kv_pair = jnp.stack(
        [key_loc.reshape(shard_len, kv_width), value_loc.reshape(shard_len, kv_width)]
    )
    extended = padded(kv_pair, (("seq", 1),), BLOCK_TOKENS)
    kv_tiles = kv_pair.reshape(2, blocks, BLOCK_TOKENS, kv_width).transpose(1, 0, 2, 3)
    global_owner = global_blocks // blocks
    global_offset = global_blocks % blocks
    own_global = (jnp.arange(blocks)[None, :] == global_offset[:, None]) & (
        global_owner == own_index
    )[:, None]
    all_entries = (
        random_blocks.reshape(seq_count, blocks, 3)
        .transpose(0, 2, 1)
        .reshape(seq_count, entry_count)
    )
    all_owner = all_entries // blocks
    entry_ids = jnp.arange(entry_count)
    entry_earlier = entry_ids[None, :] < entry_ids[:, None]
    all_rank = jnp.sum(
        (all_owner[:, :, None] == all_owner[:, None, :]) & entry_earlier[None], axis=2
    )
    my_entries = lax.dynamic_index_in_dim(all_entries, own_index, 0, keepdims=False)
    my_owner = lax.dynamic_index_in_dim(all_owner, own_index, 0, keepdims=False)
    my_rank = lax.dynamic_index_in_dim(all_rank, own_index, 0, keepdims=False)
    my_slot = my_owner * capacity + my_rank
    owned_here = (all_owner == own_index)[:, :, None] & (
        all_rank[:, :, None] == jnp.arange(capacity)[None, None, :]
    )
    offset_match = (all_entries % blocks)[:, :, None] == jnp.arange(blocks)[None, None, :]
    selector = jnp.einsum(
        "tec,teo->tco",
        owned_here.astype(jnp.bfloat16),
        offset_match.astype(jnp.bfloat16),
        preferred_element_type=jnp.float32,
    ).astype(jnp.bfloat16)
    everything = lax.all_gather(kv_pair, "seq", axis=1, tiled=True)
    query_loc, everything, grad_loc = lax.optimization_barrier((query_loc, everything, grad_loc))
    grad_loc = lax.all_to_all(grad_loc, "head", split_axis=1, concat_axis=0, tiled=True)
    tiled_all = everything.reshape(2, block_total_count, BLOCK_TOKENS, kv_width)
    random_tiles = jnp.take(tiled_all, my_entries, axis=1).transpose(1, 0, 2, 3)
    global_tiles = jnp.take(tiled_all, global_blocks, axis=1).transpose(1, 0, 2, 3)
    random_by_block = random_tiles.reshape(3, blocks, 2, BLOCK_TOKENS, kv_width).transpose(
        1, 0, 2, 3, 4
    )
    block_ids = own_index * blocks + jnp.arange(blocks)
    listed = jnp.concatenate(
        [
            jnp.stack([block_ids - 1, block_ids, block_ids + 1], axis=1),
            jnp.broadcast_to(global_blocks[None, :], (blocks, 2)),
            my_entries.reshape(3, blocks).T,
        ],
        axis=1,
    )
    inside = (listed >= 0) & (listed < block_total_count)
    tile_ids = jnp.arange(8)
    tile_earlier = tile_ids[None, :] < tile_ids[:, None]
    repeat = jnp.any((listed[:, :, None] == listed[:, None, :]) & tile_earlier[None], axis=2)
    live = inside & jnp.logical_not(repeat)

    tiles_per_block = []
    for position in range(blocks):
        near_tiles = lax.slice_in_dim(
            extended, position * BLOCK_TOKENS, (position + 3) * BLOCK_TOKENS, axis=1
        )
        near_tiles = near_tiles.reshape(2, 3, BLOCK_TOKENS, kv_width).transpose(1, 0, 2, 3)
        tiles_per_block.append(
            jnp.concatenate([near_tiles, global_tiles, random_by_block[position]], axis=0)
        )
    all_tiles = jnp.stack(tiles_per_block)
    tile_count = all_tiles.shape[1]
    bias = jnp.where(live, 0.0, -jnp.inf).astype(jnp.float32)
    bias = jnp.repeat(bias, BLOCK_TOKENS, axis=1).reshape(blocks, 1, tile_count * BLOCK_TOKENS)
    out_q, grad_q, tile_grads = attention_call(
        query_loc.reshape(blocks, BLOCK_TOKENS, heads_q * head_width),
        all_tiles,
        grad_loc.reshape(blocks, BLOCK_TOKENS, heads_q * head_width),
        bias,
        heads_kv,
        score_scale,
    )
    output_block_rows = out_q.reshape(blocks, BLOCK_TOKENS, heads_q, head_width)
    query_gradient_rows = grad_q.reshape(blocks, BLOCK_TOKENS, heads_q, head_width)
    pad_spec_low = ((0, 2), (0, 0), (0, 0), (0, 0))
    pad_spec_mid = ((1, 1), (0, 0), (0, 0), (0, 0))
    pad_spec_high = ((2, 0), (0, 0), (0, 0), (0, 0))
    window_sum = (
        jnp.pad(tile_grads[:, 0], pad_spec_low)
        + jnp.pad(tile_grads[:, 1], pad_spec_mid)
        + jnp.pad(tile_grads[:, 2], pad_spec_high)
    )
    rims = jnp.concatenate([window_sum[0], window_sum[blocks + 1]], axis=1)
    returned_rims = padded(rims.astype(jnp.bfloat16), (("seq", 1),), BLOCK_TOKENS).astype(
        rims.dtype
    )
    interior = window_sum[1 : blocks + 1]
    interior = (
        interior.at[0]
        .add(returned_rims[:, :BLOCK_TOKENS])
        .at[blocks - 1]
        .add(returned_rims[:, 3 * BLOCK_TOKENS :])
    )
    global_terms = jnp.sum(tile_grads[:, 3:5], axis=0)
    global_total = tree_sum(global_terms, "seq")
    own_weight = own_global.astype(jnp.float32)[:, :, None, None, None]
    interior = interior + jnp.sum(own_weight * global_total[:, None], axis=0)
    random_terms = (
        tile_grads[:, 5:8]
        .transpose(1, 0, 2, 3, 4)
        .reshape(entry_count, 2, BLOCK_TOKENS, kv_width)
        .astype(jnp.bfloat16)
    )
    slot_onehot = (my_slot[:, None] == jnp.arange(seq_count * capacity)[None, :]).astype(
        jnp.bfloat16
    )
    back_buffer = jnp.einsum(
        "es,exbw->sxbw", slot_onehot, random_terms, preferred_element_type=jnp.float32
    ).astype(jnp.bfloat16)
    returned_terms = exchange(back_buffer, "seq", 0, 0)
    interior = interior + jnp.einsum(
        "tco,tcxbw->oxbw",
        selector,
        returned_terms.reshape(seq_count, capacity, 2, BLOCK_TOKENS, kv_width),
        preferred_element_type=jnp.float32,
    )
    kv_grad = interior.transpose(1, 0, 2, 3).reshape(2, shard_len, kv_width).astype(jnp.bfloat16)
    out_all = output_block_rows.reshape(shard_len, heads_q, head_width)
    query_grad_all = query_gradient_rows.reshape(shard_len, heads_q, head_width)
    key_grad_all = kv_grad[0].reshape(shard_len, heads_kv, head_width)
    value_grad_all = kv_grad[1].reshape(shard_len, heads_kv, head_width)
    out_back = lax.all_to_all(out_all, "head", split_axis=0, concat_axis=1, tiled=True)
    query_back = lax.all_to_all(query_grad_all, "head", split_axis=0, concat_axis=1, tiled=True)
    (out_back, query_back), kv_grad = lax.optimization_barrier(((out_back, query_back), kv_grad))
    kv_grad = kv_grad.reshape(2, shard_len, heads_kv, head_width)
    kv_back = lax.all_to_all(kv_grad, "head", split_axis=1, concat_axis=2, tiled=True)
    return (out_back, query_back, kv_back[0], kv_back[1])


def solution(mesh):
    placed = (
        P(("seq", "head"), None, None),
        P(("seq", "head"), None, None),
        P(("seq", "head"), None, None),
        P(("seq", "head"), None, None),
        P(),
        P(),
    )
    return jax.shard_map(
        per_device,
        mesh=mesh,
        in_specs=placed,
        out_specs=(
            P(("seq", "head"), None, None),
            P(("seq", "head"), None, None),
            P(("seq", "head"), None, None),
            P(("seq", "head"), None, None),
        ),
        check_vma=False,
    )
```

```python
import functools
import math

import jax
import jax.numpy as jnp
from jax import lax
from jax.experimental import pallas as pl
from jax.sharding import PartitionSpec as P

BLOCK_TOKENS = 128


def rows_of(ref, group, width):
    return jnp.concatenate([ref[:, g * width:(g + 1) * width] for g in range(group)], axis=0)


def store_rows(ref, value, group, width):
    tokens = ref.shape[0]
    for g in range(group):
        ref[:, g * width:(g + 1) * width] = value[g * tokens:(g + 1) * tokens, :]


def softmax_rows(q, k, bias, scale):
    rows_by_cols = (((1,), (1,)), ((), ()))
    s = lax.dot_general(q, k, rows_by_cols, preferred_element_type=jnp.float32) * scale
    s = s + bias
    e = jnp.exp(s - jnp.max(s, axis=1, keepdims=True))
    return e / jnp.sum(e, axis=1, keepdims=True)


def forward_kernel(q_ref, k_ref, v_ref, bias_ref, out_ref, *, scale):
    group = q_ref.shape[1] // q_ref.shape[0]
    width = k_ref.shape[-1]
    q = rows_of(q_ref, group, width)
    k = k_ref[...].reshape(-1, width)
    v = v_ref[...].reshape(-1, width)
    p_low = softmax_rows(q, k, bias_ref[...], scale).astype(jnp.bfloat16)
    o_low = jnp.dot(p_low, v, preferred_element_type=jnp.float32).astype(jnp.bfloat16)
    store_rows(out_ref, o_low, group, width)


def backward_kernel(q_ref, k_ref, v_ref, do_ref, o_ref, bias_ref, dq_ref, grad_ref, *, scale):
    group = q_ref.shape[1] // q_ref.shape[0]
    width = k_ref.shape[-1]
    q = rows_of(q_ref, group, width)
    do = rows_of(do_ref, group, width)
    o_low = rows_of(o_ref, group, width)
    k = k_ref[...].reshape(-1, width)
    v = v_ref[...].reshape(-1, width)
    rows_by_cols = (((1,), (1,)), ((), ()))
    over_rows = (((0,), (0,)), ((), ()))
    p = softmax_rows(q, k, bias_ref[...], scale)
    p_low = p.astype(jnp.bfloat16)
    delta = jnp.sum(do.astype(jnp.float32) * o_low.astype(jnp.float32), axis=1, keepdims=True)
    dp = lax.dot_general(do, v, rows_by_cols, preferred_element_type=jnp.float32)
    ds_low = (p * (dp - delta)).astype(jnp.bfloat16)
    dq = jnp.dot(ds_low, k, preferred_element_type=jnp.float32) * scale
    store_rows(dq_ref, dq.astype(jnp.bfloat16), group, width)
    dk = lax.dot_general(ds_low, q, over_rows, preferred_element_type=jnp.float32) * scale
    dv = lax.dot_general(p_low, do, over_rows, preferred_element_type=jnp.float32)
    grad_ref[:, 0] = dk.reshape(grad_ref.shape[0], -1, width)
    grad_ref[:, 1] = dv.reshape(grad_ref.shape[0], -1, width)


def attention_call(q, tiles, do, bias, heads_kv, scale):
    blocks, tokens, q_width = q.shape
    tile_count, head_width = tiles.shape[1], tiles.shape[-1] // heads_kv
    rows_width = q_width // heads_kv
    q_spec = pl.BlockSpec((None, tokens, rows_width), lambda j, h: (j, 0, h))
    k_spec = pl.BlockSpec((None, tile_count, None, tokens, head_width), lambda j, h: (j, 0, 0, 0, h))
    v_spec = pl.BlockSpec((None, tile_count, None, tokens, head_width), lambda j, h: (j, 0, 1, 0, h))
    b_spec = pl.BlockSpec((None, 1, bias.shape[-1]), lambda j, h: (j, 0, 0))
    g_spec = pl.BlockSpec((None, tile_count, 2, tokens, head_width), lambda j, h: (j, 0, 0, 0, h))
    steps = blocks * heads_kv
    rows = tokens * (rows_width // head_width)
    keys_n = tile_count * tokens
    matmul = 2 * rows * keys_n * head_width * steps
    moved = 2 * (3 * q.size + 2 * tiles.size) + 4 * tiles.size
    out = pl.pallas_call(
        functools.partial(forward_kernel, scale=scale),
        cost_estimate=pl.CostEstimate(
            flops=2 * matmul, transcendentals=rows * keys_n * steps, bytes_accessed=moved
        ),
        grid=(blocks, heads_kv),
        in_specs=[q_spec, k_spec, v_spec, b_spec],
        out_specs=q_spec,
        out_shape=jax.ShapeDtypeStruct(q.shape, jnp.bfloat16),
    )(q, tiles, tiles, bias)
    out, do = lax.optimization_barrier((out, do))
    grad_q, grads = pl.pallas_call(
        functools.partial(backward_kernel, scale=scale),
        cost_estimate=pl.CostEstimate(
            flops=5 * matmul, transcendentals=rows * keys_n * steps, bytes_accessed=moved
        ),
        grid=(blocks, heads_kv),
        in_specs=[q_spec, k_spec, v_spec, q_spec, q_spec, b_spec],
        out_specs=[q_spec, g_spec],
        out_shape=[
            jax.ShapeDtypeStruct(q.shape, jnp.bfloat16),
            jax.ShapeDtypeStruct(tiles.shape, jnp.float32),
        ],
    )(q, tiles, tiles, do, out, bias)
    return out, grad_q, grads


def exchange(array, axis, split_axis, concat_axis):
    count = lax.axis_size(axis)
    own = lax.axis_index(axis)
    piece = array.shape[split_axis] // count
    received = []
    for shift in range(count):
        target = (own + shift) % count
        part = lax.dynamic_slice_in_dim(array, target * piece, piece, split_axis)
        if shift:
            pairs = [(i, (i + shift) % count) for i in range(count)]
            part = lax.ppermute(part, axis, pairs)
        received.append(part)
    order = (own - jnp.arange(count)) % count
    stacked = jnp.take(jnp.stack(received), order, axis=0)
    stacked = jnp.moveaxis(stacked, 0, concat_axis)
    shape = list(array.shape)
    shape[split_axis] = piece
    shape[concat_axis] *= count
    return stacked.reshape(shape)


def padded(shard, sides, width):
    for axis, dim in sides:
        count, length = (lax.axis_size(axis), shard.shape[dim])
        up = [(i, (i + 1) % count) for i in range(count - 1)]
        down = [(j, i) for i, j in up]
        last = lax.slice_in_dim(shard, length - width, length, axis=dim)
        leading = lax.slice_in_dim(shard, 0, width, axis=dim)
        before = lax.ppermute(last, axis, up)
        after = lax.ppermute(leading, axis, down)
        shard = jnp.concatenate([before, shard, after], axis=dim)
    return shard


def from_root(block, axis, owner):
    block = jnp.where(lax.axis_index(axis) == owner, block, jnp.zeros_like(block))
    return lax.psum(block, axis)


def tree_sum(part, axis):
    count = lax.axis_size(axis)
    if count & (count - 1):
        return lax.psum(part.astype(jnp.bfloat16), axis).astype(jnp.float32)
    stride = 1
    while stride < count:
        pairs = [(i, i ^ stride) for i in range(count)]
        other = lax.ppermute(part.astype(jnp.bfloat16), axis, pairs)
        part = part + other.astype(jnp.float32)
        stride *= 2
    return part


def per_device(queries, keys, values, output_gradient, global_blocks, random_blocks):
    kv_loc = lax.all_to_all(
        jnp.stack([keys, values], axis=2), "head", split_axis=1, concat_axis=0, tiled=True
    )
    key_loc, value_loc = kv_loc[:, :, 0], kv_loc[:, :, 1]
    query_loc = lax.all_to_all(queries, "head", split_axis=1, concat_axis=0, tiled=True)
    grad_loc = output_gradient
    shard_len, heads_q, head_width = query_loc.shape
    heads_kv = key_loc.shape[1]
    heads_per_group = heads_q // heads_kv
    kv_width = heads_kv * head_width
    blocks = shard_len // BLOCK_TOKENS
    seq_count = lax.axis_size("seq")
    own_index = lax.axis_index("seq")
    block_total_count = seq_count * blocks
    capacity = (3 * blocks + seq_count - 2) // (seq_count - 1)
    entry_count = 3 * blocks
    score_scale = 1.0 / math.sqrt(head_width)
    kv_pair = jnp.stack(
        [key_loc.reshape(shard_len, kv_width), value_loc.reshape(shard_len, kv_width)]
    )
    extended = padded(kv_pair, (("seq", 1),), BLOCK_TOKENS)
    kv_tiles = kv_pair.reshape(2, blocks, BLOCK_TOKENS, kv_width).transpose(1, 0, 2, 3)
    global_owner = global_blocks // blocks
    global_offset = global_blocks % blocks
    own_global = (jnp.arange(blocks)[None, :] == global_offset[:, None]) & (
        global_owner == own_index
    )[:, None]
    all_entries = (
        random_blocks.reshape(seq_count, blocks, 3)
        .transpose(0, 2, 1)
        .reshape(seq_count, entry_count)
    )
    all_owner = all_entries // blocks
    entry_ids = jnp.arange(entry_count)
    entry_earlier = entry_ids[None, :] < entry_ids[:, None]
    all_rank = jnp.sum(
        (all_owner[:, :, None] == all_owner[:, None, :]) & entry_earlier[None], axis=2
    )
    my_entries = lax.dynamic_index_in_dim(all_entries, own_index, 0, keepdims=False)
    my_owner = lax.dynamic_index_in_dim(all_owner, own_index, 0, keepdims=False)
    my_rank = lax.dynamic_index_in_dim(all_rank, own_index, 0, keepdims=False)
    my_slot = my_owner * capacity + my_rank
    owned_here = (all_owner == own_index)[:, :, None] & (
        all_rank[:, :, None] == jnp.arange(capacity)[None, None, :]
    )
    offset_match = (all_entries % blocks)[:, :, None] == jnp.arange(blocks)[None, None, :]
    selector = jnp.einsum(
        "tec,teo->tco",
        owned_here.astype(jnp.bfloat16),
        offset_match.astype(jnp.bfloat16),
        preferred_element_type=jnp.float32,
    ).astype(jnp.bfloat16)
    everything = lax.all_gather(kv_pair, "seq", axis=1, tiled=True)
    query_loc, everything, grad_loc = lax.optimization_barrier((query_loc, everything, grad_loc))
    grad_loc = lax.all_to_all(grad_loc, "head", split_axis=1, concat_axis=0, tiled=True)
    tiled_all = everything.reshape(2, block_total_count, BLOCK_TOKENS, kv_width)
    random_tiles = jnp.take(tiled_all, my_entries, axis=1).transpose(1, 0, 2, 3)
    global_tiles = jnp.take(tiled_all, global_blocks, axis=1).transpose(1, 0, 2, 3)
    random_by_block = random_tiles.reshape(3, blocks, 2, BLOCK_TOKENS, kv_width).transpose(
        1, 0, 2, 3, 4
    )
    block_ids = own_index * blocks + jnp.arange(blocks)
    listed = jnp.concatenate(
        [
            jnp.stack([block_ids - 1, block_ids, block_ids + 1], axis=1),
            jnp.broadcast_to(global_blocks[None, :], (blocks, 2)),
            my_entries.reshape(3, blocks).T,
        ],
        axis=1,
    )
    inside = (listed >= 0) & (listed < block_total_count)
    tile_ids = jnp.arange(8)
    tile_earlier = tile_ids[None, :] < tile_ids[:, None]
    repeat = jnp.any((listed[:, :, None] == listed[:, None, :]) & tile_earlier[None], axis=2)
    live = inside & jnp.logical_not(repeat)

    tiles_per_block = []
    for position in range(blocks):
        near_tiles = lax.slice_in_dim(
            extended, position * BLOCK_TOKENS, (position + 3) * BLOCK_TOKENS, axis=1
        )
        near_tiles = near_tiles.reshape(2, 3, BLOCK_TOKENS, kv_width).transpose(1, 0, 2, 3)
        tiles_per_block.append(
            jnp.concatenate([near_tiles, global_tiles, random_by_block[position]], axis=0)
        )
    all_tiles = jnp.stack(tiles_per_block)
    tile_count = all_tiles.shape[1]
    bias = jnp.where(live, 0.0, -jnp.inf).astype(jnp.float32)
    bias = jnp.repeat(bias, BLOCK_TOKENS, axis=1).reshape(blocks, 1, tile_count * BLOCK_TOKENS)
    out_q, grad_q, tile_grads = attention_call(
        query_loc.reshape(blocks, BLOCK_TOKENS, heads_q * head_width),
        all_tiles,
        grad_loc.reshape(blocks, BLOCK_TOKENS, heads_q * head_width),
        bias,
        heads_kv,
        score_scale,
    )
    output_block_rows = out_q.reshape(blocks, BLOCK_TOKENS, heads_q, head_width)
    query_gradient_rows = grad_q.reshape(blocks, BLOCK_TOKENS, heads_q, head_width)
    pad_spec_low = ((0, 2), (0, 0), (0, 0), (0, 0))
    pad_spec_mid = ((1, 1), (0, 0), (0, 0), (0, 0))
    pad_spec_high = ((2, 0), (0, 0), (0, 0), (0, 0))
    window_sum = (
        jnp.pad(tile_grads[:, 0], pad_spec_low)
        + jnp.pad(tile_grads[:, 1], pad_spec_mid)
        + jnp.pad(tile_grads[:, 2], pad_spec_high)
    )
    rims = jnp.concatenate([window_sum[0], window_sum[blocks + 1]], axis=1)
    returned_rims = padded(rims.astype(jnp.bfloat16), (("seq", 1),), BLOCK_TOKENS).astype(
        rims.dtype
    )
    interior = window_sum[1 : blocks + 1]
    interior = (
        interior.at[0]
        .add(returned_rims[:, :BLOCK_TOKENS])
        .at[blocks - 1]
        .add(returned_rims[:, 3 * BLOCK_TOKENS :])
    )
    global_terms = jnp.sum(tile_grads[:, 3:5], axis=0)
    global_total = tree_sum(global_terms, "seq")
    own_weight = own_global.astype(jnp.float32)[:, :, None, None, None]
    interior = interior + jnp.sum(own_weight * global_total[:, None], axis=0)
    random_terms = (
        tile_grads[:, 5:8]
        .transpose(1, 0, 2, 3, 4)
        .reshape(entry_count, 2, BLOCK_TOKENS, kv_width)
        .astype(jnp.bfloat16)
    )
    slot_onehot = (my_slot[:, None] == jnp.arange(seq_count * capacity)[None, :]).astype(
        jnp.bfloat16
    )
    back_buffer = jnp.einsum(
        "es,exbw->sxbw", slot_onehot, random_terms, preferred_element_type=jnp.float32
    ).astype(jnp.bfloat16)
    returned_terms = exchange(back_buffer, "seq", 0, 0)
    interior = interior + jnp.einsum(
        "tco,tcxbw->oxbw",
        selector,
        returned_terms.reshape(seq_count, capacity, 2, BLOCK_TOKENS, kv_width),
        preferred_element_type=jnp.float32,
    )
    kv_grad = interior.transpose(1, 0, 2, 3).reshape(2, shard_len, kv_width).astype(jnp.bfloat16)
    out_all = output_block_rows.reshape(shard_len, heads_q, head_width)
    query_grad_all = query_gradient_rows.reshape(shard_len, heads_q, head_width)
    key_grad_all = kv_grad[0].reshape(shard_len, heads_kv, head_width)
    value_grad_all = kv_grad[1].reshape(shard_len, heads_kv, head_width)
    out_back = lax.all_to_all(out_all, "head", split_axis=0, concat_axis=1, tiled=True)
    query_back = lax.all_to_all(query_grad_all, "head", split_axis=0, concat_axis=1, tiled=True)
    kv_grad = kv_grad.reshape(2, shard_len, heads_kv, head_width)
    kv_back = exchange(kv_grad, "head", 1, 2)
    return (out_back, query_back, kv_back[0], kv_back[1])


def solution(mesh):
    placed = (
        P(("seq", "head"), None, None),
        P(("seq", "head"), None, None),
        P(("seq", "head"), None, None),
        P(("seq", "head"), None, None),
        P(),
        P(),
    )
    return jax.shard_map(
        per_device,
        mesh=mesh,
        in_specs=placed,
        out_specs=(
            P(("seq", "head"), None, None),
            P(("seq", "head"), None, None),
            P(("seq", "head"), None, None),
            P(("seq", "head"), None, None),
        ),
        check_vma=False,
    )
```

```python
import functools
import math

import jax
import jax.numpy as jnp
from jax import lax
from jax.experimental import pallas as pl
from jax.sharding import PartitionSpec as P

BLOCK_TOKENS = 128


def rows_of(ref, group, width):
    return jnp.concatenate([ref[:, g * width:(g + 1) * width] for g in range(group)], axis=0)


def store_rows(ref, value, group, width):
    tokens = ref.shape[0]
    for g in range(group):
        ref[:, g * width:(g + 1) * width] = value[g * tokens:(g + 1) * tokens, :]


def softmax_rows(q, k, bias, scale):
    rows_by_cols = (((1,), (1,)), ((), ()))
    s = lax.dot_general(q, k, rows_by_cols, preferred_element_type=jnp.float32) * scale
    s = s + bias
    e = jnp.exp(s - jnp.max(s, axis=1, keepdims=True))
    return e / jnp.sum(e, axis=1, keepdims=True)


def forward_kernel(q_ref, k_ref, v_ref, bias_ref, out_ref, *, scale):
    group = q_ref.shape[1] // q_ref.shape[0]
    width = k_ref.shape[-1]
    q = rows_of(q_ref, group, width)
    k = k_ref[...].reshape(-1, width)
    v = v_ref[...].reshape(-1, width)
    p_low = softmax_rows(q, k, bias_ref[...], scale).astype(jnp.bfloat16)
    o_low = jnp.dot(p_low, v, preferred_element_type=jnp.float32).astype(jnp.bfloat16)
    store_rows(out_ref, o_low, group, width)


def backward_kernel(q_ref, k_ref, v_ref, do_ref, o_ref, bias_ref, dq_ref, grad_ref, *, scale):
    group = q_ref.shape[1] // q_ref.shape[0]
    width = k_ref.shape[-1]
    q = rows_of(q_ref, group, width)
    do = rows_of(do_ref, group, width)
    o_low = rows_of(o_ref, group, width)
    k = k_ref[...].reshape(-1, width)
    v = v_ref[...].reshape(-1, width)
    rows_by_cols = (((1,), (1,)), ((), ()))
    over_rows = (((0,), (0,)), ((), ()))
    p = softmax_rows(q, k, bias_ref[...], scale)
    p_low = p.astype(jnp.bfloat16)
    delta = jnp.sum(do.astype(jnp.float32) * o_low.astype(jnp.float32), axis=1, keepdims=True)
    dp = lax.dot_general(do, v, rows_by_cols, preferred_element_type=jnp.float32)
    ds_low = (p * (dp - delta)).astype(jnp.bfloat16)
    dq = jnp.dot(ds_low, k, preferred_element_type=jnp.float32) * scale
    store_rows(dq_ref, dq.astype(jnp.bfloat16), group, width)
    dk = lax.dot_general(ds_low, q, over_rows, preferred_element_type=jnp.float32) * scale
    dv = lax.dot_general(p_low, do, over_rows, preferred_element_type=jnp.float32)
    grad_ref[:, 0] = dk.reshape(grad_ref.shape[0], -1, width)
    grad_ref[:, 1] = dv.reshape(grad_ref.shape[0], -1, width)


def attention_call(q, tiles, do, bias, heads_kv, scale):
    blocks, tokens, q_width = q.shape
    tile_count, head_width = tiles.shape[1], tiles.shape[-1] // heads_kv
    rows_width = q_width // heads_kv
    q_spec = pl.BlockSpec((None, tokens, rows_width), lambda j, h: (j, 0, h))
    k_spec = pl.BlockSpec((None, tile_count, None, tokens, head_width), lambda j, h: (j, 0, 0, 0, h))
    v_spec = pl.BlockSpec((None, tile_count, None, tokens, head_width), lambda j, h: (j, 0, 1, 0, h))
    b_spec = pl.BlockSpec((None, 1, bias.shape[-1]), lambda j, h: (j, 0, 0))
    g_spec = pl.BlockSpec((None, tile_count, 2, tokens, head_width), lambda j, h: (j, 0, 0, 0, h))
    steps = blocks * heads_kv
    rows = tokens * (rows_width // head_width)
    keys_n = tile_count * tokens
    matmul = 2 * rows * keys_n * head_width * steps
    moved = 2 * (3 * q.size + 2 * tiles.size) + 4 * tiles.size
    out = pl.pallas_call(
        functools.partial(forward_kernel, scale=scale),
        cost_estimate=pl.CostEstimate(
            flops=2 * matmul, transcendentals=rows * keys_n * steps, bytes_accessed=moved
        ),
        grid=(blocks, heads_kv),
        in_specs=[q_spec, k_spec, v_spec, b_spec],
        out_specs=q_spec,
        out_shape=jax.ShapeDtypeStruct(q.shape, jnp.bfloat16),
    )(q, tiles, tiles, bias)
    out, do = lax.optimization_barrier((out, do))
    grad_q, grads = pl.pallas_call(
        functools.partial(backward_kernel, scale=scale),
        cost_estimate=pl.CostEstimate(
            flops=5 * matmul, transcendentals=rows * keys_n * steps, bytes_accessed=moved
        ),
        grid=(blocks, heads_kv),
        in_specs=[q_spec, k_spec, v_spec, q_spec, q_spec, b_spec],
        out_specs=[q_spec, g_spec],
        out_shape=[
            jax.ShapeDtypeStruct(q.shape, jnp.bfloat16),
            jax.ShapeDtypeStruct(tiles.shape, jnp.float32),
        ],
    )(q, tiles, tiles, do, out, bias)
    return out, grad_q, grads


def exchange(array, axis, split_axis, concat_axis):
    count = lax.axis_size(axis)
    own = lax.axis_index(axis)
    piece = array.shape[split_axis] // count
    received = []
    for shift in range(count):
        target = (own + shift) % count
        part = lax.dynamic_slice_in_dim(array, target * piece, piece, split_axis)
        if shift:
            pairs = [(i, (i + shift) % count) for i in range(count)]
            part = lax.ppermute(part, axis, pairs)
        received.append(part)
    order = (own - jnp.arange(count)) % count
    stacked = jnp.take(jnp.stack(received), order, axis=0)
    stacked = jnp.moveaxis(stacked, 0, concat_axis)
    shape = list(array.shape)
    shape[split_axis] = piece
    shape[concat_axis] *= count
    return stacked.reshape(shape)


def padded(shard, sides, width):
    for axis, dim in sides:
        count, length = (lax.axis_size(axis), shard.shape[dim])
        up = [(i, (i + 1) % count) for i in range(count - 1)]
        down = [(j, i) for i, j in up]
        last = lax.slice_in_dim(shard, length - width, length, axis=dim)
        leading = lax.slice_in_dim(shard, 0, width, axis=dim)
        before = lax.ppermute(last, axis, up)
        after = lax.ppermute(leading, axis, down)
        shard = jnp.concatenate([before, shard, after], axis=dim)
    return shard


def from_root(block, axis, owner):
    block = jnp.where(lax.axis_index(axis) == owner, block, jnp.zeros_like(block))
    return lax.psum(block, axis)


def tree_sum(part, axis):
    count = lax.axis_size(axis)
    if count & (count - 1):
        return lax.psum(part.astype(jnp.bfloat16), axis).astype(jnp.float32)
    stride = 1
    while stride < count:
        pairs = [(i, i ^ stride) for i in range(count)]
        other = lax.ppermute(part.astype(jnp.bfloat16), axis, pairs)
        part = part + other.astype(jnp.float32)
        stride *= 2
    return part


def per_device(queries, keys, values, output_gradient, global_blocks, random_blocks):
    query_loc, key_loc, value_loc, grad_loc = (
        lax.all_to_all(queries, "head", split_axis=1, concat_axis=0, tiled=True),
        lax.all_to_all(keys, "head", split_axis=1, concat_axis=0, tiled=True),
        lax.all_to_all(values, "head", split_axis=1, concat_axis=0, tiled=True),
        output_gradient,
    )
    shard_len, heads_q, head_width = query_loc.shape
    heads_kv = key_loc.shape[1]
    heads_per_group = heads_q // heads_kv
    kv_width = heads_kv * head_width
    blocks = shard_len // BLOCK_TOKENS
    seq_count = lax.axis_size("seq")
    own_index = lax.axis_index("seq")
    block_total_count = seq_count * blocks
    capacity = (3 * blocks + seq_count - 2) // (seq_count - 1)
    entry_count = 3 * blocks
    score_scale = 1.0 / math.sqrt(head_width)
    kv_pair = jnp.stack(
        [key_loc.reshape(shard_len, kv_width), value_loc.reshape(shard_len, kv_width)]
    )
    extended = padded(kv_pair, (("seq", 1),), BLOCK_TOKENS)
    kv_tiles = kv_pair.reshape(2, blocks, BLOCK_TOKENS, kv_width).transpose(1, 0, 2, 3)
    global_owner = global_blocks // blocks
    global_offset = global_blocks % blocks
    own_global = (jnp.arange(blocks)[None, :] == global_offset[:, None]) & (
        global_owner == own_index
    )[:, None]
    all_entries = (
        random_blocks.reshape(seq_count, blocks, 3)
        .transpose(0, 2, 1)
        .reshape(seq_count, entry_count)
    )
    all_owner = all_entries // blocks
    entry_ids = jnp.arange(entry_count)
    entry_earlier = entry_ids[None, :] < entry_ids[:, None]
    all_rank = jnp.sum(
        (all_owner[:, :, None] == all_owner[:, None, :]) & entry_earlier[None], axis=2
    )
    my_entries = lax.dynamic_index_in_dim(all_entries, own_index, 0, keepdims=False)
    my_owner = lax.dynamic_index_in_dim(all_owner, own_index, 0, keepdims=False)
    my_rank = lax.dynamic_index_in_dim(all_rank, own_index, 0, keepdims=False)
    my_slot = my_owner * capacity + my_rank
    owned_here = (all_owner == own_index)[:, :, None] & (
        all_rank[:, :, None] == jnp.arange(capacity)[None, None, :]
    )
    offset_match = (all_entries % blocks)[:, :, None] == jnp.arange(blocks)[None, None, :]
    selector = jnp.einsum(
        "tec,teo->tco",
        owned_here.astype(jnp.bfloat16),
        offset_match.astype(jnp.bfloat16),
        preferred_element_type=jnp.float32,
    ).astype(jnp.bfloat16)
    everything = lax.all_gather(kv_pair, "seq", axis=1, tiled=True)
    query_loc, everything, grad_loc = lax.optimization_barrier((query_loc, everything, grad_loc))
    grad_loc = lax.all_to_all(grad_loc, "head", split_axis=1, concat_axis=0, tiled=True)
    tiled_all = everything.reshape(2, block_total_count, BLOCK_TOKENS, kv_width)
    random_tiles = jnp.take(tiled_all, my_entries, axis=1).transpose(1, 0, 2, 3)
    global_tiles = jnp.take(tiled_all, global_blocks, axis=1).transpose(1, 0, 2, 3)
    random_by_block = random_tiles.reshape(3, blocks, 2, BLOCK_TOKENS, kv_width).transpose(
        1, 0, 2, 3, 4
    )
    block_ids = own_index * blocks + jnp.arange(blocks)
    listed = jnp.concatenate(
        [
            jnp.stack([block_ids - 1, block_ids, block_ids + 1], axis=1),
            jnp.broadcast_to(global_blocks[None, :], (blocks, 2)),
            my_entries.reshape(3, blocks).T,
        ],
        axis=1,
    )
    inside = (listed >= 0) & (listed < block_total_count)
    tile_ids = jnp.arange(8)
    tile_earlier = tile_ids[None, :] < tile_ids[:, None]
    repeat = jnp.any((listed[:, :, None] == listed[:, None, :]) & tile_earlier[None], axis=2)
    live = inside & jnp.logical_not(repeat)

    tiles_per_block = []
    for position in range(blocks):
        near_tiles = lax.slice_in_dim(
            extended, position * BLOCK_TOKENS, (position + 3) * BLOCK_TOKENS, axis=1
        )
        near_tiles = near_tiles.reshape(2, 3, BLOCK_TOKENS, kv_width).transpose(1, 0, 2, 3)
        tiles_per_block.append(
            jnp.concatenate([near_tiles, global_tiles, random_by_block[position]], axis=0)
        )
    all_tiles = jnp.stack(tiles_per_block)
    tile_count = all_tiles.shape[1]
    bias = jnp.where(live, 0.0, -jnp.inf).astype(jnp.float32)
    bias = jnp.repeat(bias, BLOCK_TOKENS, axis=1).reshape(blocks, 1, tile_count * BLOCK_TOKENS)
    out_q, grad_q, tile_grads = attention_call(
        query_loc.reshape(blocks, BLOCK_TOKENS, heads_q * head_width),
        all_tiles,
        grad_loc.reshape(blocks, BLOCK_TOKENS, heads_q * head_width),
        bias,
        heads_kv,
        score_scale,
    )
    output_block_rows = out_q.reshape(blocks, BLOCK_TOKENS, heads_q, head_width)
    query_gradient_rows = grad_q.reshape(blocks, BLOCK_TOKENS, heads_q, head_width)
    pad_spec_low = ((0, 2), (0, 0), (0, 0), (0, 0))
    pad_spec_mid = ((1, 1), (0, 0), (0, 0), (0, 0))
    pad_spec_high = ((2, 0), (0, 0), (0, 0), (0, 0))
    window_sum = (
        jnp.pad(tile_grads[:, 0], pad_spec_low)
        + jnp.pad(tile_grads[:, 1], pad_spec_mid)
        + jnp.pad(tile_grads[:, 2], pad_spec_high)
    )
    rims = jnp.concatenate([window_sum[0], window_sum[blocks + 1]], axis=1)
    returned_rims = padded(rims.astype(jnp.bfloat16), (("seq", 1),), BLOCK_TOKENS).astype(
        rims.dtype
    )
    interior = window_sum[1 : blocks + 1]
    interior = (
        interior.at[0]
        .add(returned_rims[:, :BLOCK_TOKENS])
        .at[blocks - 1]
        .add(returned_rims[:, 3 * BLOCK_TOKENS :])
    )
    global_terms = jnp.sum(tile_grads[:, 3:5], axis=0)
    global_total = tree_sum(global_terms, "seq")
    own_weight = own_global.astype(jnp.float32)[:, :, None, None, None]
    interior = interior + jnp.sum(own_weight * global_total[:, None], axis=0)
    random_terms = (
        tile_grads[:, 5:8]
        .transpose(1, 0, 2, 3, 4)
        .reshape(entry_count, 2, BLOCK_TOKENS, kv_width)
        .astype(jnp.bfloat16)
    )
    slot_onehot = (my_slot[:, None] == jnp.arange(seq_count * capacity)[None, :]).astype(
        jnp.bfloat16
    )
    back_buffer = jnp.einsum(
        "es,exbw->sxbw", slot_onehot, random_terms, preferred_element_type=jnp.float32
    ).astype(jnp.bfloat16)
    returned_terms = exchange(back_buffer, "seq", 0, 0)
    interior = interior + jnp.einsum(
        "tco,tcxbw->oxbw",
        selector,
        returned_terms.reshape(seq_count, capacity, 2, BLOCK_TOKENS, kv_width),
        preferred_element_type=jnp.float32,
    )
    kv_grad = interior.transpose(1, 0, 2, 3).reshape(2, shard_len, kv_width).astype(jnp.bfloat16)
    out_all = output_block_rows.reshape(shard_len, heads_q, head_width)
    query_grad_all = query_gradient_rows.reshape(shard_len, heads_q, head_width)
    key_grad_all = kv_grad[0].reshape(shard_len, heads_kv, head_width)
    value_grad_all = kv_grad[1].reshape(shard_len, heads_kv, head_width)
    out_back = lax.all_to_all(out_all, "head", split_axis=0, concat_axis=1, tiled=True)
    query_back = exchange(query_grad_all, "head", 0, 1)
    out_back, kv_grad = lax.optimization_barrier((out_back, kv_grad))
    kv_grad = kv_grad.reshape(2, shard_len, heads_kv, head_width)
    kv_back = lax.all_to_all(kv_grad, "head", split_axis=1, concat_axis=2, tiled=True)
    return (out_back, query_back, kv_back[0], kv_back[1])


def solution(mesh):
    placed = (
        P(("seq", "head"), None, None),
        P(("seq", "head"), None, None),
        P(("seq", "head"), None, None),
        P(("seq", "head"), None, None),
        P(),
        P(),
    )
    return jax.shard_map(
        per_device,
        mesh=mesh,
        in_specs=placed,
        out_specs=(
            P(("seq", "head"), None, None),
            P(("seq", "head"), None, None),
            P(("seq", "head"), None, None),
            P(("seq", "head"), None, None),
        ),
        check_vma=False,
    )
```

```python
import functools
import math

import jax
import jax.numpy as jnp
from jax import lax
from jax.experimental import pallas as pl
from jax.sharding import PartitionSpec as P

BLOCK_TOKENS = 128


def rows_of(ref, group, width):
    return jnp.concatenate([ref[:, g * width:(g + 1) * width] for g in range(group)], axis=0)


def store_rows(ref, value, group, width):
    tokens = ref.shape[0]
    for g in range(group):
        ref[:, g * width:(g + 1) * width] = value[g * tokens:(g + 1) * tokens, :]


def softmax_rows(q, k, bias, scale):
    rows_by_cols = (((1,), (1,)), ((), ()))
    s = lax.dot_general(q, k, rows_by_cols, preferred_element_type=jnp.float32) * scale
    s = s + bias
    e = jnp.exp(s - jnp.max(s, axis=1, keepdims=True))
    return e / jnp.sum(e, axis=1, keepdims=True)


def forward_kernel(q_ref, k_ref, v_ref, bias_ref, out_ref, *, scale):
    group = q_ref.shape[1] // q_ref.shape[0]
    width = k_ref.shape[-1]
    q = rows_of(q_ref, group, width)
    k = k_ref[...].reshape(-1, width)
    v = v_ref[...].reshape(-1, width)
    p_low = softmax_rows(q, k, bias_ref[...], scale).astype(jnp.bfloat16)
    o_low = jnp.dot(p_low, v, preferred_element_type=jnp.float32).astype(jnp.bfloat16)
    store_rows(out_ref, o_low, group, width)


def backward_kernel(q_ref, k_ref, v_ref, do_ref, o_ref, bias_ref, dq_ref, grad_ref, *, scale):
    group = q_ref.shape[1] // q_ref.shape[0]
    width = k_ref.shape[-1]
    q = rows_of(q_ref, group, width)
    do = rows_of(do_ref, group, width)
    o_low = rows_of(o_ref, group, width)
    k = k_ref[...].reshape(-1, width)
    v = v_ref[...].reshape(-1, width)
    rows_by_cols = (((1,), (1,)), ((), ()))
    over_rows = (((0,), (0,)), ((), ()))
    p = softmax_rows(q, k, bias_ref[...], scale)
    p_low = p.astype(jnp.bfloat16)
    delta = jnp.sum(do.astype(jnp.float32) * o_low.astype(jnp.float32), axis=1, keepdims=True)
    dp = lax.dot_general(do, v, rows_by_cols, preferred_element_type=jnp.float32)
    ds_low = (p * (dp - delta)).astype(jnp.bfloat16)
    dq = jnp.dot(ds_low, k, preferred_element_type=jnp.float32) * scale
    store_rows(dq_ref, dq.astype(jnp.bfloat16), group, width)
    dk = lax.dot_general(ds_low, q, over_rows, preferred_element_type=jnp.float32) * scale
    dv = lax.dot_general(p_low, do, over_rows, preferred_element_type=jnp.float32)
    grad_ref[:, 0] = dk.reshape(grad_ref.shape[0], -1, width)
    grad_ref[:, 1] = dv.reshape(grad_ref.shape[0], -1, width)


def attention_call(q, tiles, do, bias, heads_kv, scale):
    blocks, tokens, q_width = q.shape
    tile_count, head_width = tiles.shape[1], tiles.shape[-1] // heads_kv
    rows_width = q_width // heads_kv
    q_spec = pl.BlockSpec((None, tokens, rows_width), lambda j, h: (j, 0, h))
    k_spec = pl.BlockSpec((None, tile_count, None, tokens, head_width), lambda j, h: (j, 0, 0, 0, h))
    v_spec = pl.BlockSpec((None, tile_count, None, tokens, head_width), lambda j, h: (j, 0, 1, 0, h))
    b_spec = pl.BlockSpec((None, 1, bias.shape[-1]), lambda j, h: (j, 0, 0))
    g_spec = pl.BlockSpec((None, tile_count, 2, tokens, head_width), lambda j, h: (j, 0, 0, 0, h))
    steps = blocks * heads_kv
    rows = tokens * (rows_width // head_width)
    keys_n = tile_count * tokens
    matmul = 2 * rows * keys_n * head_width * steps
    moved = 2 * (3 * q.size + 2 * tiles.size) + 4 * tiles.size
    out = pl.pallas_call(
        functools.partial(forward_kernel, scale=scale),
        cost_estimate=pl.CostEstimate(
            flops=2 * matmul, transcendentals=rows * keys_n * steps, bytes_accessed=moved
        ),
        grid=(blocks, heads_kv),
        in_specs=[q_spec, k_spec, v_spec, b_spec],
        out_specs=q_spec,
        out_shape=jax.ShapeDtypeStruct(q.shape, jnp.bfloat16),
    )(q, tiles, tiles, bias)
    out, do = lax.optimization_barrier((out, do))
    grad_q, grads = pl.pallas_call(
        functools.partial(backward_kernel, scale=scale),
        cost_estimate=pl.CostEstimate(
            flops=5 * matmul, transcendentals=rows * keys_n * steps, bytes_accessed=moved
        ),
        grid=(blocks, heads_kv),
        in_specs=[q_spec, k_spec, v_spec, q_spec, q_spec, b_spec],
        out_specs=[q_spec, g_spec],
        out_shape=[
            jax.ShapeDtypeStruct(q.shape, jnp.bfloat16),
            jax.ShapeDtypeStruct(tiles.shape, jnp.float32),
        ],
    )(q, tiles, tiles, do, out, bias)
    return out, grad_q, grads


def exchange(array, axis, split_axis, concat_axis):
    count = lax.axis_size(axis)
    own = lax.axis_index(axis)
    piece = array.shape[split_axis] // count
    received = []
    for shift in range(count):
        target = (own + shift) % count
        part = lax.dynamic_slice_in_dim(array, target * piece, piece, split_axis)
        if shift:
            pairs = [(i, (i + shift) % count) for i in range(count)]
            part = lax.ppermute(part, axis, pairs)
        received.append(part)
    order = (own - jnp.arange(count)) % count
    stacked = jnp.take(jnp.stack(received), order, axis=0)
    stacked = jnp.moveaxis(stacked, 0, concat_axis)
    shape = list(array.shape)
    shape[split_axis] = piece
    shape[concat_axis] *= count
    return stacked.reshape(shape)


def padded(shard, sides, width):
    for axis, dim in sides:
        count, length = (lax.axis_size(axis), shard.shape[dim])
        up = [(i, (i + 1) % count) for i in range(count - 1)]
        down = [(j, i) for i, j in up]
        last = lax.slice_in_dim(shard, length - width, length, axis=dim)
        leading = lax.slice_in_dim(shard, 0, width, axis=dim)
        before = lax.ppermute(last, axis, up)
        after = lax.ppermute(leading, axis, down)
        shard = jnp.concatenate([before, shard, after], axis=dim)
    return shard


def from_root(block, axis, owner):
    block = jnp.where(lax.axis_index(axis) == owner, block, jnp.zeros_like(block))
    return lax.psum(block, axis)


def tree_sum(part, axis):
    count = lax.axis_size(axis)
    if count & (count - 1):
        return lax.psum(part.astype(jnp.bfloat16), axis).astype(jnp.float32)
    stride = 1
    while stride < count:
        pairs = [(i, i ^ stride) for i in range(count)]
        other = lax.ppermute(part.astype(jnp.bfloat16), axis, pairs)
        part = part + other.astype(jnp.float32)
        stride *= 2
    return part


def per_device(queries, keys, values, output_gradient, global_blocks, random_blocks):
    kv_loc = lax.all_to_all(
        jnp.stack([keys, values], axis=2), "head", split_axis=1, concat_axis=0, tiled=True
    )
    key_loc, value_loc = kv_loc[:, :, 0], kv_loc[:, :, 1]
    query_loc = lax.all_to_all(queries, "head", split_axis=1, concat_axis=0, tiled=True)
    grad_loc = output_gradient
    shard_len, heads_q, head_width = query_loc.shape
    heads_kv = key_loc.shape[1]
    heads_per_group = heads_q // heads_kv
    kv_width = heads_kv * head_width
    blocks = shard_len // BLOCK_TOKENS
    seq_count = lax.axis_size("seq")
    own_index = lax.axis_index("seq")
    block_total_count = seq_count * blocks
    capacity = (3 * blocks + seq_count - 2) // (seq_count - 1)
    entry_count = 3 * blocks
    score_scale = 1.0 / math.sqrt(head_width)
    kv_pair = jnp.stack(
        [key_loc.reshape(shard_len, kv_width), value_loc.reshape(shard_len, kv_width)]
    )
    extended = padded(kv_pair, (("seq", 1),), BLOCK_TOKENS)
    kv_tiles = kv_pair.reshape(2, blocks, BLOCK_TOKENS, kv_width).transpose(1, 0, 2, 3)
    global_owner = global_blocks // blocks
    global_offset = global_blocks % blocks
    own_global = (jnp.arange(blocks)[None, :] == global_offset[:, None]) & (
        global_owner == own_index
    )[:, None]
    all_entries = (
        random_blocks.reshape(seq_count, blocks, 3)
        .transpose(0, 2, 1)
        .reshape(seq_count, entry_count)
    )
    all_owner = all_entries // blocks
    entry_ids = jnp.arange(entry_count)
    entry_earlier = entry_ids[None, :] < entry_ids[:, None]
    all_rank = jnp.sum(
        (all_owner[:, :, None] == all_owner[:, None, :]) & entry_earlier[None], axis=2
    )
    my_entries = lax.dynamic_index_in_dim(all_entries, own_index, 0, keepdims=False)
    my_owner = lax.dynamic_index_in_dim(all_owner, own_index, 0, keepdims=False)
    my_rank = lax.dynamic_index_in_dim(all_rank, own_index, 0, keepdims=False)
    my_slot = my_owner * capacity + my_rank
    owned_here = (all_owner == own_index)[:, :, None] & (
        all_rank[:, :, None] == jnp.arange(capacity)[None, None, :]
    )
    offset_match = (all_entries % blocks)[:, :, None] == jnp.arange(blocks)[None, None, :]
    selector = jnp.einsum(
        "tec,teo->tco",
        owned_here.astype(jnp.bfloat16),
        offset_match.astype(jnp.bfloat16),
        preferred_element_type=jnp.float32,
    ).astype(jnp.bfloat16)
    everything = lax.all_gather(kv_pair, "seq", axis=1, tiled=True)
    query_loc, everything, grad_loc = lax.optimization_barrier((query_loc, everything, grad_loc))
    grad_loc = lax.all_to_all(grad_loc, "head", split_axis=1, concat_axis=0, tiled=True)
    tiled_all = everything.reshape(2, block_total_count, BLOCK_TOKENS, kv_width)
    random_tiles = jnp.take(tiled_all, my_entries, axis=1).transpose(1, 0, 2, 3)
    global_tiles = jnp.take(tiled_all, global_blocks, axis=1).transpose(1, 0, 2, 3)
    random_by_block = random_tiles.reshape(3, blocks, 2, BLOCK_TOKENS, kv_width).transpose(
        1, 0, 2, 3, 4
    )
    block_ids = own_index * blocks + jnp.arange(blocks)
    listed = jnp.concatenate(
        [
            jnp.stack([block_ids - 1, block_ids, block_ids + 1], axis=1),
            jnp.broadcast_to(global_blocks[None, :], (blocks, 2)),
            my_entries.reshape(3, blocks).T,
        ],
        axis=1,
    )
    inside = (listed >= 0) & (listed < block_total_count)
    tile_ids = jnp.arange(8)
    tile_earlier = tile_ids[None, :] < tile_ids[:, None]
    repeat = jnp.any((listed[:, :, None] == listed[:, None, :]) & tile_earlier[None], axis=2)
    live = inside & jnp.logical_not(repeat)

    tiles_per_block = []
    for position in range(blocks):
        near_tiles = lax.slice_in_dim(
            extended, position * BLOCK_TOKENS, (position + 3) * BLOCK_TOKENS, axis=1
        )
        near_tiles = near_tiles.reshape(2, 3, BLOCK_TOKENS, kv_width).transpose(1, 0, 2, 3)
        tiles_per_block.append(
            jnp.concatenate([near_tiles, global_tiles, random_by_block[position]], axis=0)
        )
    all_tiles = jnp.stack(tiles_per_block)
    tile_count = all_tiles.shape[1]
    bias = jnp.where(live, 0.0, -jnp.inf).astype(jnp.float32)
    bias = jnp.repeat(bias, BLOCK_TOKENS, axis=1).reshape(blocks, 1, tile_count * BLOCK_TOKENS)
    out_q, grad_q, tile_grads = attention_call(
        query_loc.reshape(blocks, BLOCK_TOKENS, heads_q * head_width),
        all_tiles,
        grad_loc.reshape(blocks, BLOCK_TOKENS, heads_q * head_width),
        bias,
        heads_kv,
        score_scale,
    )
    output_block_rows = out_q.reshape(blocks, BLOCK_TOKENS, heads_q, head_width)
    query_gradient_rows = grad_q.reshape(blocks, BLOCK_TOKENS, heads_q, head_width)
    pad_spec_low = ((0, 2), (0, 0), (0, 0), (0, 0))
    pad_spec_mid = ((1, 1), (0, 0), (0, 0), (0, 0))
    pad_spec_high = ((2, 0), (0, 0), (0, 0), (0, 0))
    window_sum = (
        jnp.pad(tile_grads[:, 0], pad_spec_low)
        + jnp.pad(tile_grads[:, 1], pad_spec_mid)
        + jnp.pad(tile_grads[:, 2], pad_spec_high)
    )
    rims = jnp.concatenate([window_sum[0], window_sum[blocks + 1]], axis=1)
    returned_rims = padded(rims.astype(jnp.bfloat16), (("seq", 1),), BLOCK_TOKENS).astype(
        rims.dtype
    )
    interior = window_sum[1 : blocks + 1]
    interior = (
        interior.at[0]
        .add(returned_rims[:, :BLOCK_TOKENS])
        .at[blocks - 1]
        .add(returned_rims[:, 3 * BLOCK_TOKENS :])
    )
    global_terms = jnp.sum(tile_grads[:, 3:5], axis=0)
    global_total = tree_sum(global_terms, "seq")
    own_weight = own_global.astype(jnp.float32)[:, :, None, None, None]
    interior = interior + jnp.sum(own_weight * global_total[:, None], axis=0)
    random_terms = (
        tile_grads[:, 5:8]
        .transpose(1, 0, 2, 3, 4)
        .reshape(entry_count, 2, BLOCK_TOKENS, kv_width)
        .astype(jnp.bfloat16)
    )
    slot_onehot = (my_slot[:, None] == jnp.arange(seq_count * capacity)[None, :]).astype(
        jnp.bfloat16
    )
    back_buffer = jnp.einsum(
        "es,exbw->sxbw", slot_onehot, random_terms, preferred_element_type=jnp.float32
    ).astype(jnp.bfloat16)
    returned_terms = exchange(back_buffer, "seq", 0, 0)
    interior = interior + jnp.einsum(
        "tco,tcxbw->oxbw",
        selector,
        returned_terms.reshape(seq_count, capacity, 2, BLOCK_TOKENS, kv_width),
        preferred_element_type=jnp.float32,
    )
    kv_grad = interior.transpose(1, 0, 2, 3).reshape(2, shard_len, kv_width).astype(jnp.bfloat16)
    out_all = output_block_rows.reshape(shard_len, heads_q, head_width)
    query_grad_all = query_gradient_rows.reshape(shard_len, heads_q, head_width)
    key_grad_all = kv_grad[0].reshape(shard_len, heads_kv, head_width)
    value_grad_all = kv_grad[1].reshape(shard_len, heads_kv, head_width)
    out_back = lax.all_to_all(out_all, "head", split_axis=0, concat_axis=1, tiled=True)
    query_back = lax.all_to_all(query_grad_all, "head", split_axis=0, concat_axis=1, tiled=True)
    (out_back, query_back), kv_grad = lax.optimization_barrier(((out_back, query_back), kv_grad))
    kv_grad = kv_grad.reshape(2, shard_len, heads_kv, head_width)
    kv_back = lax.all_to_all(kv_grad, "head", split_axis=1, concat_axis=2, tiled=True)
    return (out_back, query_back, kv_back[0], kv_back[1])


def solution(mesh):
    placed = (
        P(("seq", "head"), None, None),
        P(("seq", "head"), None, None),
        P(("seq", "head"), None, None),
        P(("seq", "head"), None, None),
        P(),
        P(),
    )
    return jax.shard_map(
        per_device,
        mesh=mesh,
        in_specs=placed,
        out_specs=(
            P(("seq", "head"), None, None),
            P(("seq", "head"), None, None),
            P(("seq", "head"), None, None),
            P(("seq", "head"), None, None),
        ),
        check_vma=False,
    )
```

```python
import functools
import math

import jax
import jax.numpy as jnp
from jax import lax
from jax.experimental import pallas as pl
from jax.sharding import PartitionSpec as P

BLOCK_TOKENS = 128


def rows_of(ref, group, width):
    return jnp.concatenate([ref[:, g * width:(g + 1) * width] for g in range(group)], axis=0)


def store_rows(ref, value, group, width):
    tokens = ref.shape[0]
    for g in range(group):
        ref[:, g * width:(g + 1) * width] = value[g * tokens:(g + 1) * tokens, :]


def softmax_rows(q, k, bias, scale):
    rows_by_cols = (((1,), (1,)), ((), ()))
    s = lax.dot_general(q, k, rows_by_cols, preferred_element_type=jnp.float32) * scale
    s = s + bias
    e = jnp.exp(s - jnp.max(s, axis=1, keepdims=True))
    return e / jnp.sum(e, axis=1, keepdims=True)


def forward_kernel(q_ref, k_ref, v_ref, bias_ref, out_ref, *, scale):
    width = k_ref.shape[-1]
    q = q_ref[...].reshape(-1, width)
    k = k_ref[...].reshape(-1, width)
    v = v_ref[...].reshape(-1, width)
    p_low = softmax_rows(q, k, bias_ref[...], scale).astype(jnp.bfloat16)
    o_low = jnp.dot(p_low, v, preferred_element_type=jnp.float32).astype(jnp.bfloat16)
    out_ref[...] = o_low.reshape(out_ref.shape)


def backward_kernel(q_ref, k_ref, v_ref, do_ref, o_ref, bias_ref, dq_ref, grad_ref, *, scale):
    width = k_ref.shape[-1]
    q = q_ref[...].reshape(-1, width)
    do = do_ref[...].reshape(-1, width)
    o_low = o_ref[...].reshape(-1, width)
    k = k_ref[...].reshape(-1, width)
    v = v_ref[...].reshape(-1, width)
    rows_by_cols = (((1,), (1,)), ((), ()))
    over_rows = (((0,), (0,)), ((), ()))
    p = softmax_rows(q, k, bias_ref[...], scale)
    p_low = p.astype(jnp.bfloat16)
    delta = jnp.sum(do.astype(jnp.float32) * o_low.astype(jnp.float32), axis=1, keepdims=True)
    dp = lax.dot_general(do, v, rows_by_cols, preferred_element_type=jnp.float32)
    ds_low = (p * (dp - delta)).astype(jnp.bfloat16)
    dq = jnp.dot(ds_low, k, preferred_element_type=jnp.float32) * scale
    dq_ref[...] = dq.astype(jnp.bfloat16).reshape(dq_ref.shape)
    dk = lax.dot_general(ds_low, q, over_rows, preferred_element_type=jnp.float32) * scale
    dv = lax.dot_general(p_low, do, over_rows, preferred_element_type=jnp.float32)
    grad_ref[:, 0] = dk.reshape(grad_ref.shape[0], -1, width)
    grad_ref[:, 1] = dv.reshape(grad_ref.shape[0], -1, width)


def attention_call(q, tiles, do, bias, heads_kv, scale):
    heads_kv, group, blocks, tokens, head_width = q.shape
    tile_count = tiles.shape[1]
    rows_width = group * head_width
    q_spec = pl.BlockSpec((None, group, None, tokens, head_width), lambda j, h: (h, 0, j, 0, 0))
    k_spec = pl.BlockSpec((None, tile_count, None, tokens, head_width), lambda j, h: (j, 0, 0, 0, h))
    v_spec = pl.BlockSpec((None, tile_count, None, tokens, head_width), lambda j, h: (j, 0, 1, 0, h))
    b_spec = pl.BlockSpec((None, 1, bias.shape[-1]), lambda j, h: (j, 0, 0))
    g_spec = pl.BlockSpec((None, tile_count, 2, tokens, head_width), lambda j, h: (j, 0, 0, 0, h))
    steps = blocks * heads_kv
    rows = tokens * (rows_width // head_width)
    keys_n = tile_count * tokens
    matmul = 2 * rows * keys_n * head_width * steps
    moved = 2 * (3 * q.size + 2 * tiles.size) + 4 * tiles.size
    out = pl.pallas_call(
        functools.partial(forward_kernel, scale=scale),
        cost_estimate=pl.CostEstimate(
            flops=2 * matmul, transcendentals=rows * keys_n * steps, bytes_accessed=moved
        ),
        grid=(blocks, heads_kv),
        in_specs=[q_spec, k_spec, v_spec, b_spec],
        out_specs=q_spec,
        out_shape=jax.ShapeDtypeStruct(q.shape, jnp.bfloat16),
    )(q, tiles, tiles, bias)
    out, do = lax.optimization_barrier((out, do))
    grad_q, grads = pl.pallas_call(
        functools.partial(backward_kernel, scale=scale),
        cost_estimate=pl.CostEstimate(
            flops=5 * matmul, transcendentals=rows * keys_n * steps, bytes_accessed=moved
        ),
        grid=(blocks, heads_kv),
        in_specs=[q_spec, k_spec, v_spec, q_spec, q_spec, b_spec],
        out_specs=[q_spec, g_spec],
        out_shape=[
            jax.ShapeDtypeStruct(q.shape, jnp.bfloat16),
            jax.ShapeDtypeStruct(tiles.shape, jnp.float32),
        ],
    )(q, tiles, tiles, do, out, bias)
    return out, grad_q, grads


def exchange(array, axis, split_axis, concat_axis):
    count = lax.axis_size(axis)
    own = lax.axis_index(axis)
    piece = array.shape[split_axis] // count
    received = []
    for shift in range(count):
        target = (own + shift) % count
        part = lax.dynamic_slice_in_dim(array, target * piece, piece, split_axis)
        if shift:
            pairs = [(i, (i + shift) % count) for i in range(count)]
            part = lax.ppermute(part, axis, pairs)
        received.append(part)
    order = (own - jnp.arange(count)) % count
    stacked = jnp.take(jnp.stack(received), order, axis=0)
    stacked = jnp.moveaxis(stacked, 0, concat_axis)
    shape = list(array.shape)
    shape[split_axis] = piece
    shape[concat_axis] *= count
    return stacked.reshape(shape)


def padded(shard, sides, width):
    for axis, dim in sides:
        count, length = (lax.axis_size(axis), shard.shape[dim])
        up = [(i, (i + 1) % count) for i in range(count - 1)]
        down = [(j, i) for i, j in up]
        last = lax.slice_in_dim(shard, length - width, length, axis=dim)
        leading = lax.slice_in_dim(shard, 0, width, axis=dim)
        before = lax.ppermute(last, axis, up)
        after = lax.ppermute(leading, axis, down)
        shard = jnp.concatenate([before, shard, after], axis=dim)
    return shard


def from_root(block, axis, owner):
    block = jnp.where(lax.axis_index(axis) == owner, block, jnp.zeros_like(block))
    return lax.psum(block, axis)


def tree_sum(part, axis):
    count = lax.axis_size(axis)
    if count & (count - 1):
        return lax.psum(part.astype(jnp.bfloat16), axis).astype(jnp.float32)
    stride = 1
    while stride < count:
        pairs = [(i, i ^ stride) for i in range(count)]
        other = lax.ppermute(part.astype(jnp.bfloat16), axis, pairs)
        part = part + other.astype(jnp.float32)
        stride *= 2
    return part


def per_device(queries, keys, values, output_gradient, global_blocks, random_blocks):
    query_loc, key_loc, value_loc, grad_loc = (
        lax.all_to_all(queries.transpose(1, 0, 2), "head", split_axis=0, concat_axis=1, tiled=True),
        lax.all_to_all(keys, "head", split_axis=1, concat_axis=0, tiled=True),
        lax.all_to_all(values, "head", split_axis=1, concat_axis=0, tiled=True),
        output_gradient,
    )
    heads_q, shard_len, head_width = query_loc.shape
    heads_kv = key_loc.shape[1]
    heads_per_group = heads_q // heads_kv
    kv_width = heads_kv * head_width
    blocks = shard_len // BLOCK_TOKENS
    seq_count = lax.axis_size("seq")
    own_index = lax.axis_index("seq")
    block_total_count = seq_count * blocks
    capacity = (3 * blocks + seq_count - 2) // (seq_count - 1)
    entry_count = 3 * blocks
    score_scale = 1.0 / math.sqrt(head_width)
    kv_pair = jnp.stack(
        [key_loc.reshape(shard_len, kv_width), value_loc.reshape(shard_len, kv_width)]
    )
    extended = padded(kv_pair, (("seq", 1),), BLOCK_TOKENS)
    kv_tiles = kv_pair.reshape(2, blocks, BLOCK_TOKENS, kv_width).transpose(1, 0, 2, 3)
    global_owner = global_blocks // blocks
    global_offset = global_blocks % blocks
    own_global = (jnp.arange(blocks)[None, :] == global_offset[:, None]) & (
        global_owner == own_index
    )[:, None]
    all_entries = (
        random_blocks.reshape(seq_count, blocks, 3)
        .transpose(0, 2, 1)
        .reshape(seq_count, entry_count)
    )
    all_owner = all_entries // blocks
    entry_ids = jnp.arange(entry_count)
    entry_earlier = entry_ids[None, :] < entry_ids[:, None]
    all_rank = jnp.sum(
        (all_owner[:, :, None] == all_owner[:, None, :]) & entry_earlier[None], axis=2
    )
    my_entries = lax.dynamic_index_in_dim(all_entries, own_index, 0, keepdims=False)
    my_owner = lax.dynamic_index_in_dim(all_owner, own_index, 0, keepdims=False)
    my_rank = lax.dynamic_index_in_dim(all_rank, own_index, 0, keepdims=False)
    my_slot = my_owner * capacity + my_rank
    owned_here = (all_owner == own_index)[:, :, None] & (
        all_rank[:, :, None] == jnp.arange(capacity)[None, None, :]
    )
    offset_match = (all_entries % blocks)[:, :, None] == jnp.arange(blocks)[None, None, :]
    selector = jnp.einsum(
        "tec,teo->tco",
        owned_here.astype(jnp.bfloat16),
        offset_match.astype(jnp.bfloat16),
        preferred_element_type=jnp.float32,
    ).astype(jnp.bfloat16)
    everything = lax.all_gather(kv_pair, "seq", axis=1, tiled=True)
    query_loc, everything, grad_loc = lax.optimization_barrier((query_loc, everything, grad_loc))
    grad_loc = lax.all_to_all(grad_loc.transpose(1, 0, 2), "head", split_axis=0, concat_axis=1, tiled=True)
    tiled_all = everything.reshape(2, block_total_count, BLOCK_TOKENS, kv_width)
    random_tiles = jnp.take(tiled_all, my_entries, axis=1).transpose(1, 0, 2, 3)
    global_tiles = jnp.take(tiled_all, global_blocks, axis=1).transpose(1, 0, 2, 3)
    random_by_block = random_tiles.reshape(3, blocks, 2, BLOCK_TOKENS, kv_width).transpose(
        1, 0, 2, 3, 4
    )
    block_ids = own_index * blocks + jnp.arange(blocks)
    listed = jnp.concatenate(
        [
            jnp.stack([block_ids - 1, block_ids, block_ids + 1], axis=1),
            jnp.broadcast_to(global_blocks[None, :], (blocks, 2)),
            my_entries.reshape(3, blocks).T,
        ],
        axis=1,
    )
    inside = (listed >= 0) & (listed < block_total_count)
    tile_ids = jnp.arange(8)
    tile_earlier = tile_ids[None, :] < tile_ids[:, None]
    repeat = jnp.any((listed[:, :, None] == listed[:, None, :]) & tile_earlier[None], axis=2)
    live = inside & jnp.logical_not(repeat)

    tiles_per_block = []
    for position in range(blocks):
        near_tiles = lax.slice_in_dim(
            extended, position * BLOCK_TOKENS, (position + 3) * BLOCK_TOKENS, axis=1
        )
        near_tiles = near_tiles.reshape(2, 3, BLOCK_TOKENS, kv_width).transpose(1, 0, 2, 3)
        tiles_per_block.append(
            jnp.concatenate([near_tiles, global_tiles, random_by_block[position]], axis=0)
        )
    all_tiles = jnp.stack(tiles_per_block)
    tile_count = all_tiles.shape[1]
    bias = jnp.where(live, 0.0, -jnp.inf).astype(jnp.float32)
    bias = jnp.repeat(bias, BLOCK_TOKENS, axis=1).reshape(blocks, 1, tile_count * BLOCK_TOKENS)
    out_q, grad_q, tile_grads = attention_call(
        query_loc.reshape(heads_kv, heads_per_group, blocks, BLOCK_TOKENS, head_width),
        all_tiles,
        grad_loc.reshape(heads_kv, heads_per_group, blocks, BLOCK_TOKENS, head_width),
        bias,
        heads_kv,
        score_scale,
    )
    pad_spec_low = ((0, 2), (0, 0), (0, 0), (0, 0))
    pad_spec_mid = ((1, 1), (0, 0), (0, 0), (0, 0))
    pad_spec_high = ((2, 0), (0, 0), (0, 0), (0, 0))
    window_sum = (
        jnp.pad(tile_grads[:, 0], pad_spec_low)
        + jnp.pad(tile_grads[:, 1], pad_spec_mid)
        + jnp.pad(tile_grads[:, 2], pad_spec_high)
    )
    rims = jnp.concatenate([window_sum[0], window_sum[blocks + 1]], axis=1)
    returned_rims = padded(rims.astype(jnp.bfloat16), (("seq", 1),), BLOCK_TOKENS).astype(
        rims.dtype
    )
    interior = window_sum[1 : blocks + 1]
    interior = (
        interior.at[0]
        .add(returned_rims[:, :BLOCK_TOKENS])
        .at[blocks - 1]
        .add(returned_rims[:, 3 * BLOCK_TOKENS :])
    )
    global_terms = jnp.sum(tile_grads[:, 3:5], axis=0)
    global_total = tree_sum(global_terms, "seq")
    own_weight = own_global.astype(jnp.float32)[:, :, None, None, None]
    interior = interior + jnp.sum(own_weight * global_total[:, None], axis=0)
    random_terms = (
        tile_grads[:, 5:8]
        .transpose(1, 0, 2, 3, 4)
        .reshape(entry_count, 2, BLOCK_TOKENS, kv_width)
        .astype(jnp.bfloat16)
    )
    slot_onehot = (my_slot[:, None] == jnp.arange(seq_count * capacity)[None, :]).astype(
        jnp.bfloat16
    )
    back_buffer = jnp.einsum(
        "es,exbw->sxbw", slot_onehot, random_terms, preferred_element_type=jnp.float32
    ).astype(jnp.bfloat16)
    returned_terms = exchange(back_buffer, "seq", 0, 0)
    interior = interior + jnp.einsum(
        "tco,tcxbw->oxbw",
        selector,
        returned_terms.reshape(seq_count, capacity, 2, BLOCK_TOKENS, kv_width),
        preferred_element_type=jnp.float32,
    )
    kv_grad = interior.transpose(1, 0, 2, 3).reshape(2, shard_len, kv_width).astype(jnp.bfloat16)
    out_all = out_q.reshape(heads_q, shard_len, head_width)
    query_grad_all = grad_q.reshape(heads_q, shard_len, head_width)
    key_grad_all = kv_grad[0].reshape(shard_len, heads_kv, head_width)
    value_grad_all = kv_grad[1].reshape(shard_len, heads_kv, head_width)
    out_back = lax.all_to_all(out_all, "head", split_axis=1, concat_axis=0, tiled=True)
    query_back = lax.all_to_all(query_grad_all, "head", split_axis=1, concat_axis=0, tiled=True)
    (out_back, query_back), kv_grad = lax.optimization_barrier(((out_back, query_back), kv_grad))
    kv_grad = kv_grad.reshape(2, shard_len, heads_kv, head_width)
    kv_back = lax.all_to_all(kv_grad, "head", split_axis=1, concat_axis=2, tiled=True)
    return (out_back.transpose(1, 0, 2), query_back.transpose(1, 0, 2), kv_back[0], kv_back[1])


def solution(mesh):
    placed = (
        P(("seq", "head"), None, None),
        P(("seq", "head"), None, None),
        P(("seq", "head"), None, None),
        P(("seq", "head"), None, None),
        P(),
        P(),
    )
    return jax.shard_map(
        per_device,
        mesh=mesh,
        in_specs=placed,
        out_specs=(
            P(("seq", "head"), None, None),
            P(("seq", "head"), None, None),
            P(("seq", "head"), None, None),
            P(("seq", "head"), None, None),
        ),
        check_vma=False,
    )
```

```python
import functools
import math

import jax
import jax.numpy as jnp
from jax import lax
from jax.experimental import pallas as pl
from jax.sharding import PartitionSpec as P

BLOCK_TOKENS = 128


def rows_of(ref, group, width):
    return jnp.concatenate([ref[:, g * width:(g + 1) * width] for g in range(group)], axis=0)


def store_rows(ref, value, group, width):
    tokens = ref.shape[0]
    for g in range(group):
        ref[:, g * width:(g + 1) * width] = value[g * tokens:(g + 1) * tokens, :]


def softmax_rows(q, k, bias, scale):
    rows_by_cols = (((1,), (1,)), ((), ()))
    s = lax.dot_general(q, k, rows_by_cols, preferred_element_type=jnp.float32) * scale
    s = s + bias
    e = jnp.exp(s - jnp.max(s, axis=1, keepdims=True))
    return e / jnp.sum(e, axis=1, keepdims=True)


def forward_kernel(q_ref, k_ref, v_ref, bias_ref, out_ref, *, scale):
    width = k_ref.shape[-1]
    q = q_ref[...].reshape(-1, width)
    k = k_ref[...].reshape(-1, width)
    v = v_ref[...].reshape(-1, width)
    p_low = softmax_rows(q, k, bias_ref[...], scale).astype(jnp.bfloat16)
    o_low = jnp.dot(p_low, v, preferred_element_type=jnp.float32).astype(jnp.bfloat16)
    out_ref[...] = o_low.reshape(out_ref.shape)


def backward_kernel(q_ref, k_ref, v_ref, do_ref, o_ref, bias_ref, dq_ref, grad_ref, *, scale):
    width = k_ref.shape[-1]
    q = q_ref[...].reshape(-1, width)
    do = do_ref[...].reshape(-1, width)
    o_low = o_ref[...].reshape(-1, width)
    k = k_ref[...].reshape(-1, width)
    v = v_ref[...].reshape(-1, width)
    rows_by_cols = (((1,), (1,)), ((), ()))
    over_rows = (((0,), (0,)), ((), ()))
    p = softmax_rows(q, k, bias_ref[...], scale)
    p_low = p.astype(jnp.bfloat16)
    delta = jnp.sum(do.astype(jnp.float32) * o_low.astype(jnp.float32), axis=1, keepdims=True)
    dp = lax.dot_general(do, v, rows_by_cols, preferred_element_type=jnp.float32)
    ds_low = (p * (dp - delta)).astype(jnp.bfloat16)
    dq = jnp.dot(ds_low, k, preferred_element_type=jnp.float32) * scale
    dq_ref[...] = dq.astype(jnp.bfloat16).reshape(dq_ref.shape)
    dk = lax.dot_general(ds_low, q, over_rows, preferred_element_type=jnp.float32) * scale
    dv = lax.dot_general(p_low, do, over_rows, preferred_element_type=jnp.float32)
    grad_ref[:, 0] = dk.reshape(grad_ref.shape[0], -1, width)
    grad_ref[:, 1] = dv.reshape(grad_ref.shape[0], -1, width)


def attention_call(q, tiles, do, bias, heads_kv, scale):
    heads_kv, group, blocks, tokens, head_width = q.shape
    tile_count = tiles.shape[1]
    rows_width = group * head_width
    q_spec = pl.BlockSpec((None, group, None, tokens, head_width), lambda j, h: (h, 0, j, 0, 0))
    o_spec = pl.BlockSpec((None, None, group, tokens, head_width), lambda j, h: (j, h, 0, 0, 0))
    o_shape = jax.ShapeDtypeStruct((blocks, heads_kv, group, tokens, head_width), jnp.bfloat16)
    k_spec = pl.BlockSpec((None, tile_count, None, tokens, head_width), lambda j, h: (j, 0, 0, 0, h))
    v_spec = pl.BlockSpec((None, tile_count, None, tokens, head_width), lambda j, h: (j, 0, 1, 0, h))
    b_spec = pl.BlockSpec((None, 1, bias.shape[-1]), lambda j, h: (j, 0, 0))
    g_spec = pl.BlockSpec((None, tile_count, 2, tokens, head_width), lambda j, h: (j, 0, 0, 0, h))
    steps = blocks * heads_kv
    rows = tokens * (rows_width // head_width)
    keys_n = tile_count * tokens
    matmul = 2 * rows * keys_n * head_width * steps
    moved = 2 * (3 * q.size + 2 * tiles.size) + 4 * tiles.size
    out = pl.pallas_call(
        functools.partial(forward_kernel, scale=scale),
        cost_estimate=pl.CostEstimate(
            flops=2 * matmul, transcendentals=rows * keys_n * steps, bytes_accessed=moved
        ),
        grid=(blocks, heads_kv),
        in_specs=[q_spec, k_spec, v_spec, b_spec],
        out_specs=o_spec,
        out_shape=o_shape,
    )(q, tiles, tiles, bias)
    out, do = lax.optimization_barrier((out, do))
    grad_q, grads = pl.pallas_call(
        functools.partial(backward_kernel, scale=scale),
        cost_estimate=pl.CostEstimate(
            flops=5 * matmul, transcendentals=rows * keys_n * steps, bytes_accessed=moved
        ),
        grid=(blocks, heads_kv),
        in_specs=[q_spec, k_spec, v_spec, q_spec, o_spec, b_spec],
        out_specs=[o_spec, g_spec],
        out_shape=[
            o_shape,
            jax.ShapeDtypeStruct(tiles.shape, jnp.float32),
        ],
    )(q, tiles, tiles, do, out, bias)
    return out, grad_q, grads


def exchange(array, axis, split_axis, concat_axis):
    count = lax.axis_size(axis)
    own = lax.axis_index(axis)
    piece = array.shape[split_axis] // count
    received = []
    for shift in range(count):
        target = (own + shift) % count
        part = lax.dynamic_slice_in_dim(array, target * piece, piece, split_axis)
        if shift:
            pairs = [(i, (i + shift) % count) for i in range(count)]
            part = lax.ppermute(part, axis, pairs)
        received.append(part)
    order = (own - jnp.arange(count)) % count
    stacked = jnp.take(jnp.stack(received), order, axis=0)
    stacked = jnp.moveaxis(stacked, 0, concat_axis)
    shape = list(array.shape)
    shape[split_axis] = piece
    shape[concat_axis] *= count
    return stacked.reshape(shape)


def padded(shard, sides, width):
    for axis, dim in sides:
        count, length = (lax.axis_size(axis), shard.shape[dim])
        up = [(i, (i + 1) % count) for i in range(count - 1)]
        down = [(j, i) for i, j in up]
        last = lax.slice_in_dim(shard, length - width, length, axis=dim)
        leading = lax.slice_in_dim(shard, 0, width, axis=dim)
        before = lax.ppermute(last, axis, up)
        after = lax.ppermute(leading, axis, down)
        shard = jnp.concatenate([before, shard, after], axis=dim)
    return shard


def from_root(block, axis, owner):
    block = jnp.where(lax.axis_index(axis) == owner, block, jnp.zeros_like(block))
    return lax.psum(block, axis)


def tree_sum(part, axis):
    count = lax.axis_size(axis)
    if count & (count - 1):
        return lax.psum(part.astype(jnp.bfloat16), axis).astype(jnp.float32)
    stride = 1
    while stride < count:
        pairs = [(i, i ^ stride) for i in range(count)]
        other = lax.ppermute(part.astype(jnp.bfloat16), axis, pairs)
        part = part + other.astype(jnp.float32)
        stride *= 2
    return part


def per_device(queries, keys, values, output_gradient, global_blocks, random_blocks):
    query_loc, key_loc, value_loc, grad_loc = (
        lax.all_to_all(queries.transpose(1, 0, 2), "head", split_axis=0, concat_axis=1, tiled=True),
        lax.all_to_all(keys, "head", split_axis=1, concat_axis=0, tiled=True),
        lax.all_to_all(values, "head", split_axis=1, concat_axis=0, tiled=True),
        output_gradient,
    )
    heads_q, shard_len, head_width = query_loc.shape
    heads_kv = key_loc.shape[1]
    heads_per_group = heads_q // heads_kv
    kv_width = heads_kv * head_width
    blocks = shard_len // BLOCK_TOKENS
    seq_count = lax.axis_size("seq")
    own_index = lax.axis_index("seq")
    block_total_count = seq_count * blocks
    capacity = (3 * blocks + seq_count - 2) // (seq_count - 1)
    entry_count = 3 * blocks
    score_scale = 1.0 / math.sqrt(head_width)
    kv_pair = jnp.stack(
        [key_loc.reshape(shard_len, kv_width), value_loc.reshape(shard_len, kv_width)]
    )
    extended = padded(kv_pair, (("seq", 1),), BLOCK_TOKENS)
    kv_tiles = kv_pair.reshape(2, blocks, BLOCK_TOKENS, kv_width).transpose(1, 0, 2, 3)
    global_owner = global_blocks // blocks
    global_offset = global_blocks % blocks
    own_global = (jnp.arange(blocks)[None, :] == global_offset[:, None]) & (
        global_owner == own_index
    )[:, None]
    all_entries = (
        random_blocks.reshape(seq_count, blocks, 3)
        .transpose(0, 2, 1)
        .reshape(seq_count, entry_count)
    )
    all_owner = all_entries // blocks
    entry_ids = jnp.arange(entry_count)
    entry_earlier = entry_ids[None, :] < entry_ids[:, None]
    all_rank = jnp.sum(
        (all_owner[:, :, None] == all_owner[:, None, :]) & entry_earlier[None], axis=2
    )
    my_entries = lax.dynamic_index_in_dim(all_entries, own_index, 0, keepdims=False)
    my_owner = lax.dynamic_index_in_dim(all_owner, own_index, 0, keepdims=False)
    my_rank = lax.dynamic_index_in_dim(all_rank, own_index, 0, keepdims=False)
    my_slot = my_owner * capacity + my_rank
    owned_here = (all_owner == own_index)[:, :, None] & (
        all_rank[:, :, None] == jnp.arange(capacity)[None, None, :]
    )
    offset_match = (all_entries % blocks)[:, :, None] == jnp.arange(blocks)[None, None, :]
    selector = jnp.einsum(
        "tec,teo->tco",
        owned_here.astype(jnp.bfloat16),
        offset_match.astype(jnp.bfloat16),
        preferred_element_type=jnp.float32,
    ).astype(jnp.bfloat16)
    everything = lax.all_gather(kv_pair, "seq", axis=1, tiled=True)
    grad_loc = grad_loc.transpose(1, 0, 2)
    query_loc, everything, grad_loc = lax.optimization_barrier((query_loc, everything, grad_loc))
    grad_loc = lax.all_to_all(grad_loc, "head", split_axis=0, concat_axis=1, tiled=True)
    tiled_all = everything.reshape(2, block_total_count, BLOCK_TOKENS, kv_width)
    random_tiles = jnp.take(tiled_all, my_entries, axis=1).transpose(1, 0, 2, 3)
    global_tiles = jnp.take(tiled_all, global_blocks, axis=1).transpose(1, 0, 2, 3)
    random_by_block = random_tiles.reshape(3, blocks, 2, BLOCK_TOKENS, kv_width).transpose(
        1, 0, 2, 3, 4
    )
    block_ids = own_index * blocks + jnp.arange(blocks)
    listed = jnp.concatenate(
        [
            jnp.stack([block_ids - 1, block_ids, block_ids + 1], axis=1),
            jnp.broadcast_to(global_blocks[None, :], (blocks, 2)),
            my_entries.reshape(3, blocks).T,
        ],
        axis=1,
    )
    inside = (listed >= 0) & (listed < block_total_count)
    tile_ids = jnp.arange(8)
    tile_earlier = tile_ids[None, :] < tile_ids[:, None]
    repeat = jnp.any((listed[:, :, None] == listed[:, None, :]) & tile_earlier[None], axis=2)
    live = inside & jnp.logical_not(repeat)

    tiles_per_block = []
    for position in range(blocks):
        near_tiles = lax.slice_in_dim(
            extended, position * BLOCK_TOKENS, (position + 3) * BLOCK_TOKENS, axis=1
        )
        near_tiles = near_tiles.reshape(2, 3, BLOCK_TOKENS, kv_width).transpose(1, 0, 2, 3)
        tiles_per_block.append(
            jnp.concatenate([near_tiles, global_tiles, random_by_block[position]], axis=0)
        )
    all_tiles = jnp.stack(tiles_per_block)
    tile_count = all_tiles.shape[1]
    bias = jnp.where(live, 0.0, -jnp.inf).astype(jnp.float32)
    bias = jnp.repeat(bias, BLOCK_TOKENS, axis=1).reshape(blocks, 1, tile_count * BLOCK_TOKENS)
    out_q, grad_q, tile_grads = attention_call(
        query_loc.reshape(heads_kv, heads_per_group, blocks, BLOCK_TOKENS, head_width),
        all_tiles,
        grad_loc.reshape(heads_kv, heads_per_group, blocks, BLOCK_TOKENS, head_width),
        bias,
        heads_kv,
        score_scale,
    )
    pad_spec_low = ((0, 2), (0, 0), (0, 0), (0, 0))
    pad_spec_mid = ((1, 1), (0, 0), (0, 0), (0, 0))
    pad_spec_high = ((2, 0), (0, 0), (0, 0), (0, 0))
    window_sum = (
        jnp.pad(tile_grads[:, 0], pad_spec_low)
        + jnp.pad(tile_grads[:, 1], pad_spec_mid)
        + jnp.pad(tile_grads[:, 2], pad_spec_high)
    )
    rims = jnp.concatenate([window_sum[0], window_sum[blocks + 1]], axis=1)
    returned_rims = padded(rims.astype(jnp.bfloat16), (("seq", 1),), BLOCK_TOKENS).astype(
        rims.dtype
    )
    interior = window_sum[1 : blocks + 1]
    interior = (
        interior.at[0]
        .add(returned_rims[:, :BLOCK_TOKENS])
        .at[blocks - 1]
        .add(returned_rims[:, 3 * BLOCK_TOKENS :])
    )
    global_terms = jnp.sum(tile_grads[:, 3:5], axis=0)
    global_total = tree_sum(global_terms, "seq")
    own_weight = own_global.astype(jnp.float32)[:, :, None, None, None]
    interior = interior + jnp.sum(own_weight * global_total[:, None], axis=0)
    random_terms = (
        tile_grads[:, 5:8]
        .transpose(1, 0, 2, 3, 4)
        .reshape(entry_count, 2, BLOCK_TOKENS, kv_width)
        .astype(jnp.bfloat16)
    )
    slot_onehot = (my_slot[:, None] == jnp.arange(seq_count * capacity)[None, :]).astype(
        jnp.bfloat16
    )
    back_buffer = jnp.einsum(
        "es,exbw->sxbw", slot_onehot, random_terms, preferred_element_type=jnp.float32
    ).astype(jnp.bfloat16)
    returned_terms = exchange(back_buffer, "seq", 0, 0)
    interior = interior + jnp.einsum(
        "tco,tcxbw->oxbw",
        selector,
        returned_terms.reshape(seq_count, capacity, 2, BLOCK_TOKENS, kv_width),
        preferred_element_type=jnp.float32,
    )
    kv_grad = interior.transpose(1, 0, 2, 3).reshape(2, shard_len, kv_width).astype(jnp.bfloat16)
    out_all = out_q.reshape(blocks, heads_q, BLOCK_TOKENS, head_width)
    query_grad_all = grad_q.reshape(blocks, heads_q, BLOCK_TOKENS, head_width)
    key_grad_all = kv_grad[0].reshape(shard_len, heads_kv, head_width)
    value_grad_all = kv_grad[1].reshape(shard_len, heads_kv, head_width)
    out_back = lax.all_to_all(out_all, "head", split_axis=0, concat_axis=1, tiled=True)
    query_back = lax.all_to_all(query_grad_all, "head", split_axis=0, concat_axis=1, tiled=True)
    (out_back, query_back), kv_grad = lax.optimization_barrier(((out_back, query_back), kv_grad))
    kv_grad = kv_grad.reshape(2, shard_len, heads_kv, head_width)
    kv_back = lax.all_to_all(kv_grad, "head", split_axis=1, concat_axis=2, tiled=True)
    out_back = out_back.reshape(-1, BLOCK_TOKENS, head_width).transpose(1, 0, 2)
    query_back = query_back.reshape(-1, BLOCK_TOKENS, head_width).transpose(1, 0, 2)
    return (out_back, query_back, kv_back[0], kv_back[1])


def solution(mesh):
    placed = (
        P(("seq", "head"), None, None),
        P(("seq", "head"), None, None),
        P(("seq", "head"), None, None),
        P(("seq", "head"), None, None),
        P(),
        P(),
    )
    return jax.shard_map(
        per_device,
        mesh=mesh,
        in_specs=placed,
        out_specs=(
            P(("seq", "head"), None, None),
            P(("seq", "head"), None, None),
            P(("seq", "head"), None, None),
            P(("seq", "head"), None, None),
        ),
        check_vma=False,
    )
```

```python
import functools
import math

import jax
import jax.numpy as jnp
from jax import lax
from jax.experimental import pallas as pl
from jax.sharding import PartitionSpec as P

BLOCK_TOKENS = 128


def rows_of(ref, group, width):
    return jnp.concatenate([ref[:, g * width:(g + 1) * width] for g in range(group)], axis=0)


def store_rows(ref, value, group, width):
    tokens = ref.shape[0]
    for g in range(group):
        ref[:, g * width:(g + 1) * width] = value[g * tokens:(g + 1) * tokens, :]


def softmax_rows(q, k, bias, scale):
    rows_by_cols = (((1,), (1,)), ((), ()))
    s = lax.dot_general(q, k, rows_by_cols, preferred_element_type=jnp.float32) * scale
    s = s + bias
    e = jnp.exp(s - jnp.max(s, axis=1, keepdims=True))
    return e / jnp.sum(e, axis=1, keepdims=True)


def forward_kernel(q_ref, k_ref, v_ref, bias_ref, out_ref, *, scale):
    width = k_ref.shape[-1]
    q = q_ref[...].reshape(-1, width)
    k = k_ref[...].reshape(-1, width)
    v = v_ref[...].reshape(-1, width)
    p_low = softmax_rows(q, k, bias_ref[...], scale).astype(jnp.bfloat16)
    o_low = jnp.dot(p_low, v, preferred_element_type=jnp.float32).astype(jnp.bfloat16)
    out_ref[...] = o_low.reshape(out_ref.shape)


def backward_kernel(q_ref, k_ref, v_ref, do_ref, o_ref, bias_ref, dq_ref, grad_ref, *, scale):
    width = k_ref.shape[-1]
    q = q_ref[...].reshape(-1, width)
    do = do_ref[...].reshape(-1, width)
    o_low = o_ref[...].reshape(-1, width)
    k = k_ref[...].reshape(-1, width)
    v = v_ref[...].reshape(-1, width)
    rows_by_cols = (((1,), (1,)), ((), ()))
    over_rows = (((0,), (0,)), ((), ()))
    p = softmax_rows(q, k, bias_ref[...], scale)
    p_low = p.astype(jnp.bfloat16)
    delta = jnp.sum(do.astype(jnp.float32) * o_low.astype(jnp.float32), axis=1, keepdims=True)
    dp = lax.dot_general(do, v, rows_by_cols, preferred_element_type=jnp.float32)
    ds_low = (p * (dp - delta)).astype(jnp.bfloat16)
    dq = jnp.dot(ds_low, k, preferred_element_type=jnp.float32) * scale
    dq_ref[...] = dq.astype(jnp.bfloat16).reshape(dq_ref.shape)
    dk = lax.dot_general(ds_low, q, over_rows, preferred_element_type=jnp.float32) * scale
    dv = lax.dot_general(p_low, do, over_rows, preferred_element_type=jnp.float32)
    grad_ref[:, 0] = dk.reshape(grad_ref.shape[0], -1, width)
    grad_ref[:, 1] = dv.reshape(grad_ref.shape[0], -1, width)


def attention_call(q, tiles, do, bias, heads_kv, scale):
    heads_kv, group, blocks, tokens, head_width = q.shape
    tile_count = tiles.shape[1]
    rows_width = group * head_width
    q_spec = pl.BlockSpec((None, group, None, tokens, head_width), lambda j, h: (h, 0, j, 0, 0))
    o_spec = pl.BlockSpec((None, None, group, tokens, head_width), lambda j, h: (j, h, 0, 0, 0))
    o_shape = jax.ShapeDtypeStruct((blocks, heads_kv, group, tokens, head_width), jnp.bfloat16)
    k_spec = pl.BlockSpec((None, tile_count, None, tokens, head_width), lambda j, h: (j, 0, 0, 0, h))
    v_spec = pl.BlockSpec((None, tile_count, None, tokens, head_width), lambda j, h: (j, 0, 1, 0, h))
    b_spec = pl.BlockSpec((None, 1, bias.shape[-1]), lambda j, h: (j, 0, 0))
    g_spec = pl.BlockSpec((None, tile_count, 2, tokens, head_width), lambda j, h: (j, 0, 0, 0, h))
    steps = blocks * heads_kv
    rows = tokens * (rows_width // head_width)
    keys_n = tile_count * tokens
    matmul = 2 * rows * keys_n * head_width * steps
    moved = 2 * (3 * q.size + 2 * tiles.size) + 4 * tiles.size
    out = pl.pallas_call(
        functools.partial(forward_kernel, scale=scale),
        cost_estimate=pl.CostEstimate(
            flops=2 * matmul, transcendentals=rows * keys_n * steps, bytes_accessed=moved
        ),
        grid=(blocks, heads_kv),
        in_specs=[q_spec, k_spec, v_spec, b_spec],
        out_specs=o_spec,
        out_shape=o_shape,
    )(q, tiles, tiles, bias)
    out, do = lax.optimization_barrier((out, do))
    grad_q, grads = pl.pallas_call(
        functools.partial(backward_kernel, scale=scale),
        cost_estimate=pl.CostEstimate(
            flops=5 * matmul, transcendentals=rows * keys_n * steps, bytes_accessed=moved
        ),
        grid=(blocks, heads_kv),
        in_specs=[q_spec, k_spec, v_spec, q_spec, o_spec, b_spec],
        out_specs=[o_spec, g_spec],
        out_shape=[
            o_shape,
            jax.ShapeDtypeStruct(tiles.shape, jnp.float32),
        ],
    )(q, tiles, tiles, do, out, bias)
    return out, grad_q, grads


def exchange(array, axis, split_axis, concat_axis):
    count = lax.axis_size(axis)
    own = lax.axis_index(axis)
    piece = array.shape[split_axis] // count
    received = []
    for shift in range(count):
        target = (own + shift) % count
        part = lax.dynamic_slice_in_dim(array, target * piece, piece, split_axis)
        if shift:
            pairs = [(i, (i + shift) % count) for i in range(count)]
            part = lax.ppermute(part, axis, pairs)
        received.append(part)
    order = (own - jnp.arange(count)) % count
    stacked = jnp.take(jnp.stack(received), order, axis=0)
    stacked = jnp.moveaxis(stacked, 0, concat_axis)
    shape = list(array.shape)
    shape[split_axis] = piece
    shape[concat_axis] *= count
    return stacked.reshape(shape)


def padded(shard, sides, width):
    for axis, dim in sides:
        count, length = (lax.axis_size(axis), shard.shape[dim])
        up = [(i, (i + 1) % count) for i in range(count - 1)]
        down = [(j, i) for i, j in up]
        last = lax.slice_in_dim(shard, length - width, length, axis=dim)
        leading = lax.slice_in_dim(shard, 0, width, axis=dim)
        before = lax.ppermute(last, axis, up)
        after = lax.ppermute(leading, axis, down)
        shard = jnp.concatenate([before, shard, after], axis=dim)
    return shard


def from_root(block, axis, owner):
    block = jnp.where(lax.axis_index(axis) == owner, block, jnp.zeros_like(block))
    return lax.psum(block, axis)


def tree_sum(part, axis):
    count = lax.axis_size(axis)
    if count & (count - 1):
        return lax.psum(part.astype(jnp.bfloat16), axis).astype(jnp.float32)
    stride = 1
    while stride < count:
        pairs = [(i, i ^ stride) for i in range(count)]
        other = lax.ppermute(part.astype(jnp.bfloat16), axis, pairs)
        part = part + other.astype(jnp.float32)
        stride *= 2
    return part


def per_device(queries, keys, values, output_gradient, global_blocks, random_blocks):
    query_loc, key_loc, value_loc, grad_loc = (
        lax.all_to_all(queries.transpose(1, 0, 2), "head", split_axis=0, concat_axis=1, tiled=True),
        None,
        None,
        output_gradient,
    )
    kv_loc = lax.all_to_all(
        jnp.stack([keys, values]), "head", split_axis=2, concat_axis=1, tiled=True
    )
    key_loc, value_loc = kv_loc[0], kv_loc[1]
    heads_q, shard_len, head_width = query_loc.shape
    heads_kv = key_loc.shape[1]
    heads_per_group = heads_q // heads_kv
    kv_width = heads_kv * head_width
    blocks = shard_len // BLOCK_TOKENS
    seq_count = lax.axis_size("seq")
    own_index = lax.axis_index("seq")
    block_total_count = seq_count * blocks
    capacity = (3 * blocks + seq_count - 2) // (seq_count - 1)
    entry_count = 3 * blocks
    score_scale = 1.0 / math.sqrt(head_width)
    kv_pair = kv_loc.reshape(2, shard_len, kv_width)
    extended = padded(kv_pair, (("seq", 1),), BLOCK_TOKENS)
    kv_tiles = kv_pair.reshape(2, blocks, BLOCK_TOKENS, kv_width).transpose(1, 0, 2, 3)
    global_owner = global_blocks // blocks
    global_offset = global_blocks % blocks
    own_global = (jnp.arange(blocks)[None, :] == global_offset[:, None]) & (
        global_owner == own_index
    )[:, None]
    all_entries = (
        random_blocks.reshape(seq_count, blocks, 3)
        .transpose(0, 2, 1)
        .reshape(seq_count, entry_count)
    )
    all_owner = all_entries // blocks
    entry_ids = jnp.arange(entry_count)
    entry_earlier = entry_ids[None, :] < entry_ids[:, None]
    all_rank = jnp.sum(
        (all_owner[:, :, None] == all_owner[:, None, :]) & entry_earlier[None], axis=2
    )
    my_entries = lax.dynamic_index_in_dim(all_entries, own_index, 0, keepdims=False)
    my_owner = lax.dynamic_index_in_dim(all_owner, own_index, 0, keepdims=False)
    my_rank = lax.dynamic_index_in_dim(all_rank, own_index, 0, keepdims=False)
    my_slot = my_owner * capacity + my_rank
    owned_here = (all_owner == own_index)[:, :, None] & (
        all_rank[:, :, None] == jnp.arange(capacity)[None, None, :]
    )
    offset_match = (all_entries % blocks)[:, :, None] == jnp.arange(blocks)[None, None, :]
    selector = jnp.einsum(
        "tec,teo->tco",
        owned_here.astype(jnp.bfloat16),
        offset_match.astype(jnp.bfloat16),
        preferred_element_type=jnp.float32,
    ).astype(jnp.bfloat16)
    everything = lax.all_gather(kv_pair, "seq", axis=1, tiled=True)
    grad_loc = grad_loc.transpose(1, 0, 2)
    query_loc, everything, grad_loc = lax.optimization_barrier((query_loc, everything, grad_loc))
    grad_loc = lax.all_to_all(grad_loc, "head", split_axis=0, concat_axis=1, tiled=True)
    tiled_all = everything.reshape(2, block_total_count, BLOCK_TOKENS, kv_width)
    random_tiles = jnp.take(tiled_all, my_entries, axis=1).transpose(1, 0, 2, 3)
    global_tiles = jnp.take(tiled_all, global_blocks, axis=1).transpose(1, 0, 2, 3)
    random_by_block = random_tiles.reshape(3, blocks, 2, BLOCK_TOKENS, kv_width).transpose(
        1, 0, 2, 3, 4
    )
    block_ids = own_index * blocks + jnp.arange(blocks)
    listed = jnp.concatenate(
        [
            jnp.stack([block_ids - 1, block_ids, block_ids + 1], axis=1),
            jnp.broadcast_to(global_blocks[None, :], (blocks, 2)),
            my_entries.reshape(3, blocks).T,
        ],
        axis=1,
    )
    inside = (listed >= 0) & (listed < block_total_count)
    tile_ids = jnp.arange(8)
    tile_earlier = tile_ids[None, :] < tile_ids[:, None]
    repeat = jnp.any((listed[:, :, None] == listed[:, None, :]) & tile_earlier[None], axis=2)
    live = inside & jnp.logical_not(repeat)

    tiles_per_block = []
    for position in range(blocks):
        near_tiles = lax.slice_in_dim(
            extended, position * BLOCK_TOKENS, (position + 3) * BLOCK_TOKENS, axis=1
        )
        near_tiles = near_tiles.reshape(2, 3, BLOCK_TOKENS, kv_width).transpose(1, 0, 2, 3)
        tiles_per_block.append(
            jnp.concatenate([near_tiles, global_tiles, random_by_block[position]], axis=0)
        )
    all_tiles = jnp.stack(tiles_per_block)
    tile_count = all_tiles.shape[1]
    bias = jnp.where(live, 0.0, -jnp.inf).astype(jnp.float32)
    bias = jnp.repeat(bias, BLOCK_TOKENS, axis=1).reshape(blocks, 1, tile_count * BLOCK_TOKENS)
    out_q, grad_q, tile_grads = attention_call(
        query_loc.reshape(heads_kv, heads_per_group, blocks, BLOCK_TOKENS, head_width),
        all_tiles,
        grad_loc.reshape(heads_kv, heads_per_group, blocks, BLOCK_TOKENS, head_width),
        bias,
        heads_kv,
        score_scale,
    )
    pad_spec_low = ((0, 2), (0, 0), (0, 0), (0, 0))
    pad_spec_mid = ((1, 1), (0, 0), (0, 0), (0, 0))
    pad_spec_high = ((2, 0), (0, 0), (0, 0), (0, 0))
    window_sum = (
        jnp.pad(tile_grads[:, 0], pad_spec_low)
        + jnp.pad(tile_grads[:, 1], pad_spec_mid)
        + jnp.pad(tile_grads[:, 2], pad_spec_high)
    )
    rims = jnp.concatenate([window_sum[0], window_sum[blocks + 1]], axis=1)
    returned_rims = padded(rims.astype(jnp.bfloat16), (("seq", 1),), BLOCK_TOKENS).astype(
        rims.dtype
    )
    interior = window_sum[1 : blocks + 1]
    interior = (
        interior.at[0]
        .add(returned_rims[:, :BLOCK_TOKENS])
        .at[blocks - 1]
        .add(returned_rims[:, 3 * BLOCK_TOKENS :])
    )
    global_terms = jnp.sum(tile_grads[:, 3:5], axis=0)
    global_total = tree_sum(global_terms, "seq")
    own_weight = own_global.astype(jnp.float32)[:, :, None, None, None]
    interior = interior + jnp.sum(own_weight * global_total[:, None], axis=0)
    random_terms = (
        tile_grads[:, 5:8]
        .transpose(1, 0, 2, 3, 4)
        .reshape(entry_count, 2, BLOCK_TOKENS, kv_width)
        .astype(jnp.bfloat16)
    )
    slot_onehot = (my_slot[:, None] == jnp.arange(seq_count * capacity)[None, :]).astype(
        jnp.bfloat16
    )
    back_buffer = jnp.einsum(
        "es,exbw->sxbw", slot_onehot, random_terms, preferred_element_type=jnp.float32
    ).astype(jnp.bfloat16)
    returned_terms = exchange(back_buffer, "seq", 0, 0)
    interior = interior + jnp.einsum(
        "tco,tcxbw->oxbw",
        selector,
        returned_terms.reshape(seq_count, capacity, 2, BLOCK_TOKENS, kv_width),
        preferred_element_type=jnp.float32,
    )
    kv_grad = interior.transpose(1, 0, 2, 3).reshape(2, shard_len, kv_width).astype(jnp.bfloat16)
    out_all = out_q.reshape(blocks, heads_q, BLOCK_TOKENS, head_width)
    query_grad_all = grad_q.reshape(blocks, heads_q, BLOCK_TOKENS, head_width)
    key_grad_all = kv_grad[0].reshape(shard_len, heads_kv, head_width)
    value_grad_all = kv_grad[1].reshape(shard_len, heads_kv, head_width)
    out_back = lax.all_to_all(out_all, "head", split_axis=0, concat_axis=1, tiled=True)
    query_back = lax.all_to_all(query_grad_all, "head", split_axis=0, concat_axis=1, tiled=True)
    kv_blocks = interior.astype(jnp.bfloat16).reshape(
        blocks, 2, BLOCK_TOKENS, heads_kv, head_width
    )
    (out_back, query_back), kv_blocks = lax.optimization_barrier(((out_back, query_back), kv_blocks))
    kv_back = lax.all_to_all(kv_blocks, "head", split_axis=0, concat_axis=3, tiled=True)[0]
    out_back = out_back.reshape(-1, BLOCK_TOKENS, head_width).transpose(1, 0, 2)
    query_back = query_back.reshape(-1, BLOCK_TOKENS, head_width).transpose(1, 0, 2)
    return (out_back, query_back, kv_back[0], kv_back[1])


def solution(mesh):
    placed = (
        P(("seq", "head"), None, None),
        P(("seq", "head"), None, None),
        P(("seq", "head"), None, None),
        P(("seq", "head"), None, None),
        P(),
        P(),
    )
    return jax.shard_map(
        per_device,
        mesh=mesh,
        in_specs=placed,
        out_specs=(
            P(("seq", "head"), None, None),
            P(("seq", "head"), None, None),
            P(("seq", "head"), None, None),
            P(("seq", "head"), None, None),
        ),
        check_vma=False,
    )
```

```python
import functools
import math

import jax
import jax.numpy as jnp
from jax import lax
from jax.experimental import pallas as pl
from jax.sharding import PartitionSpec as P

BLOCK_TOKENS = 128


def rows_of(ref, group, width):
    return jnp.concatenate([ref[:, g * width:(g + 1) * width] for g in range(group)], axis=0)


def store_rows(ref, value, group, width):
    tokens = ref.shape[0]
    for g in range(group):
        ref[:, g * width:(g + 1) * width] = value[g * tokens:(g + 1) * tokens, :]


def softmax_rows(q, k, bias, scale):
    rows_by_cols = (((1,), (1,)), ((), ()))
    s = lax.dot_general(q, k, rows_by_cols, preferred_element_type=jnp.float32) * scale
    s = s + bias
    e = jnp.exp(s - jnp.max(s, axis=1, keepdims=True))
    return e / jnp.sum(e, axis=1, keepdims=True)


def forward_kernel(q_ref, k_ref, v_ref, bias_ref, out_ref, *, scale):
    width = k_ref.shape[-1]
    q = q_ref[...].reshape(-1, width)
    k = k_ref[...].reshape(-1, width)
    v = v_ref[...].reshape(-1, width)
    p_low = softmax_rows(q, k, bias_ref[...], scale).astype(jnp.bfloat16)
    o_low = jnp.dot(p_low, v, preferred_element_type=jnp.float32).astype(jnp.bfloat16)
    store_rows(out_ref, o_low, out_ref.shape[1] // width, width)


def backward_kernel(q_ref, k_ref, v_ref, do_ref, o_ref, bias_ref, dq_ref, grad_ref, *, scale):
    width = k_ref.shape[-1]
    q = q_ref[...].reshape(-1, width)
    do = do_ref[...].reshape(-1, width)
    o_low = rows_of(o_ref, o_ref.shape[1] // width, width)
    k = k_ref[...].reshape(-1, width)
    v = v_ref[...].reshape(-1, width)
    rows_by_cols = (((1,), (1,)), ((), ()))
    over_rows = (((0,), (0,)), ((), ()))
    p = softmax_rows(q, k, bias_ref[...], scale)
    p_low = p.astype(jnp.bfloat16)
    delta = jnp.sum(do.astype(jnp.float32) * o_low.astype(jnp.float32), axis=1, keepdims=True)
    dp = lax.dot_general(do, v, rows_by_cols, preferred_element_type=jnp.float32)
    ds_low = (p * (dp - delta)).astype(jnp.bfloat16)
    dq = jnp.dot(ds_low, k, preferred_element_type=jnp.float32) * scale
    store_rows(dq_ref, dq.astype(jnp.bfloat16), dq_ref.shape[1] // width, width)
    dk = lax.dot_general(ds_low, q, over_rows, preferred_element_type=jnp.float32) * scale
    dv = lax.dot_general(p_low, do, over_rows, preferred_element_type=jnp.float32)
    grad_ref[:, 0] = dk.reshape(grad_ref.shape[0], -1, width)
    grad_ref[:, 1] = dv.reshape(grad_ref.shape[0], -1, width)


def attention_call(q, tiles, do, bias, heads_kv, scale):
    heads_kv, group, blocks, tokens, head_width = q.shape
    tile_count = tiles.shape[1]
    rows_width = group * head_width
    q_spec = pl.BlockSpec((None, group, None, tokens, head_width), lambda j, h: (h, 0, j, 0, 0))
    o_spec = pl.BlockSpec((None, tokens, rows_width), lambda j, h: (j, 0, h))
    o_shape = jax.ShapeDtypeStruct((blocks, tokens, heads_kv * rows_width), jnp.bfloat16)
    k_spec = pl.BlockSpec((None, tile_count, None, tokens, head_width), lambda j, h: (j, 0, 0, 0, h))
    v_spec = pl.BlockSpec((None, tile_count, None, tokens, head_width), lambda j, h: (j, 0, 1, 0, h))
    b_spec = pl.BlockSpec((None, 1, bias.shape[-1]), lambda j, h: (j, 0, 0))
    g_spec = pl.BlockSpec((None, tile_count, 2, tokens, head_width), lambda j, h: (j, 0, 0, 0, h))
    steps = blocks * heads_kv
    rows = tokens * (rows_width // head_width)
    keys_n = tile_count * tokens
    matmul = 2 * rows * keys_n * head_width * steps
    moved = 2 * (3 * q.size + 2 * tiles.size) + 4 * tiles.size
    out = pl.pallas_call(
        functools.partial(forward_kernel, scale=scale),
        cost_estimate=pl.CostEstimate(
            flops=2 * matmul, transcendentals=rows * keys_n * steps, bytes_accessed=moved
        ),
        grid=(blocks, heads_kv),
        in_specs=[q_spec, k_spec, v_spec, b_spec],
        out_specs=o_spec,
        out_shape=o_shape,
    )(q, tiles, tiles, bias)
    out, do = lax.optimization_barrier((out, do))
    grad_q, grads = pl.pallas_call(
        functools.partial(backward_kernel, scale=scale),
        cost_estimate=pl.CostEstimate(
            flops=5 * matmul, transcendentals=rows * keys_n * steps, bytes_accessed=moved
        ),
        grid=(blocks, heads_kv),
        in_specs=[q_spec, k_spec, v_spec, q_spec, o_spec, b_spec],
        out_specs=[o_spec, g_spec],
        out_shape=[
            o_shape,
            jax.ShapeDtypeStruct(tiles.shape, jnp.float32),
        ],
    )(q, tiles, tiles, do, out, bias)
    return out, grad_q, grads


def exchange(array, axis, split_axis, concat_axis):
    count = lax.axis_size(axis)
    own = lax.axis_index(axis)
    piece = array.shape[split_axis] // count
    received = []
    for shift in range(count):
        target = (own + shift) % count
        part = lax.dynamic_slice_in_dim(array, target * piece, piece, split_axis)
        if shift:
            pairs = [(i, (i + shift) % count) for i in range(count)]
            part = lax.ppermute(part, axis, pairs)
        received.append(part)
    order = (own - jnp.arange(count)) % count
    stacked = jnp.take(jnp.stack(received), order, axis=0)
    stacked = jnp.moveaxis(stacked, 0, concat_axis)
    shape = list(array.shape)
    shape[split_axis] = piece
    shape[concat_axis] *= count
    return stacked.reshape(shape)


def padded(shard, sides, width):
    for axis, dim in sides:
        count, length = (lax.axis_size(axis), shard.shape[dim])
        up = [(i, (i + 1) % count) for i in range(count - 1)]
        down = [(j, i) for i, j in up]
        last = lax.slice_in_dim(shard, length - width, length, axis=dim)
        leading = lax.slice_in_dim(shard, 0, width, axis=dim)
        before = lax.ppermute(last, axis, up)
        after = lax.ppermute(leading, axis, down)
        shard = jnp.concatenate([before, shard, after], axis=dim)
    return shard


def from_root(block, axis, owner):
    block = jnp.where(lax.axis_index(axis) == owner, block, jnp.zeros_like(block))
    return lax.psum(block, axis)


def tree_sum(part, axis):
    count = lax.axis_size(axis)
    if count & (count - 1):
        return lax.psum(part.astype(jnp.bfloat16), axis).astype(jnp.float32)
    stride = 1
    while stride < count:
        pairs = [(i, i ^ stride) for i in range(count)]
        other = lax.ppermute(part.astype(jnp.bfloat16), axis, pairs)
        part = part + other.astype(jnp.float32)
        stride *= 2
    return part


def per_device(queries, keys, values, output_gradient, global_blocks, random_blocks):
    query_loc, key_loc, value_loc, grad_loc = (
        lax.all_to_all(queries.transpose(1, 0, 2), "head", split_axis=0, concat_axis=1, tiled=True),
        None,
        None,
        output_gradient,
    )
    kv_loc = lax.all_to_all(
        jnp.stack([keys, values]), "head", split_axis=2, concat_axis=1, tiled=True
    )
    key_loc, value_loc = kv_loc[0], kv_loc[1]
    heads_q, shard_len, head_width = query_loc.shape
    heads_kv = key_loc.shape[1]
    heads_per_group = heads_q // heads_kv
    kv_width = heads_kv * head_width
    blocks = shard_len // BLOCK_TOKENS
    seq_count = lax.axis_size("seq")
    own_index = lax.axis_index("seq")
    block_total_count = seq_count * blocks
    capacity = (3 * blocks + seq_count - 2) // (seq_count - 1)
    entry_count = 3 * blocks
    score_scale = 1.0 / math.sqrt(head_width)
    kv_pair = kv_loc.reshape(2, shard_len, kv_width)
    extended = padded(kv_pair, (("seq", 1),), BLOCK_TOKENS)
    kv_tiles = kv_pair.reshape(2, blocks, BLOCK_TOKENS, kv_width).transpose(1, 0, 2, 3)
    global_owner = global_blocks // blocks
    global_offset = global_blocks % blocks
    own_global = (jnp.arange(blocks)[None, :] == global_offset[:, None]) & (
        global_owner == own_index
    )[:, None]
    all_entries = (
        random_blocks.reshape(seq_count, blocks, 3)
        .transpose(0, 2, 1)
        .reshape(seq_count, entry_count)
    )
    all_owner = all_entries // blocks
    entry_ids = jnp.arange(entry_count)
    entry_earlier = entry_ids[None, :] < entry_ids[:, None]
    all_rank = jnp.sum(
        (all_owner[:, :, None] == all_owner[:, None, :]) & entry_earlier[None], axis=2
    )
    my_entries = lax.dynamic_index_in_dim(all_entries, own_index, 0, keepdims=False)
    my_owner = lax.dynamic_index_in_dim(all_owner, own_index, 0, keepdims=False)
    my_rank = lax.dynamic_index_in_dim(all_rank, own_index, 0, keepdims=False)
    my_slot = my_owner * capacity + my_rank
    owned_here = (all_owner == own_index)[:, :, None] & (
        all_rank[:, :, None] == jnp.arange(capacity)[None, None, :]
    )
    offset_match = (all_entries % blocks)[:, :, None] == jnp.arange(blocks)[None, None, :]
    selector = jnp.einsum(
        "tec,teo->tco",
        owned_here.astype(jnp.bfloat16),
        offset_match.astype(jnp.bfloat16),
        preferred_element_type=jnp.float32,
    ).astype(jnp.bfloat16)
    everything = lax.all_gather(kv_pair, "seq", axis=1, tiled=True)
    grad_loc = grad_loc.transpose(1, 0, 2)
    query_loc, everything, grad_loc = lax.optimization_barrier((query_loc, everything, grad_loc))
    grad_loc = lax.all_to_all(grad_loc, "head", split_axis=0, concat_axis=1, tiled=True)
    tiled_all = everything.reshape(2, block_total_count, BLOCK_TOKENS, kv_width)
    random_tiles = jnp.take(tiled_all, my_entries, axis=1).transpose(1, 0, 2, 3)
    global_tiles = jnp.take(tiled_all, global_blocks, axis=1).transpose(1, 0, 2, 3)
    random_by_block = random_tiles.reshape(3, blocks, 2, BLOCK_TOKENS, kv_width).transpose(
        1, 0, 2, 3, 4
    )
    block_ids = own_index * blocks + jnp.arange(blocks)
    listed = jnp.concatenate(
        [
            jnp.stack([block_ids - 1, block_ids, block_ids + 1], axis=1),
            jnp.broadcast_to(global_blocks[None, :], (blocks, 2)),
            my_entries.reshape(3, blocks).T,
        ],
        axis=1,
    )
    inside = (listed >= 0) & (listed < block_total_count)
    tile_ids = jnp.arange(8)
    tile_earlier = tile_ids[None, :] < tile_ids[:, None]
    repeat = jnp.any((listed[:, :, None] == listed[:, None, :]) & tile_earlier[None], axis=2)
    live = inside & jnp.logical_not(repeat)

    tiles_per_block = []
    for position in range(blocks):
        near_tiles = lax.slice_in_dim(
            extended, position * BLOCK_TOKENS, (position + 3) * BLOCK_TOKENS, axis=1
        )
        near_tiles = near_tiles.reshape(2, 3, BLOCK_TOKENS, kv_width).transpose(1, 0, 2, 3)
        tiles_per_block.append(
            jnp.concatenate([near_tiles, global_tiles, random_by_block[position]], axis=0)
        )
    all_tiles = jnp.stack(tiles_per_block)
    tile_count = all_tiles.shape[1]
    bias = jnp.where(live, 0.0, -jnp.inf).astype(jnp.float32)
    bias = jnp.repeat(bias, BLOCK_TOKENS, axis=1).reshape(blocks, 1, tile_count * BLOCK_TOKENS)
    out_q, grad_q, tile_grads = attention_call(
        query_loc.reshape(heads_kv, heads_per_group, blocks, BLOCK_TOKENS, head_width),
        all_tiles,
        grad_loc.reshape(heads_kv, heads_per_group, blocks, BLOCK_TOKENS, head_width),
        bias,
        heads_kv,
        score_scale,
    )
    pad_spec_low = ((0, 2), (0, 0), (0, 0), (0, 0))
    pad_spec_mid = ((1, 1), (0, 0), (0, 0), (0, 0))
    pad_spec_high = ((2, 0), (0, 0), (0, 0), (0, 0))
    window_sum = (
        jnp.pad(tile_grads[:, 0], pad_spec_low)
        + jnp.pad(tile_grads[:, 1], pad_spec_mid)
        + jnp.pad(tile_grads[:, 2], pad_spec_high)
    )
    rims = jnp.concatenate([window_sum[0], window_sum[blocks + 1]], axis=1)
    returned_rims = padded(rims.astype(jnp.bfloat16), (("seq", 1),), BLOCK_TOKENS).astype(
        rims.dtype
    )
    interior = window_sum[1 : blocks + 1]
    interior = (
        interior.at[0]
        .add(returned_rims[:, :BLOCK_TOKENS])
        .at[blocks - 1]
        .add(returned_rims[:, 3 * BLOCK_TOKENS :])
    )
    global_terms = jnp.sum(tile_grads[:, 3:5], axis=0)
    global_total = tree_sum(global_terms, "seq")
    own_weight = own_global.astype(jnp.float32)[:, :, None, None, None]
    interior = interior + jnp.sum(own_weight * global_total[:, None], axis=0)
    random_terms = (
        tile_grads[:, 5:8]
        .transpose(1, 0, 2, 3, 4)
        .reshape(entry_count, 2, BLOCK_TOKENS, kv_width)
        .astype(jnp.bfloat16)
    )
    slot_onehot = (my_slot[:, None] == jnp.arange(seq_count * capacity)[None, :]).astype(
        jnp.bfloat16
    )
    back_buffer = jnp.einsum(
        "es,exbw->sxbw", slot_onehot, random_terms, preferred_element_type=jnp.float32
    ).astype(jnp.bfloat16)
    returned_terms = exchange(back_buffer, "seq", 0, 0)
    interior = interior + jnp.einsum(
        "tco,tcxbw->oxbw",
        selector,
        returned_terms.reshape(seq_count, capacity, 2, BLOCK_TOKENS, kv_width),
        preferred_element_type=jnp.float32,
    )
    kv_grad = interior.transpose(1, 0, 2, 3).reshape(2, shard_len, kv_width).astype(jnp.bfloat16)
    out_all = out_q
    query_grad_all = grad_q
    key_grad_all = kv_grad[0].reshape(shard_len, heads_kv, head_width)
    value_grad_all = kv_grad[1].reshape(shard_len, heads_kv, head_width)
    out_back = lax.all_to_all(out_all, "head", split_axis=0, concat_axis=2, tiled=True)
    query_back = lax.all_to_all(query_grad_all, "head", split_axis=0, concat_axis=2, tiled=True)
    kv_blocks = interior.astype(jnp.bfloat16).reshape(
        blocks, 2, BLOCK_TOKENS, heads_kv, head_width
    )
    (out_back, query_back), kv_blocks = lax.optimization_barrier(((out_back, query_back), kv_blocks))
    kv_back = lax.all_to_all(kv_blocks, "head", split_axis=0, concat_axis=3, tiled=True)[0]
    out_back = out_back.reshape(BLOCK_TOKENS, -1, head_width)
    query_back = query_back.reshape(BLOCK_TOKENS, -1, head_width)
    return (out_back, query_back, kv_back[0], kv_back[1])


def solution(mesh):
    placed = (
        P(("seq", "head"), None, None),
        P(("seq", "head"), None, None),
        P(("seq", "head"), None, None),
        P(("seq", "head"), None, None),
        P(),
        P(),
    )
    return jax.shard_map(
        per_device,
        mesh=mesh,
        in_specs=placed,
        out_specs=(
            P(("seq", "head"), None, None),
            P(("seq", "head"), None, None),
            P(("seq", "head"), None, None),
            P(("seq", "head"), None, None),
        ),
        check_vma=False,
    )
```

```python
import functools
import math

import jax
import jax.numpy as jnp
from jax import lax
from jax.experimental import pallas as pl
from jax.sharding import PartitionSpec as P

BLOCK_TOKENS = 128


def rows_of(ref, group, width):
    return jnp.concatenate([ref[:, g * width:(g + 1) * width] for g in range(group)], axis=0)


def store_rows(ref, value, group, width):
    tokens = ref.shape[0]
    for g in range(group):
        ref[:, g * width:(g + 1) * width] = value[g * tokens:(g + 1) * tokens, :]


def scores_of(q, k, bias, scale):
    rows_by_cols = (((1,), (1,)), ((), ()))
    s = lax.dot_general(q, k, rows_by_cols, preferred_element_type=jnp.float32) * scale
    return s + bias


def forward_kernel(q_ref, k_ref, v_ref, bias_ref, out_ref, max_ref, sum_ref, *, scale):
    width = k_ref.shape[-1]
    q = q_ref[...].reshape(-1, width)
    k = k_ref[...].reshape(-1, width)
    v = v_ref[...].reshape(-1, width)
    s = scores_of(q, k, bias_ref[...], scale)
    row_max = jnp.max(s, axis=1, keepdims=True)
    e = jnp.exp(s - row_max)
    row_sum = jnp.sum(e, axis=1, keepdims=True)
    max_ref[...] = row_max
    sum_ref[...] = row_sum
    p_low = (e / row_sum).astype(jnp.bfloat16)
    o_low = jnp.dot(p_low, v, preferred_element_type=jnp.float32).astype(jnp.bfloat16)
    out_ref[...] = o_low.reshape(out_ref.shape)


def backward_kernel(
    q_ref, k_ref, v_ref, do_ref, o_ref, bias_ref, max_ref, sum_ref, dq_ref, grad_ref, *, scale
):
    width = k_ref.shape[-1]
    q = q_ref[...].reshape(-1, width)
    do = do_ref[...].reshape(-1, width)
    o_low = o_ref[...].reshape(-1, width)
    k = k_ref[...].reshape(-1, width)
    v = v_ref[...].reshape(-1, width)
    rows_by_cols = (((1,), (1,)), ((), ()))
    over_rows = (((0,), (0,)), ((), ()))
    p = jnp.exp(scores_of(q, k, bias_ref[...], scale) - max_ref[...]) / sum_ref[...]
    p_low = p.astype(jnp.bfloat16)
    delta = jnp.sum(do.astype(jnp.float32) * o_low.astype(jnp.float32), axis=1, keepdims=True)
    dp = lax.dot_general(do, v, rows_by_cols, preferred_element_type=jnp.float32)
    ds_low = (p * (dp - delta)).astype(jnp.bfloat16)
    dq = jnp.dot(ds_low, k, preferred_element_type=jnp.float32) * scale
    dq_ref[...] = dq.astype(jnp.bfloat16).reshape(dq_ref.shape)
    dk = lax.dot_general(ds_low, q, over_rows, preferred_element_type=jnp.float32) * scale
    dv = lax.dot_general(p_low, do, over_rows, preferred_element_type=jnp.float32)
    grad_ref[:, 0] = dk.reshape(grad_ref.shape[0], -1, width)
    grad_ref[:, 1] = dv.reshape(grad_ref.shape[0], -1, width)


def attention_call(q, tiles, do, bias, heads_kv, scale):
    heads_kv, group, blocks, tokens, head_width = q.shape
    tile_count = tiles.shape[1]
    rows_width = group * head_width
    q_spec = pl.BlockSpec((None, group, None, tokens, head_width), lambda j, h: (h, 0, j, 0, 0))
    o_spec = pl.BlockSpec((None, None, group, tokens, head_width), lambda j, h: (j, h, 0, 0, 0))
    r_spec = pl.BlockSpec((None, None, group * tokens, 1), lambda j, h: (j, h, 0, 0))
    r_shape = jax.ShapeDtypeStruct((blocks, heads_kv, group * tokens, 1), jnp.float32)
    o_shape = jax.ShapeDtypeStruct((blocks, heads_kv, group, tokens, head_width), jnp.bfloat16)
    k_spec = pl.BlockSpec((None, tile_count, None, tokens, head_width), lambda j, h: (j, 0, 0, 0, h))
    v_spec = pl.BlockSpec((None, tile_count, None, tokens, head_width), lambda j, h: (j, 0, 1, 0, h))
    b_spec = pl.BlockSpec((None, 1, bias.shape[-1]), lambda j, h: (j, 0, 0))
    g_spec = pl.BlockSpec((None, tile_count, 2, tokens, head_width), lambda j, h: (j, 0, 0, 0, h))
    steps = blocks * heads_kv
    rows = tokens * (rows_width // head_width)
    keys_n = tile_count * tokens
    matmul = 2 * rows * keys_n * head_width * steps
    moved = 2 * (3 * q.size + 2 * tiles.size) + 4 * tiles.size
    out = pl.pallas_call(
        functools.partial(forward_kernel, scale=scale),
        cost_estimate=pl.CostEstimate(
            flops=2 * matmul, transcendentals=rows * keys_n * steps, bytes_accessed=moved
        ),
        grid=(blocks, heads_kv),
        in_specs=[q_spec, k_spec, v_spec, b_spec],
        out_specs=[o_spec, r_spec, r_spec],
        out_shape=[o_shape, r_shape, r_shape],
    )(q, tiles, tiles, bias)
    out, row_max, row_sum = out
    out, do = lax.optimization_barrier((out, do))
    grad_q, grads = pl.pallas_call(
        functools.partial(backward_kernel, scale=scale),
        cost_estimate=pl.CostEstimate(
            flops=5 * matmul, transcendentals=rows * keys_n * steps, bytes_accessed=moved
        ),
        grid=(blocks, heads_kv),
        in_specs=[q_spec, k_spec, v_spec, q_spec, o_spec, b_spec, r_spec, r_spec],
        out_specs=[o_spec, g_spec],
        out_shape=[
            o_shape,
            jax.ShapeDtypeStruct(tiles.shape, jnp.float32),
        ],
    )(q, tiles, tiles, do, out, bias, row_max, row_sum)
    return out, grad_q, grads


def exchange(array, axis, split_axis, concat_axis):
    count = lax.axis_size(axis)
    own = lax.axis_index(axis)
    piece = array.shape[split_axis] // count
    received = []
    for shift in range(count):
        target = (own + shift) % count
        part = lax.dynamic_slice_in_dim(array, target * piece, piece, split_axis)
        if shift:
            pairs = [(i, (i + shift) % count) for i in range(count)]
            part = lax.ppermute(part, axis, pairs)
        received.append(part)
    order = (own - jnp.arange(count)) % count
    stacked = jnp.take(jnp.stack(received), order, axis=0)
    stacked = jnp.moveaxis(stacked, 0, concat_axis)
    shape = list(array.shape)
    shape[split_axis] = piece
    shape[concat_axis] *= count
    return stacked.reshape(shape)


def padded(shard, sides, width):
    for axis, dim in sides:
        count, length = (lax.axis_size(axis), shard.shape[dim])
        up = [(i, (i + 1) % count) for i in range(count - 1)]
        down = [(j, i) for i, j in up]
        last = lax.slice_in_dim(shard, length - width, length, axis=dim)
        leading = lax.slice_in_dim(shard, 0, width, axis=dim)
        before = lax.ppermute(last, axis, up)
        after = lax.ppermute(leading, axis, down)
        shard = jnp.concatenate([before, shard, after], axis=dim)
    return shard


def from_root(block, axis, owner):
    block = jnp.where(lax.axis_index(axis) == owner, block, jnp.zeros_like(block))
    return lax.psum(block, axis)


def tree_sum(part, axis):
    count = lax.axis_size(axis)
    if count & (count - 1):
        return lax.psum(part.astype(jnp.bfloat16), axis).astype(jnp.float32)
    stride = 1
    while stride < count:
        pairs = [(i, i ^ stride) for i in range(count)]
        other = lax.ppermute(part.astype(jnp.bfloat16), axis, pairs)
        part = part + other.astype(jnp.float32)
        stride *= 2
    return part


def per_device(queries, keys, values, output_gradient, global_blocks, random_blocks):
    query_loc, key_loc, value_loc, grad_loc = (
        lax.all_to_all(queries.transpose(1, 0, 2), "head", split_axis=0, concat_axis=1, tiled=True),
        None,
        None,
        output_gradient,
    )
    kv_loc = lax.all_to_all(
        jnp.stack([keys, values]), "head", split_axis=2, concat_axis=1, tiled=True
    )
    key_loc, value_loc = kv_loc[0], kv_loc[1]
    heads_q, shard_len, head_width = query_loc.shape
    heads_kv = key_loc.shape[1]
    heads_per_group = heads_q // heads_kv
    kv_width = heads_kv * head_width
    blocks = shard_len // BLOCK_TOKENS
    seq_count = lax.axis_size("seq")
    own_index = lax.axis_index("seq")
    block_total_count = seq_count * blocks
    capacity = (3 * blocks + seq_count - 2) // (seq_count - 1)
    entry_count = 3 * blocks
    score_scale = 1.0 / math.sqrt(head_width)
    kv_pair = kv_loc.reshape(2, shard_len, kv_width)
    extended = padded(kv_pair, (("seq", 1),), BLOCK_TOKENS)
    kv_tiles = kv_pair.reshape(2, blocks, BLOCK_TOKENS, kv_width).transpose(1, 0, 2, 3)
    global_owner = global_blocks // blocks
    global_offset = global_blocks % blocks
    own_global = (jnp.arange(blocks)[None, :] == global_offset[:, None]) & (
        global_owner == own_index
    )[:, None]
    all_entries = (
        random_blocks.reshape(seq_count, blocks, 3)
        .transpose(0, 2, 1)
        .reshape(seq_count, entry_count)
    )
    all_owner = all_entries // blocks
    entry_ids = jnp.arange(entry_count)
    entry_earlier = entry_ids[None, :] < entry_ids[:, None]
    all_rank = jnp.sum(
        (all_owner[:, :, None] == all_owner[:, None, :]) & entry_earlier[None], axis=2
    )
    my_entries = lax.dynamic_index_in_dim(all_entries, own_index, 0, keepdims=False)
    my_owner = lax.dynamic_index_in_dim(all_owner, own_index, 0, keepdims=False)
    my_rank = lax.dynamic_index_in_dim(all_rank, own_index, 0, keepdims=False)
    my_slot = my_owner * capacity + my_rank
    owned_here = (all_owner == own_index)[:, :, None] & (
        all_rank[:, :, None] == jnp.arange(capacity)[None, None, :]
    )
    offset_match = (all_entries % blocks)[:, :, None] == jnp.arange(blocks)[None, None, :]
    selector = jnp.einsum(
        "tec,teo->tco",
        owned_here.astype(jnp.bfloat16),
        offset_match.astype(jnp.bfloat16),
        preferred_element_type=jnp.float32,
    ).astype(jnp.bfloat16)
    everything = lax.all_gather(kv_pair, "seq", axis=1, tiled=True)
    grad_loc = grad_loc.transpose(1, 0, 2)
    query_loc, everything, grad_loc = lax.optimization_barrier((query_loc, everything, grad_loc))
    grad_loc = lax.all_to_all(grad_loc, "head", split_axis=0, concat_axis=1, tiled=True)
    tiled_all = everything.reshape(2, block_total_count, BLOCK_TOKENS, kv_width)
    random_tiles = jnp.take(tiled_all, my_entries, axis=1).transpose(1, 0, 2, 3)
    global_tiles = jnp.take(tiled_all, global_blocks, axis=1).transpose(1, 0, 2, 3)
    random_by_block = random_tiles.reshape(3, blocks, 2, BLOCK_TOKENS, kv_width).transpose(
        1, 0, 2, 3, 4
    )
    block_ids = own_index * blocks + jnp.arange(blocks)
    listed = jnp.concatenate(
        [
            jnp.stack([block_ids - 1, block_ids, block_ids + 1], axis=1),
            jnp.broadcast_to(global_blocks[None, :], (blocks, 2)),
            my_entries.reshape(3, blocks).T,
        ],
        axis=1,
    )
    inside = (listed >= 0) & (listed < block_total_count)
    tile_ids = jnp.arange(8)
    tile_earlier = tile_ids[None, :] < tile_ids[:, None]
    repeat = jnp.any((listed[:, :, None] == listed[:, None, :]) & tile_earlier[None], axis=2)
    live = inside & jnp.logical_not(repeat)

    tiles_per_block = []
    for position in range(blocks):
        near_tiles = lax.slice_in_dim(
            extended, position * BLOCK_TOKENS, (position + 3) * BLOCK_TOKENS, axis=1
        )
        near_tiles = near_tiles.reshape(2, 3, BLOCK_TOKENS, kv_width).transpose(1, 0, 2, 3)
        tiles_per_block.append(
            jnp.concatenate([near_tiles, global_tiles, random_by_block[position]], axis=0)
        )
    all_tiles = jnp.stack(tiles_per_block)
    tile_count = all_tiles.shape[1]
    bias = jnp.where(live, 0.0, -jnp.inf).astype(jnp.float32)
    bias = jnp.repeat(bias, BLOCK_TOKENS, axis=1).reshape(blocks, 1, tile_count * BLOCK_TOKENS)
    out_q, grad_q, tile_grads = attention_call(
        query_loc.reshape(heads_kv, heads_per_group, blocks, BLOCK_TOKENS, head_width),
        all_tiles,
        grad_loc.reshape(heads_kv, heads_per_group, blocks, BLOCK_TOKENS, head_width),
        bias,
        heads_kv,
        score_scale,
    )
    pad_spec_low = ((0, 2), (0, 0), (0, 0), (0, 0))
    pad_spec_mid = ((1, 1), (0, 0), (0, 0), (0, 0))
    pad_spec_high = ((2, 0), (0, 0), (0, 0), (0, 0))
    window_sum = (
        jnp.pad(tile_grads[:, 0], pad_spec_low)
        + jnp.pad(tile_grads[:, 1], pad_spec_mid)
        + jnp.pad(tile_grads[:, 2], pad_spec_high)
    )
    rims = jnp.concatenate([window_sum[0], window_sum[blocks + 1]], axis=1)
    returned_rims = padded(rims.astype(jnp.bfloat16), (("seq", 1),), BLOCK_TOKENS).astype(
        rims.dtype
    )
    interior = window_sum[1 : blocks + 1]
    interior = (
        interior.at[0]
        .add(returned_rims[:, :BLOCK_TOKENS])
        .at[blocks - 1]
        .add(returned_rims[:, 3 * BLOCK_TOKENS :])
    )
    global_terms = jnp.sum(tile_grads[:, 3:5], axis=0)
    global_total = tree_sum(global_terms, "seq")
    own_weight = own_global.astype(jnp.float32)[:, :, None, None, None]
    interior = interior + jnp.sum(own_weight * global_total[:, None], axis=0)
    random_terms = (
        tile_grads[:, 5:8]
        .transpose(1, 0, 2, 3, 4)
        .reshape(entry_count, 2, BLOCK_TOKENS, kv_width)
        .astype(jnp.bfloat16)
    )
    slot_onehot = (my_slot[:, None] == jnp.arange(seq_count * capacity)[None, :]).astype(
        jnp.bfloat16
    )
    back_buffer = jnp.einsum(
        "es,exbw->sxbw", slot_onehot, random_terms, preferred_element_type=jnp.float32
    ).astype(jnp.bfloat16)
    returned_terms = exchange(back_buffer, "seq", 0, 0)
    interior = interior + jnp.einsum(
        "tco,tcxbw->oxbw",
        selector,
        returned_terms.reshape(seq_count, capacity, 2, BLOCK_TOKENS, kv_width),
        preferred_element_type=jnp.float32,
    )
    kv_grad = interior.transpose(1, 0, 2, 3).reshape(2, shard_len, kv_width).astype(jnp.bfloat16)
    out_all = out_q.reshape(blocks, heads_q, BLOCK_TOKENS, head_width)
    query_grad_all = grad_q.reshape(blocks, heads_q, BLOCK_TOKENS, head_width)
    key_grad_all = kv_grad[0].reshape(shard_len, heads_kv, head_width)
    value_grad_all = kv_grad[1].reshape(shard_len, heads_kv, head_width)
    out_back = lax.all_to_all(out_all, "head", split_axis=0, concat_axis=1, tiled=True)
    query_back = lax.all_to_all(query_grad_all, "head", split_axis=0, concat_axis=1, tiled=True)
    kv_blocks = interior.astype(jnp.bfloat16).reshape(
        blocks, 2, BLOCK_TOKENS, heads_kv, head_width
    )
    (out_back, query_back), kv_blocks = lax.optimization_barrier(((out_back, query_back), kv_blocks))
    kv_back = lax.all_to_all(kv_blocks, "head", split_axis=0, concat_axis=3, tiled=True)[0]
    out_back = out_back.reshape(-1, BLOCK_TOKENS, head_width).transpose(1, 0, 2)
    query_back = query_back.reshape(-1, BLOCK_TOKENS, head_width).transpose(1, 0, 2)
    return (out_back, query_back, kv_back[0], kv_back[1])


def solution(mesh):
    placed = (
        P(("seq", "head"), None, None),
        P(("seq", "head"), None, None),
        P(("seq", "head"), None, None),
        P(("seq", "head"), None, None),
        P(),
        P(),
    )
    return jax.shard_map(
        per_device,
        mesh=mesh,
        in_specs=placed,
        out_specs=(
            P(("seq", "head"), None, None),
            P(("seq", "head"), None, None),
            P(("seq", "head"), None, None),
            P(("seq", "head"), None, None),
        ),
        check_vma=False,
    )
```

```python
import functools
import math

import jax
import jax.numpy as jnp
from jax import lax
from jax.experimental import pallas as pl
from jax.sharding import PartitionSpec as P

BLOCK_TOKENS = 128


def rows_of(ref, group, width):
    return jnp.concatenate([ref[:, g * width:(g + 1) * width] for g in range(group)], axis=0)


def store_rows(ref, value, group, width):
    tokens = ref.shape[0]
    for g in range(group):
        ref[:, g * width:(g + 1) * width] = value[g * tokens:(g + 1) * tokens, :]


def scores_of(q, k, bias, scale):
    rows_by_cols = (((1,), (1,)), ((), ()))
    s = lax.dot_general(q, k, rows_by_cols, preferred_element_type=jnp.float32) * scale
    return s + bias


def forward_kernel(q_ref, k_ref, v_ref, bias_ref, out_ref, max_ref, sum_ref, *, scale):
    width = k_ref.shape[-1]
    q = q_ref[...].reshape(-1, width)
    k = k_ref[...].reshape(-1, width)
    v = v_ref[...].reshape(-1, width)
    s = scores_of(q, k, bias_ref[...], scale)
    row_max = jnp.max(s, axis=1, keepdims=True)
    e = jnp.exp(s - row_max)
    row_sum = jnp.sum(e, axis=1, keepdims=True)
    max_ref[...] = row_max
    sum_ref[...] = row_sum
    p_low = (e * (1.0 / row_sum)).astype(jnp.bfloat16)
    o_low = jnp.dot(p_low, v, preferred_element_type=jnp.float32).astype(jnp.bfloat16)
    out_ref[...] = o_low.reshape(out_ref.shape)


def backward_kernel(
    q_ref, k_ref, v_ref, do_ref, o_ref, bias_ref, max_ref, sum_ref, dq_ref, grad_ref, *, scale
):
    width = k_ref.shape[-1]
    q = q_ref[...].reshape(-1, width)
    do = do_ref[...].reshape(-1, width)
    o_low = o_ref[...].reshape(-1, width)
    k = k_ref[...].reshape(-1, width)
    v = v_ref[...].reshape(-1, width)
    rows_by_cols = (((1,), (1,)), ((), ()))
    over_rows = (((0,), (0,)), ((), ()))
    p = jnp.exp(scores_of(q, k, bias_ref[...], scale) - max_ref[...]) * (1.0 / sum_ref[...])
    p_low = p.astype(jnp.bfloat16)
    delta = jnp.sum(do.astype(jnp.float32) * o_low.astype(jnp.float32), axis=1, keepdims=True)
    dp = lax.dot_general(do, v, rows_by_cols, preferred_element_type=jnp.float32)
    ds_low = (p * (dp - delta)).astype(jnp.bfloat16)
    dq = jnp.dot(ds_low, k, preferred_element_type=jnp.float32) * scale
    dq_ref[...] = dq.astype(jnp.bfloat16).reshape(dq_ref.shape)
    dk = lax.dot_general(ds_low, q, over_rows, preferred_element_type=jnp.float32) * scale
    dv = lax.dot_general(p_low, do, over_rows, preferred_element_type=jnp.float32)
    grad_ref[:, 0] = dk.reshape(grad_ref.shape[0], -1, width)
    grad_ref[:, 1] = dv.reshape(grad_ref.shape[0], -1, width)


def attention_call(q, tiles, do, bias, heads_kv, scale):
    heads_kv, group, blocks, tokens, head_width = q.shape
    tile_count = tiles.shape[1]
    rows_width = group * head_width
    q_spec = pl.BlockSpec((None, group, None, tokens, head_width), lambda j, h: (h, 0, j, 0, 0))
    o_spec = pl.BlockSpec((None, None, group, tokens, head_width), lambda j, h: (j, h, 0, 0, 0))
    r_spec = pl.BlockSpec((None, None, group * tokens, 1), lambda j, h: (j, h, 0, 0))
    r_shape = jax.ShapeDtypeStruct((blocks, heads_kv, group * tokens, 1), jnp.float32)
    o_shape = jax.ShapeDtypeStruct((blocks, heads_kv, group, tokens, head_width), jnp.bfloat16)
    k_spec = pl.BlockSpec((None, tile_count, None, tokens, head_width), lambda j, h: (j, 0, 0, 0, h))
    v_spec = pl.BlockSpec((None, tile_count, None, tokens, head_width), lambda j, h: (j, 0, 1, 0, h))
    b_spec = pl.BlockSpec((None, 1, bias.shape[-1]), lambda j, h: (j, 0, 0))
    g_spec = pl.BlockSpec((None, tile_count, 2, tokens, head_width), lambda j, h: (j, 0, 0, 0, h))
    steps = blocks * heads_kv
    rows = tokens * (rows_width // head_width)
    keys_n = tile_count * tokens
    matmul = 2 * rows * keys_n * head_width * steps
    moved = 2 * (3 * q.size + 2 * tiles.size) + 4 * tiles.size
    out = pl.pallas_call(
        functools.partial(forward_kernel, scale=scale),
        cost_estimate=pl.CostEstimate(
            flops=2 * matmul, transcendentals=rows * keys_n * steps, bytes_accessed=moved
        ),
        grid=(blocks, heads_kv),
        in_specs=[q_spec, k_spec, v_spec, b_spec],
        out_specs=[o_spec, r_spec, r_spec],
        out_shape=[o_shape, r_shape, r_shape],
    )(q, tiles, tiles, bias)
    out, row_max, row_sum = out
    out, do = lax.optimization_barrier((out, do))
    grad_q, grads = pl.pallas_call(
        functools.partial(backward_kernel, scale=scale),
        cost_estimate=pl.CostEstimate(
            flops=5 * matmul, transcendentals=rows * keys_n * steps, bytes_accessed=moved
        ),
        grid=(blocks, heads_kv),
        in_specs=[q_spec, k_spec, v_spec, q_spec, o_spec, b_spec, r_spec, r_spec],
        out_specs=[o_spec, g_spec],
        out_shape=[
            o_shape,
            jax.ShapeDtypeStruct(tiles.shape, jnp.float32),
        ],
    )(q, tiles, tiles, do, out, bias, row_max, row_sum)
    return out, grad_q, grads


def exchange(array, axis, split_axis, concat_axis):
    count = lax.axis_size(axis)
    own = lax.axis_index(axis)
    piece = array.shape[split_axis] // count
    received = []
    for shift in range(count):
        target = (own + shift) % count
        part = lax.dynamic_slice_in_dim(array, target * piece, piece, split_axis)
        if shift:
            pairs = [(i, (i + shift) % count) for i in range(count)]
            part = lax.ppermute(part, axis, pairs)
        received.append(part)
    order = (own - jnp.arange(count)) % count
    stacked = jnp.take(jnp.stack(received), order, axis=0)
    stacked = jnp.moveaxis(stacked, 0, concat_axis)
    shape = list(array.shape)
    shape[split_axis] = piece
    shape[concat_axis] *= count
    return stacked.reshape(shape)


def padded(shard, sides, width):
    for axis, dim in sides:
        count, length = (lax.axis_size(axis), shard.shape[dim])
        up = [(i, (i + 1) % count) for i in range(count - 1)]
        down = [(j, i) for i, j in up]
        last = lax.slice_in_dim(shard, length - width, length, axis=dim)
        leading = lax.slice_in_dim(shard, 0, width, axis=dim)
        before = lax.ppermute(last, axis, up)
        after = lax.ppermute(leading, axis, down)
        shard = jnp.concatenate([before, shard, after], axis=dim)
    return shard


def from_root(block, axis, owner):
    block = jnp.where(lax.axis_index(axis) == owner, block, jnp.zeros_like(block))
    return lax.psum(block, axis)


def tree_sum(part, axis):
    count = lax.axis_size(axis)
    if count & (count - 1):
        return lax.psum(part.astype(jnp.bfloat16), axis).astype(jnp.float32)
    stride = 1
    while stride < count:
        pairs = [(i, i ^ stride) for i in range(count)]
        other = lax.ppermute(part.astype(jnp.bfloat16), axis, pairs)
        part = part + other.astype(jnp.float32)
        stride *= 2
    return part


def per_device(queries, keys, values, output_gradient, global_blocks, random_blocks):
    query_loc, key_loc, value_loc, grad_loc = (
        lax.all_to_all(queries.transpose(1, 0, 2), "head", split_axis=0, concat_axis=1, tiled=True),
        None,
        None,
        output_gradient,
    )
    kv_loc = lax.all_to_all(
        jnp.stack([keys, values]), "head", split_axis=2, concat_axis=1, tiled=True
    )
    key_loc, value_loc = kv_loc[0], kv_loc[1]
    heads_q, shard_len, head_width = query_loc.shape
    heads_kv = key_loc.shape[1]
    heads_per_group = heads_q // heads_kv
    kv_width = heads_kv * head_width
    blocks = shard_len // BLOCK_TOKENS
    seq_count = lax.axis_size("seq")
    own_index = lax.axis_index("seq")
    block_total_count = seq_count * blocks
    capacity = (3 * blocks + seq_count - 2) // (seq_count - 1)
    entry_count = 3 * blocks
    score_scale = 1.0 / math.sqrt(head_width)
    kv_pair = kv_loc.reshape(2, shard_len, kv_width)
    extended = padded(kv_pair, (("seq", 1),), BLOCK_TOKENS)
    kv_tiles = kv_pair.reshape(2, blocks, BLOCK_TOKENS, kv_width).transpose(1, 0, 2, 3)
    global_owner = global_blocks // blocks
    global_offset = global_blocks % blocks
    own_global = (jnp.arange(blocks)[None, :] == global_offset[:, None]) & (
        global_owner == own_index
    )[:, None]
    all_entries = (
        random_blocks.reshape(seq_count, blocks, 3)
        .transpose(0, 2, 1)
        .reshape(seq_count, entry_count)
    )
    all_owner = all_entries // blocks
    entry_ids = jnp.arange(entry_count)
    entry_earlier = entry_ids[None, :] < entry_ids[:, None]
    all_rank = jnp.sum(
        (all_owner[:, :, None] == all_owner[:, None, :]) & entry_earlier[None], axis=2
    )
    my_entries = lax.dynamic_index_in_dim(all_entries, own_index, 0, keepdims=False)
    my_owner = lax.dynamic_index_in_dim(all_owner, own_index, 0, keepdims=False)
    my_rank = lax.dynamic_index_in_dim(all_rank, own_index, 0, keepdims=False)
    my_slot = my_owner * capacity + my_rank
    owned_here = (all_owner == own_index)[:, :, None] & (
        all_rank[:, :, None] == jnp.arange(capacity)[None, None, :]
    )
    offset_match = (all_entries % blocks)[:, :, None] == jnp.arange(blocks)[None, None, :]
    selector = jnp.einsum(
        "tec,teo->tco",
        owned_here.astype(jnp.bfloat16),
        offset_match.astype(jnp.bfloat16),
        preferred_element_type=jnp.float32,
    ).astype(jnp.bfloat16)
    everything = lax.all_gather(kv_pair, "seq", axis=1, tiled=True)
    grad_loc = grad_loc.transpose(1, 0, 2)
    query_loc, everything, grad_loc = lax.optimization_barrier((query_loc, everything, grad_loc))
    grad_loc = lax.all_to_all(grad_loc, "head", split_axis=0, concat_axis=1, tiled=True)
    tiled_all = everything.reshape(2, block_total_count, BLOCK_TOKENS, kv_width)
    random_tiles = jnp.take(tiled_all, my_entries, axis=1).transpose(1, 0, 2, 3)
    global_tiles = jnp.take(tiled_all, global_blocks, axis=1).transpose(1, 0, 2, 3)
    random_by_block = random_tiles.reshape(3, blocks, 2, BLOCK_TOKENS, kv_width).transpose(
        1, 0, 2, 3, 4
    )
    block_ids = own_index * blocks + jnp.arange(blocks)
    listed = jnp.concatenate(
        [
            jnp.stack([block_ids - 1, block_ids, block_ids + 1], axis=1),
            jnp.broadcast_to(global_blocks[None, :], (blocks, 2)),
            my_entries.reshape(3, blocks).T,
        ],
        axis=1,
    )
    inside = (listed >= 0) & (listed < block_total_count)
    tile_ids = jnp.arange(8)
    tile_earlier = tile_ids[None, :] < tile_ids[:, None]
    repeat = jnp.any((listed[:, :, None] == listed[:, None, :]) & tile_earlier[None], axis=2)
    live = inside & jnp.logical_not(repeat)

    tiles_per_block = []
    for position in range(blocks):
        near_tiles = lax.slice_in_dim(
            extended, position * BLOCK_TOKENS, (position + 3) * BLOCK_TOKENS, axis=1
        )
        near_tiles = near_tiles.reshape(2, 3, BLOCK_TOKENS, kv_width).transpose(1, 0, 2, 3)
        tiles_per_block.append(
            jnp.concatenate([near_tiles, global_tiles, random_by_block[position]], axis=0)
        )
    all_tiles = jnp.stack(tiles_per_block)
    tile_count = all_tiles.shape[1]
    bias = jnp.where(live, 0.0, -jnp.inf).astype(jnp.float32)
    bias = jnp.repeat(bias, BLOCK_TOKENS, axis=1).reshape(blocks, 1, tile_count * BLOCK_TOKENS)
    out_q, grad_q, tile_grads = attention_call(
        query_loc.reshape(heads_kv, heads_per_group, blocks, BLOCK_TOKENS, head_width),
        all_tiles,
        grad_loc.reshape(heads_kv, heads_per_group, blocks, BLOCK_TOKENS, head_width),
        bias,
        heads_kv,
        score_scale,
    )
    pad_spec_low = ((0, 2), (0, 0), (0, 0), (0, 0))
    pad_spec_mid = ((1, 1), (0, 0), (0, 0), (0, 0))
    pad_spec_high = ((2, 0), (0, 0), (0, 0), (0, 0))
    window_sum = (
        jnp.pad(tile_grads[:, 0], pad_spec_low)
        + jnp.pad(tile_grads[:, 1], pad_spec_mid)
        + jnp.pad(tile_grads[:, 2], pad_spec_high)
    )
    rims = jnp.concatenate([window_sum[0], window_sum[blocks + 1]], axis=1)
    returned_rims = padded(rims.astype(jnp.bfloat16), (("seq", 1),), BLOCK_TOKENS).astype(
        rims.dtype
    )
    interior = window_sum[1 : blocks + 1]
    interior = (
        interior.at[0]
        .add(returned_rims[:, :BLOCK_TOKENS])
        .at[blocks - 1]
        .add(returned_rims[:, 3 * BLOCK_TOKENS :])
    )
    global_terms = jnp.sum(tile_grads[:, 3:5], axis=0)
    global_total = tree_sum(global_terms, "seq")
    own_weight = own_global.astype(jnp.float32)[:, :, None, None, None]
    interior = interior + jnp.sum(own_weight * global_total[:, None], axis=0)
    random_terms = (
        tile_grads[:, 5:8]
        .transpose(1, 0, 2, 3, 4)
        .reshape(entry_count, 2, BLOCK_TOKENS, kv_width)
        .astype(jnp.bfloat16)
    )
    slot_onehot = (my_slot[:, None] == jnp.arange(seq_count * capacity)[None, :]).astype(
        jnp.bfloat16
    )
    back_buffer = jnp.einsum(
        "es,exbw->sxbw", slot_onehot, random_terms, preferred_element_type=jnp.float32
    ).astype(jnp.bfloat16)
    returned_terms = exchange(back_buffer, "seq", 0, 0)
    interior = interior + jnp.einsum(
        "tco,tcxbw->oxbw",
        selector,
        returned_terms.reshape(seq_count, capacity, 2, BLOCK_TOKENS, kv_width),
        preferred_element_type=jnp.float32,
    )
    kv_grad = interior.transpose(1, 0, 2, 3).reshape(2, shard_len, kv_width).astype(jnp.bfloat16)
    out_all = out_q.reshape(blocks, heads_q, BLOCK_TOKENS, head_width)
    query_grad_all = grad_q.reshape(blocks, heads_q, BLOCK_TOKENS, head_width)
    key_grad_all = kv_grad[0].reshape(shard_len, heads_kv, head_width)
    value_grad_all = kv_grad[1].reshape(shard_len, heads_kv, head_width)
    out_back = lax.all_to_all(out_all, "head", split_axis=0, concat_axis=1, tiled=True)
    query_back = lax.all_to_all(query_grad_all, "head", split_axis=0, concat_axis=1, tiled=True)
    kv_blocks = interior.astype(jnp.bfloat16).reshape(
        blocks, 2, BLOCK_TOKENS, heads_kv, head_width
    )
    (out_back, query_back), kv_blocks = lax.optimization_barrier(((out_back, query_back), kv_blocks))
    kv_back = lax.all_to_all(kv_blocks, "head", split_axis=0, concat_axis=3, tiled=True)[0]
    out_back = out_back.reshape(-1, BLOCK_TOKENS, head_width).transpose(1, 0, 2)
    query_back = query_back.reshape(-1, BLOCK_TOKENS, head_width).transpose(1, 0, 2)
    return (out_back, query_back, kv_back[0], kv_back[1])


def solution(mesh):
    placed = (
        P(("seq", "head"), None, None),
        P(("seq", "head"), None, None),
        P(("seq", "head"), None, None),
        P(("seq", "head"), None, None),
        P(),
        P(),
    )
    return jax.shard_map(
        per_device,
        mesh=mesh,
        in_specs=placed,
        out_specs=(
            P(("seq", "head"), None, None),
            P(("seq", "head"), None, None),
            P(("seq", "head"), None, None),
            P(("seq", "head"), None, None),
        ),
        check_vma=False,
    )
```
